32 devices in a mesh: slab: 4 (over z), tx: 4 (over y, x), ty: 2 (over core).
Axes of the slice: x: 2, y: 2, z: 4, core: 2. Of those that a mesh axis runs over, the one named last changes fastest.
Arguments:
- forcing: float32 [2, 2, 2, 256, 16, 256], P(None, None, None, 'slab', 'tx', 'ty'), may hold values from -4 to 4
- wavenumber_sq: float32 [256, 16, 256], P('slab', 'tx', 'ty'), may hold values from 1.2 to 3.6
- line_inverse: float32 [4, 4, 2, 64, 64], P('slab'), may hold values from -0.15 to 0.45
- column_class: int32 [4, 16, 256], P('slab', 'tx', 'ty'), may hold values from 0 to 3
- batch_order: int32 [2, 4, 2], P(None, 'slab'), may hold values from 0 to 1, each once within a row
- pending_trace: float32 [2, 2, 4, 16, 256], P(None, None, 'slab', 'tx', 'ty'), may hold values from -6 to 6
Outputs:
- solutions: float32 [2, 2, 2, 256, 16, 256], P(None, None, None, 'slab', 'tx', 'ty')
- final_trace: float32 [2, 2, 4, 16, 256], P(None, None, 'slab', 'tx', 'ty')
The draws below stay inside these ranges and needn't reach their ends.
Inputs may be any that keep to these rules, and one draw needn't show every extreme that they name: `batch_order`: each row names every slot once.
All inputs are finite; a program needn't handle non-finite values.
Results may differ from the reference program's by a relative error of at most 0.00028.
Values sent between devices are 32-bit elements; how exact they have to be, the bound alone decides.
No kernel may reach another device: no remote copies, remote signals or barrier semaphores. Data moves between devices by JAX's collectives and lax.ppermute only.
A program may use at most 128 MiB of HBM per device.

```python
import math
import jax
import jax.numpy as jnp
from jax import lax

DZ = 64
NCLS = 4
NSRC = 2
CORR = 3
TICKS = 2
NSLAB = 4
NZ = 256
NX = 16
NY = 256


def draw_forcing(key, part):
    shape = (TICKS, NSRC, 2, NZ, NX, NY)
    return jax.random.truncated_normal(key, -4.0, 4.0, shape, jnp.float32)


def draw_line_inverse(key, part):
    shape = (NSLAB, NCLS, 2, DZ, DZ)
    spread = 0.45 / math.sqrt(DZ)
    noise = spread * jax.random.truncated_normal(key, -3.0, 3.0, shape, jnp.float32)
    identity = jnp.eye(DZ, dtype=jnp.float32)
    diagonal = jnp.stack([identity, 0.2 * identity], axis=0)
    return 0.3 * (diagonal[None, None] + noise)


def plant(values, key, least, largest):
    extent = values.shape
    place = [jax.random.randint(jax.random.fold_in(key, axis), (), 0, extent[axis]) for axis in range(len(extent))]
    values = values.at[tuple(place)].set(least)
    longest = extent.index(max(extent))
    place[longest] = (place[longest] + 1) % extent[longest]
    return values.at[tuple(place)].set(largest)


def shard_levels(key, shape, pieces, least, top_value):
    level, own = 1.0, jax.random.fold_in(key, 6)
    for dim, blocks in pieces:
        steps = jnp.exp(jax.random.uniform(jax.random.fold_in(own, dim), (blocks,), jnp.float32, least / len(pieces), top_value / len(pieces)))
        level = level * jnp.repeat(steps, shape[dim] // blocks).reshape([-1 if axis == dim else 1 for axis in range(len(shape))])
    return level


def scatter_about(key, shape, scale, limit, shards=(), kind=jnp.bfloat16):
    entries = jax.random.normal(key, shape, jnp.float32) * scale
    if len(shards) > 0:
        entries = shard_levels(key, shape, shards, -0.22, 0.18) * entries
    return jnp.clip(entries, min=-limit, max=limit).astype(kind)


def setup_inputs(seed: int = 0) -> dict:
    key_of = jax.random.split(jax.random.key(seed), 7)
    return {
        "forcing": draw_forcing(jax.random.fold_in(key_of[6], 71), 0),
        "wavenumber_sq": jnp.clip(jnp.exp(math.log(3.6) - 1.0986122 * jax.random.uniform(key_of[1], (NZ, NX, NY), jnp.float32) ** shard_levels(key_of[1], (NZ, NX, NY), ((0, 4), (1, 4), (2, 2)), -0.2, 0.2)), 1.2, 3.6),
        "line_inverse": draw_line_inverse(jax.random.fold_in(key_of[6], 71), 0),
        "column_class": plant(jax.random.randint(key_of[3], (NSLAB, NX, NY), 0, NCLS), jax.random.fold_in(key_of[3], 1), 0, NCLS - 1).astype(jnp.int32),
        "batch_order": jax.vmap(lambda own: jax.random.permutation(own, NSRC))(jax.random.split(key_of[4], TICKS * NSLAB)).reshape((TICKS, NSLAB, NSRC)).astype(jnp.int32),
        "pending_trace": scatter_about(key_of[5], (NSRC, 2, NSLAB, NX, NY), 1.0, 6.0, ((2, 4), (3, 4), (4, 2)), jnp.float32),
    }


DAMPING = 0.25
PRECISE = lax.Precision.HIGHEST


def block_matrix(inverse):
    real = inverse[:, 0]
    imaginary = inverse[:, 1]
    upper = jnp.concatenate([real, -imaginary], axis=2)
    lower = jnp.concatenate([imaginary, real], axis=2)
    return jnp.concatenate([upper, lower], axis=1)


def precondition(field, blocks, onehot):
    shape = field.shape
    flat = field.reshape(shape[0], shape[1] * shape[2], shape[3] * shape[4])
    mapped = jnp.einsum("kab,sbc->skac", blocks, flat, precision=PRECISE)
    return jnp.sum(mapped * onehot[None, :, None, :], axis=1).reshape(shape)


def stencil(padded, diag_real, diag_imaginary):
    inner = padded[:, :, :, 1:-1, 1:-1]
    real = inner[:, 0]
    imaginary = inner[:, 1]
    diagonal = jnp.stack([diag_real * real - diag_imaginary * imaginary, diag_real * imaginary + diag_imaginary * real], axis=1)
    deeper = jnp.pad(padded, ((0, 0), (0, 0), (1, 1), (0, 0), (0, 0)))
    beside = deeper[:, :, 2:, 1:-1, 1:-1] + deeper[:, :, :-2, 1:-1, 1:-1]
    beside = beside + deeper[:, :, 1:-1, 2:, 1:-1] + deeper[:, :, 1:-1, :-2, 1:-1]
    beside = beside + deeper[:, :, 1:-1, 1:-1, 2:] + deeper[:, :, 1:-1, 1:-1, :-2]
    return diagonal - beside


def reference(forcing, wavenumber_sq, line_inverse, column_class, batch_order, pending_trace):
    incoming = pending_trace
    solutions = []
    for tick in range(TICKS):
        fields = []
        leaving = []
        for slab in range(NSLAB):
            start = slab * DZ
            wavenumber = wavenumber_sq[start:start + DZ]
            diag_real = 6.0 - wavenumber
            diag_imaginary = -DAMPING * wavenumber
            blocks = block_matrix(line_inverse[slab])
            onehot = (column_class[slab].reshape(-1)[None, :] == jnp.arange(NCLS, dtype=jnp.int32)[:, None]).astype(jnp.float32)
            sources = forcing[tick][:, :, start:start + DZ]
            rhs = jnp.take(sources, batch_order[tick, slab].astype(jnp.int32), axis=0)
            rhs = rhs.at[:, :, 0].add(incoming[:, :, slab])
            field = precondition(rhs, blocks, onehot)
            for step in range(CORR):
                padded = jnp.pad(field, ((0, 0), (0, 0), (0, 0), (1, 1), (1, 1)))
                field = field + precondition(rhs - stencil(padded, diag_real, diag_imaginary), blocks, onehot)
            fields.append(field)
            leaving.append(field[:, :, DZ - 1])
        solutions.append(jnp.concatenate(fields, axis=2))
        leaving_all = jnp.stack(leaving, axis=2)
        incoming = jnp.concatenate([jnp.zeros_like(leaving_all[:, :, :1]), leaving_all[:, :, :-1]], axis=2)
    return jnp.stack(solutions, axis=0), leaving_all
```

```python
import jax
import jax.numpy as jnp
from jax import lax
from jax.sharding import PartitionSpec as P

CORR = 3
TICKS = 2


DAMPING = 0.25
PRECISE = lax.Precision.HIGHEST


def fetch(block, axes, offsets):
    sizes = [lax.axis_size(a) for a in axes]
    pairs = []
    total = 1
    for s in sizes:
        total *= s
    for linear in range(total):
        coords = []
        rest = linear
        for s in reversed(sizes):
            coords.append(rest % s)
            rest //= s
        coords = coords[::-1]
        source = [c + d for c, d in zip(coords, offsets)]
        if all(0 <= c < s for c, s in zip(source, sizes)):
            src_linear = 0
            for c, s in zip(source, sizes):
                src_linear = src_linear * s + c
            pairs.append((src_linear, linear))
    if len(axes) == 1:
        return lax.ppermute(block, axes[0], pairs)
    return lax.ppermute(block, tuple(axes), pairs)


def with_halo(block, width, lead_axes=(), lead_offsets=()):
    nx, ny = block.shape[-2], block.shape[-1]
    rows = {-1: slice(nx - width, nx), 0: slice(0, nx), 1: slice(0, width)}
    cols = {-1: slice(ny - width, ny), 0: slice(0, ny), 1: slice(0, width)}
    bands = []
    for dx in (-1, 0, 1):
        parts = []
        for dy in (-1, 0, 1):
            piece = block[..., rows[dx], cols[dy]]
            if dx == 0 and dy == 0 and not lead_axes:
                parts.append(piece)
            else:
                parts.append(
                    fetch(piece, tuple(lead_axes) + ("tx", "ty"), tuple(lead_offsets) + (dx, dy))
                )
        bands.append(jnp.concatenate(parts, axis=-1))
    return jnp.concatenate(bands, axis=-2)


def block_matrix(inverse):
    real = inverse[:, 0]
    imaginary = inverse[:, 1]
    upper = jnp.concatenate([real, -imaginary], axis=2)
    lower = jnp.concatenate([imaginary, real], axis=2)
    return jnp.concatenate([upper, lower], axis=1)


def precondition(field, blocks, onehot):
    s, two, z, c = field.shape
    flat = field.reshape(s, two * z, c)
    masked = flat[:, None] * onehot[None, :, None, :]
    out = jnp.einsum("kab,skbc->sac", blocks, masked, precision=PRECISE)
    return out.reshape(field.shape)


def shift_cols(x, d):
    c = x.shape[-1]
    if d > 0:
        return jnp.pad(x[..., d:], [(0, 0)] * (x.ndim - 1) + [(0, d)])
    return jnp.pad(x[..., : c + d], [(0, 0)] * (x.ndim - 1) + [(-d, 0)])


def apply_a(u, diag_real, diag_imaginary, row):
    real = u[:, 0]
    imaginary = u[:, 1]
    diagonal = jnp.stack(
        [
            diag_real * real - diag_imaginary * imaginary,
            diag_real * imaginary + diag_imaginary * real,
        ],
        axis=1,
    )
    zpad = jnp.pad(u, ((0, 0), (0, 0), (1, 1), (0, 0)))
    beside = zpad[:, :, 2:] + zpad[:, :, :-2]
    beside = beside + shift_cols(u, row) + shift_cols(u, -row)
    beside = beside + shift_cols(u, 1) + shift_cols(u, -1)
    return diagonal - beside


def per_device(forcing, wavenumber_sq, line_inverse, column_class, batch_order, pending_trace):
    width = CORR
    ticks, nsrc, two, depth, nx, ny = forcing.shape
    classes = line_inverse.shape[1]
    ntx = lax.axis_size("tx")
    nty = lax.axis_size("ty")
    ex, ey = nx + 2 * width, ny + 2 * width
    cols = ex * ey

    packed = jnp.concatenate(
        [
            forcing.reshape(-1, nx, ny),
            wavenumber_sq,
            pending_trace.reshape(-1, nx, ny),
            column_class[0][None].astype(jnp.float32),
        ],
        axis=0,
    )
    extended = with_halo(packed, width)
    nf = ticks * nsrc * two * depth
    npend = nsrc * two
    forcing_e = extended[:nf].reshape(ticks, nsrc, two, depth, cols)
    wavenumber_e = extended[nf : nf + depth].reshape(depth, cols)
    pending_e = extended[nf + depth : nf + depth + npend].reshape(nsrc, two, cols)
    class_e = extended[nf + depth + npend].reshape(cols).astype(jnp.int32)

    gx = lax.axis_index("tx") * nx - width + jnp.arange(ex)
    gy = lax.axis_index("ty") * ny - width + jnp.arange(ey)
    inside = ((gx >= 0) & (gx < nx * ntx))[:, None] & ((gy >= 0) & (gy < ny * nty))[None, :]
    inside = inside.reshape(cols).astype(jnp.float32)

    blocks = block_matrix(line_inverse[0])
    onehot = (class_e[None, :] == jnp.arange(classes, dtype=jnp.int32)[:, None]).astype(jnp.float32)
    diag_real = 6.0 - wavenumber_e
    diag_imaginary = -DAMPING * wavenumber_e
    orders = batch_order[:, 0]

    incoming = pending_e
    solutions = []
    trace = None
    for tick in range(ticks):
        rhs = jnp.take(forcing_e[tick], orders[tick], axis=0)
        rhs = rhs.at[:, :, 0].add(incoming)
        field = precondition(rhs, blocks, onehot)
        for step in range(CORR):
            residual = (rhs - apply_a(field, diag_real, diag_imaginary, ey)) * inside
            field = field + precondition(residual, blocks, onehot)
        tile = field.reshape(nsrc, two, depth, ex, ey)[:, :, :, width : width + nx, width : width + ny]
        solutions.append(tile)
        trace = tile[:, :, depth - 1]
        if tick + 1 < ticks:
            incoming = with_halo(trace, width, ("slab",), (-1,)).reshape(nsrc, two, cols)
    return (jnp.stack(solutions, axis=0), trace[:, :, None])


def solution(mesh):
    in_specs = (
        P(None, None, None, "slab", "tx", "ty"),
        P("slab", "tx", "ty"),
        P("slab", None, None, None, None),
        P("slab", "tx", "ty"),
        P(None, "slab", None),
        P(None, None, "slab", "tx", "ty"),
    )
    out_specs = (P(None, None, None, "slab", "tx", "ty"), P(None, None, "slab", "tx", "ty"))
    return jax.shard_map(
        per_device, mesh=mesh, in_specs=in_specs, out_specs=out_specs, check_vma=False
    )
```

```python
import functools

import jax
import jax.numpy as jnp
from jax import lax
from jax.experimental import pallas as pl
from jax.experimental.pallas import tpu as pltpu
from jax.sharding import PartitionSpec as P

CORR = 3
TICKS = 2


DAMPING = 0.25
PRECISE = lax.Precision.HIGHEST


def fetch(block, axes, offsets):
    sizes = [lax.axis_size(a) for a in axes]
    pairs = []
    total = 1
    for s in sizes:
        total *= s
    for linear in range(total):
        coords = []
        rest = linear
        for s in reversed(sizes):
            coords.append(rest % s)
            rest //= s
        coords = coords[::-1]
        source = [c + d for c, d in zip(coords, offsets)]
        if all(0 <= c < s for c, s in zip(source, sizes)):
            src_linear = 0
            for c, s in zip(source, sizes):
                src_linear = src_linear * s + c
            pairs.append((src_linear, linear))
    if len(axes) == 1:
        return lax.ppermute(block, axes[0], pairs)
    return lax.ppermute(block, tuple(axes), pairs)


def with_halo(block, width, lead_axes=(), lead_offsets=()):
    nx, ny = block.shape[-2], block.shape[-1]
    rows = {-1: slice(nx - width, nx), 0: slice(0, nx), 1: slice(0, width)}
    cols = {-1: slice(ny - width, ny), 0: slice(0, ny), 1: slice(0, width)}
    bands = []
    for dx in (-1, 0, 1):
        parts = []
        for dy in (-1, 0, 1):
            piece = block[..., rows[dx], cols[dy]]
            if dx == 0 and dy == 0 and not lead_axes:
                parts.append(piece)
            else:
                parts.append(
                    fetch(piece, tuple(lead_axes) + ("tx", "ty"), tuple(lead_offsets) + (dx, dy))
                )
        bands.append(jnp.concatenate(parts, axis=-1))
    return jnp.concatenate(bands, axis=-2)


def tick_kernel(rhs_ref, dr_ref, di_ref, hot_ref, ins_ref, blk_ref, out_ref, *, row, depth):
    nsrc, rows, cols = rhs_ref.shape
    classes = hot_ref.shape[0]
    dr = dr_ref[...]
    di = di_ref[...]
    ins = ins_ref[...]
    hots = [hot_ref[k : k + 1, :] for k in range(classes)]
    blks = [blk_ref[k] for k in range(classes)]
    zrow = lax.broadcasted_iota(jnp.int32, (rows, cols), 0) % depth
    top = zrow == 0
    bottom = zrow == depth - 1

    def precond(x):
        acc = None
        for k in range(classes):
            t = jnp.dot(blks[k], x * hots[k], precision=PRECISE, preferred_element_type=jnp.float32)
            acc = t if acc is None else acc + t
        return acc

    def apply_a(u):
        real = u[:depth]
        imaginary = u[depth:]
        diagonal = jnp.concatenate(
            [dr * real - di * imaginary, dr * imaginary + di * real], axis=0
        )
        down = jnp.where(top, 0.0, pltpu.roll(u, 1, 0))
        up = jnp.where(bottom, 0.0, pltpu.roll(u, rows - 1, 0))
        beside = up + down
        beside = beside + pltpu.roll(u, cols - row, 1) + pltpu.roll(u, row, 1)
        beside = beside + pltpu.roll(u, cols - 1, 1) + pltpu.roll(u, 1, 1)
        return diagonal - beside

    for s in range(nsrc):
        rhs = rhs_ref[s]
        u = precond(rhs)
        for _ in range(CORR):
            u = u + precond(ins * (rhs - apply_a(u)))
        out_ref[s] = u


def run_tick(rhs, dr, di, hot, ins, blocks, row, depth):
    nsrc, rows, cols = rhs.shape
    classes = hot.shape[0]
    flops = nsrc * (CORR + 1) * classes * 2 * rows * rows * cols
    return pl.pallas_call(
        functools.partial(tick_kernel, row=row, depth=depth),
        out_shape=jax.ShapeDtypeStruct(rhs.shape, jnp.float32),
        in_specs=[pl.BlockSpec(memory_space=pltpu.VMEM)] * 6,
        out_specs=pl.BlockSpec(memory_space=pltpu.VMEM),
        cost_estimate=pl.CostEstimate(
            flops=flops, transcendentals=0, bytes_accessed=4 * (2 * rhs.size + 4 * dr.size)
        ),
    )(rhs, dr, di, hot, ins, blocks)


def block_matrix(inverse):
    real = inverse[:, 0]
    imaginary = inverse[:, 1]
    upper = jnp.concatenate([real, -imaginary], axis=2)
    lower = jnp.concatenate([imaginary, real], axis=2)
    return jnp.concatenate([upper, lower], axis=1)


def per_device(forcing, wavenumber_sq, line_inverse, column_class, batch_order, pending_trace):
    width = CORR
    ticks, nsrc, two, depth, nx, ny = forcing.shape
    classes = line_inverse.shape[1]
    ntx = lax.axis_size("tx")
    nty = lax.axis_size("ty")
    ex, ey = nx + 2 * width, ny + 2 * width
    cols = ex * ey

    packed = jnp.concatenate(
        [
            forcing.reshape(-1, nx, ny),
            wavenumber_sq,
            pending_trace.reshape(-1, nx, ny),
            column_class[0][None].astype(jnp.float32),
        ],
        axis=0,
    )
    extended = with_halo(packed, width)
    nf = ticks * nsrc * two * depth
    npend = nsrc * two
    forcing_e = extended[:nf].reshape(ticks, nsrc, two, depth, cols)
    wavenumber_e = extended[nf : nf + depth].reshape(depth, cols)
    pending_e = extended[nf + depth : nf + depth + npend].reshape(nsrc, two, cols)
    class_e = extended[nf + depth + npend].reshape(cols).astype(jnp.int32)

    padded = -(-cols // 128) * 128

    def flat(x):
        return jnp.pad(x, [(0, 0)] * (x.ndim - 1) + [(0, padded - cols)])

    gx = lax.axis_index("tx") * nx - width + jnp.arange(ex)
    gy = lax.axis_index("ty") * ny - width + jnp.arange(ey)
    inside = ((gx >= 0) & (gx < nx * ntx))[:, None] & ((gy >= 0) & (gy < ny * nty))[None, :]
    inside = flat(inside.reshape(1, cols).astype(jnp.float32))

    blocks = block_matrix(line_inverse[0])
    onehot = flat(
        (class_e[None, :] == jnp.arange(classes, dtype=jnp.int32)[:, None]).astype(jnp.float32)
    )
    diag_real = flat(6.0 - wavenumber_e)
    diag_imaginary = flat(-DAMPING * wavenumber_e)
    orders = batch_order[:, 0]

    incoming = pending_e
    solutions = []
    trace = None
    for tick in range(ticks):
        rhs = jnp.take(forcing_e[tick], orders[tick], axis=0)
        rhs = rhs.at[:, :, 0].add(incoming)
        rhs = flat(rhs).reshape(nsrc, two * depth, padded)
        field = run_tick(rhs, diag_real, diag_imaginary, onehot, inside, blocks, ey, depth)
        field = field.reshape(nsrc, two, depth, padded)[..., :cols]
        tile = field.reshape(nsrc, two, depth, ex, ey)[:, :, :, width : width + nx, width : width + ny]
        solutions.append(tile)
        trace = tile[:, :, depth - 1]
        if tick + 1 < ticks:
            incoming = with_halo(trace, width, ("slab",), (-1,)).reshape(nsrc, two, cols)
    return (jnp.stack(solutions, axis=0), trace[:, :, None])


def solution(mesh):
    in_specs = (
        P(None, None, None, "slab", "tx", "ty"),
        P("slab", "tx", "ty"),
        P("slab", None, None, None, None),
        P("slab", "tx", "ty"),
        P(None, "slab", None),
        P(None, None, "slab", "tx", "ty"),
    )
    out_specs = (P(None, None, None, "slab", "tx", "ty"), P(None, None, "slab", "tx", "ty"))
    return jax.shard_map(
        per_device, mesh=mesh, in_specs=in_specs, out_specs=out_specs, check_vma=False
    )
```

```python
import functools

import jax
import jax.numpy as jnp
from jax import lax
from jax.experimental import pallas as pl
from jax.experimental.pallas import tpu as pltpu
from jax.sharding import PartitionSpec as P

CORR = 3
TICKS = 2


DAMPING = 0.25
PRECISE = lax.Precision.HIGHEST
SPLIT = 65537.0


def fetch(block, axes, offsets):
    sizes = [lax.axis_size(a) for a in axes]
    pairs = []
    total = 1
    for s in sizes:
        total *= s
    for linear in range(total):
        coords = []
        rest = linear
        for s in reversed(sizes):
            coords.append(rest % s)
            rest //= s
        coords = coords[::-1]
        source = [c + d for c, d in zip(coords, offsets)]
        if all(0 <= c < s for c, s in zip(source, sizes)):
            src_linear = 0
            for c, s in zip(source, sizes):
                src_linear = src_linear * s + c
            pairs.append((src_linear, linear))
    if len(axes) == 1:
        return lax.ppermute(block, axes[0], pairs)
    return lax.ppermute(block, tuple(axes), pairs)


def with_halo(block, width, lead_axes=(), lead_offsets=()):
    nx, ny = block.shape[-2], block.shape[-1]
    rows = {-1: slice(nx - width, nx), 0: slice(0, nx), 1: slice(0, width)}
    cols = {-1: slice(ny - width, ny), 0: slice(0, ny), 1: slice(0, width)}
    bands = []
    for dx in (-1, 0, 1):
        parts = []
        for dy in (-1, 0, 1):
            piece = block[..., rows[dx], cols[dy]]
            if dx == 0 and dy == 0 and not lead_axes:
                parts.append(piece)
            else:
                parts.append(
                    fetch(piece, tuple(lead_axes) + ("tx", "ty"), tuple(lead_offsets) + (dx, dy))
                )
        bands.append(jnp.concatenate(parts, axis=-1))
    return jnp.concatenate(bands, axis=-2)


def tick_kernel(
    order_ref, frc_ref, inc_ref, dr_ref, di_ref, hot_ref, ins_ref, bhi_ref, blo_ref, out_ref, *, row, depth
):
    nsrc, rows, cols = frc_ref.shape
    classes = hot_ref.shape[0]
    zrow = lax.broadcasted_iota(jnp.int32, (rows, cols), 0) % depth
    top = zrow == 0
    bottom = zrow == depth - 1

    def precond(x):
        scaled = x * SPLIT
        high = scaled - (scaled - x)
        low = x - high
        hots = [hot_ref[k : k + 1, :] for k in range(classes)]
        high = jnp.concatenate([high * h for h in hots], axis=0).astype(jnp.bfloat16)
        low = jnp.concatenate([low * h for h in hots], axis=0).astype(jnp.bfloat16)
        bhi = bhi_ref[...]
        blo = blo_ref[...]
        out = jnp.dot(bhi, low, preferred_element_type=jnp.float32)
        out = out + jnp.dot(blo, high, preferred_element_type=jnp.float32)
        return out + jnp.dot(bhi, high, preferred_element_type=jnp.float32)

    def apply_a(u):
        dr = dr_ref[...]
        di = di_ref[...]
        real = u[:depth]
        imaginary = u[depth:]
        diagonal = jnp.concatenate(
            [dr * real - di * imaginary, dr * imaginary + di * real], axis=0
        )
        down = jnp.where(top, 0.0, pltpu.roll(u, 1, 0))
        up = jnp.where(bottom, 0.0, pltpu.roll(u, rows - 1, 0))
        beside = up + down
        beside = beside + pltpu.roll(u, cols - row, 1) + pltpu.roll(u, row, 1)
        beside = beside + pltpu.roll(u, cols - 1, 1) + pltpu.roll(u, 1, 1)
        return diagonal - beside

    def one_source(s, carry):
        forcing = frc_ref[order_ref[s]]
        incoming = inc_ref[s]
        layer = jnp.concatenate(
            [
                jnp.broadcast_to(incoming[0:1], (depth, cols)),
                jnp.broadcast_to(incoming[1:2], (depth, cols)),
            ],
            axis=0,
        )
        rhs = jnp.where(top, forcing + layer, forcing)

        def correct(i, u):
            return u + precond(ins_ref[...] * (rhs - apply_a(u)))

        out_ref[s] = lax.fori_loop(0, CORR, correct, precond(rhs))
        return carry

    lax.fori_loop(0, nsrc, one_source, 0)


def run_tick(order, forcing, incoming, dr, di, hot, ins, bhi, blo, row, depth):
    nsrc, rows, cols = forcing.shape
    width = bhi.shape[1]
    flops = nsrc * (CORR + 1) * 3 * 2 * rows * width * cols
    vmem = pl.BlockSpec(memory_space=pltpu.VMEM)
    return pl.pallas_call(
        functools.partial(tick_kernel, row=row, depth=depth),
        out_shape=jax.ShapeDtypeStruct(forcing.shape, jnp.float32),
        in_specs=[pl.BlockSpec(memory_space=pltpu.SMEM)] + [vmem] * 8,
        out_specs=vmem,
        cost_estimate=pl.CostEstimate(
            flops=flops, transcendentals=0, bytes_accessed=4 * (2 * forcing.size + 4 * dr.size)
        ),
    )(order, forcing, incoming, dr, di, hot, ins, bhi, blo)


def block_matrix(inverse):
    real = inverse[:, 0]
    imaginary = inverse[:, 1]
    upper = jnp.concatenate([real, -imaginary], axis=2)
    lower = jnp.concatenate([imaginary, real], axis=2)
    return jnp.concatenate([upper, lower], axis=1)


def per_device(forcing, wavenumber_sq, line_inverse, column_class, batch_order, pending_trace):
    width = CORR
    ticks, nsrc, two, depth, nx, ny = forcing.shape
    classes = line_inverse.shape[1]
    ntx = lax.axis_size("tx")
    nty = lax.axis_size("ty")
    ex, ey = nx + 2 * width, ny + 2 * width
    cols = ex * ey

    packed = jnp.concatenate(
        [
            forcing.reshape(-1, nx, ny),
            wavenumber_sq,
            pending_trace.reshape(-1, nx, ny),
            column_class[0][None].astype(jnp.float32),
        ],
        axis=0,
    )
    extended = with_halo(packed, width)
    nf = ticks * nsrc * two * depth
    npend = nsrc * two
    forcing_e = extended[:nf].reshape(ticks, nsrc, two, depth, cols)
    wavenumber_e = extended[nf : nf + depth].reshape(depth, cols)
    pending_e = extended[nf + depth : nf + depth + npend].reshape(nsrc, two, cols)
    class_e = extended[nf + depth + npend].reshape(cols).astype(jnp.int32)

    padded = -(-cols // 128) * 128

    def flat(x):
        return jnp.pad(x, [(0, 0)] * (x.ndim - 1) + [(0, padded - cols)])

    gx = lax.axis_index("tx") * nx - width + jnp.arange(ex)
    gy = lax.axis_index("ty") * ny - width + jnp.arange(ey)
    inside = ((gx >= 0) & (gx < nx * ntx))[:, None] & ((gy >= 0) & (gy < ny * nty))[None, :]
    inside = flat(inside.reshape(1, cols).astype(jnp.float32))

    blocks = block_matrix(line_inverse[0])
    side_by_side = jnp.concatenate([blocks[k] for k in range(classes)], axis=1)
    rounded = lax.reduce_precision(side_by_side, exponent_bits=8, mantissa_bits=7)
    bhi = rounded.astype(jnp.bfloat16)
    blo = (side_by_side - rounded).astype(jnp.bfloat16)
    onehot = flat(
        (class_e[None, :] == jnp.arange(classes, dtype=jnp.int32)[:, None]).astype(jnp.float32)
    )
    diag_real = flat(6.0 - wavenumber_e)
    diag_imaginary = flat(-DAMPING * wavenumber_e)
    orders = batch_order[:, 0]
    forcing_f = flat(forcing_e).reshape(ticks, nsrc, two * depth, padded)

    incoming = flat(pending_e)
    solutions = []
    trace = None
    for tick in range(ticks):
        field = run_tick(
            orders[tick], forcing_f[tick], incoming, diag_real, diag_imaginary, onehot, inside,
            bhi, blo, ey, depth,
        )
        field = field.reshape(nsrc, two, depth, padded)[..., :cols]
        tile = field.reshape(nsrc, two, depth, ex, ey)[:, :, :, width : width + nx, width : width + ny]
        solutions.append(tile)
        trace = tile[:, :, depth - 1]
        if tick + 1 < ticks:
            incoming = flat(with_halo(trace, width, ("slab",), (-1,)).reshape(nsrc, two, cols))
    return (jnp.stack(solutions, axis=0), trace[:, :, None])


def solution(mesh):
    in_specs = (
        P(None, None, None, "slab", "tx", "ty"),
        P("slab", "tx", "ty"),
        P("slab", None, None, None, None),
        P("slab", "tx", "ty"),
        P(None, "slab", None),
        P(None, None, "slab", "tx", "ty"),
    )
    out_specs = (P(None, None, None, "slab", "tx", "ty"), P(None, None, "slab", "tx", "ty"))
    return jax.shard_map(
        per_device, mesh=mesh, in_specs=in_specs, out_specs=out_specs, check_vma=False
    )
```

```python
import functools

import jax
import jax.numpy as jnp
from jax import lax
from jax.experimental import pallas as pl
from jax.experimental.pallas import tpu as pltpu
from jax.sharding import PartitionSpec as P

CORR = 3
TICKS = 2


DAMPING = 0.25
PRECISE = lax.Precision.HIGHEST
SPLIT = 65537.0


def fetch(block, axes, offsets):
    sizes = [lax.axis_size(a) for a in axes]
    pairs = []
    total = 1
    for s in sizes:
        total *= s
    for linear in range(total):
        coords = []
        rest = linear
        for s in reversed(sizes):
            coords.append(rest % s)
            rest //= s
        coords = coords[::-1]
        source = [c + d for c, d in zip(coords, offsets)]
        if all(0 <= c < s for c, s in zip(source, sizes)):
            src_linear = 0
            for c, s in zip(source, sizes):
                src_linear = src_linear * s + c
            pairs.append((src_linear, linear))
    if len(axes) == 1:
        return lax.ppermute(block, axes[0], pairs)
    return lax.ppermute(block, tuple(axes), pairs)


def halo_pieces(block, width, lead_axes=(), lead_offsets=()):
    nx, ny = block.shape[-2], block.shape[-1]
    rows = {-1: slice(nx - width, nx), 0: slice(0, nx), 1: slice(0, width)}
    cols = {-1: slice(ny - width, ny), 0: slice(0, ny), 1: slice(0, width)}
    pieces = {}
    for dx in (-1, 0, 1):
        for dy in (-1, 0, 1):
            piece = block[..., rows[dx], cols[dy]]
            if dx == 0 and dy == 0 and not lead_axes:
                pieces[dx, dy] = piece
            else:
                pieces[dx, dy] = fetch(
                    piece, tuple(lead_axes) + ("tx", "ty"), tuple(lead_offsets) + (dx, dy)
                )
    return pieces


def flat_extended(pieces, nx, width, padded):
    segments = []
    for ix in range(nx + 2 * width):
        dx = -1 if ix < width else (0 if ix < width + nx else 1)
        r = ix - (0 if dx == -1 else (width if dx == 0 else width + nx))
        for dy in (-1, 0, 1):
            segments.append(pieces[dx, dy][..., r, :])
    used = sum(s.shape[-1] for s in segments)
    lead = segments[0].shape[:-1]
    segments.append(jnp.zeros(lead + (padded - used,), segments[0].dtype))
    return jnp.concatenate(segments, axis=-1)


def tick_kernel(order_ref, pk_ref, inc_ref, ins_ref, bhi_ref, blo_ref, out_ref, *, tick, row, depth, width):
    nsrc, rows, owned = out_ref.shape
    cols = pk_ref.shape[1]
    classes = bhi_ref.shape[1] // rows
    lanes = 128
    waves = tick * nsrc * rows
    wave0 = pk_ref.shape[0] - depth - 2 * nsrc - 1
    zrow = lax.broadcasted_iota(jnp.int32, (rows, cols), 0) % depth
    top = zrow == 0
    bottom = zrow == depth - 1

    def precond(x):
        scaled = x * SPLIT
        high = scaled - (scaled - x)
        low = x - high
        label = pk_ref[pl.ds(wave0 + depth + 2 * nsrc, 1), :]
        hots = [(label == float(k)).astype(jnp.float32) for k in range(classes)]
        high = jnp.concatenate([high * h for h in hots], axis=0).astype(jnp.bfloat16)
        low = jnp.concatenate([low * h for h in hots], axis=0).astype(jnp.bfloat16)
        bhi = bhi_ref[...]
        blo = blo_ref[...]
        out = jnp.dot(bhi, low, preferred_element_type=jnp.float32)
        out = out + jnp.dot(blo, high, preferred_element_type=jnp.float32)
        return out + jnp.dot(bhi, high, preferred_element_type=jnp.float32)

    def apply_a(u):
        wave = pk_ref[pl.ds(wave0, depth), :]
        dr = 6.0 - wave
        di = -DAMPING * wave
        real = u[:depth]
        imaginary = u[depth:]
        diagonal = jnp.concatenate(
            [dr * real - di * imaginary, dr * imaginary + di * real], axis=0
        )
        down = jnp.where(top, 0.0, pltpu.roll(u, 1, 0))
        up = jnp.where(bottom, 0.0, pltpu.roll(u, rows - 1, 0))
        beside = up + down
        beside = beside + pltpu.roll(u, cols - row, 1) + pltpu.roll(u, row, 1)
        beside = beside + pltpu.roll(u, cols - 1, 1) + pltpu.roll(u, 1, 1)
        return diagonal - beside

    def one_source(s, carry):
        first = pl.multiple_of(waves + order_ref[s] * rows, rows)
        forcing = pk_ref[pl.ds(first, rows), :]
        incoming = inc_ref[s]
        layer = jnp.concatenate(
            [
                jnp.broadcast_to(incoming[0:1], (depth, cols)),
                jnp.broadcast_to(incoming[1:2], (depth, cols)),
            ],
            axis=0,
        )
        rhs = jnp.where(top, forcing + layer, forcing)

        def correct(i, u):
            return u + precond(ins_ref[...] * (rhs - apply_a(u)))

        u = lax.fori_loop(0, CORR, correct, precond(rhs))
        for x in range(owned // lanes):
            begin = (x + width) * row + width
            out_ref[s, :, x * lanes : (x + 1) * lanes] = pltpu.roll(u, cols - begin, 1)[:, :lanes]
        return carry

    lax.fori_loop(0, nsrc, one_source, 0)


def run_tick(order, packed, incoming, ins, bhi, blo, tick, row, depth, width, owned):
    nsrc = incoming.shape[0]
    rows, stacked = bhi.shape
    cols = packed.shape[1]
    flops = nsrc * (CORR + 1) * 3 * 2 * rows * stacked * cols
    vmem = pl.BlockSpec(memory_space=pltpu.VMEM)
    return pl.pallas_call(
        functools.partial(tick_kernel, tick=tick, row=row, depth=depth, width=width),
        out_shape=jax.ShapeDtypeStruct((nsrc, rows, owned), jnp.float32),
        in_specs=[pl.BlockSpec(memory_space=pltpu.SMEM)] + [vmem] * 5,
        out_specs=vmem,
        cost_estimate=pl.CostEstimate(
            flops=flops, transcendentals=0, bytes_accessed=4 * (packed.size // 2 + nsrc * rows * owned)
        ),
    )(order, packed, incoming, ins, bhi, blo)


def block_matrix(inverse):
    real = inverse[:, 0]
    imaginary = inverse[:, 1]
    upper = jnp.concatenate([real, -imaginary], axis=2)
    lower = jnp.concatenate([imaginary, real], axis=2)
    return jnp.concatenate([upper, lower], axis=1)


def per_device(forcing, wavenumber_sq, line_inverse, column_class, batch_order, pending_trace):
    width = CORR
    ticks, nsrc, two, depth, nx, ny = forcing.shape
    classes = line_inverse.shape[1]
    ntx = lax.axis_size("tx")
    nty = lax.axis_size("ty")
    ex, ey = nx + 2 * width, ny + 2 * width
    cols = ex * ey
    padded = -(-cols // 128) * 128
    assert width <= nx and width <= ny

    packed = jnp.concatenate(
        [
            forcing.reshape(-1, nx, ny),
            wavenumber_sq,
            pending_trace.reshape(-1, nx, ny),
            column_class[0][None].astype(jnp.float32),
        ],
        axis=0,
    )
    packed = flat_extended(halo_pieces(packed, width), nx, width, padded)
    first_pending = ticks * nsrc * two * depth + depth

    gx = lax.axis_index("tx") * nx - width + jnp.arange(ex)
    gy = lax.axis_index("ty") * ny - width + jnp.arange(ey)
    inside = ((gx >= 0) & (gx < nx * ntx))[:, None] & ((gy >= 0) & (gy < ny * nty))[None, :]
    inside = jnp.pad(inside.reshape(1, cols).astype(jnp.float32), ((0, 0), (0, padded - cols)))

    blocks = block_matrix(line_inverse[0])
    side_by_side = jnp.concatenate([blocks[k] for k in range(classes)], axis=1)
    rounded = lax.reduce_precision(side_by_side, exponent_bits=8, mantissa_bits=7)
    bhi = rounded.astype(jnp.bfloat16)
    blo = (side_by_side - rounded).astype(jnp.bfloat16)
    orders = batch_order[:, 0]

    incoming = packed[first_pending : first_pending + nsrc * two].reshape(nsrc, two, padded)
    solutions = []
    trace = None
    for tick in range(ticks):
        field = run_tick(
            orders[tick], packed, incoming, inside, bhi, blo, tick, ey, depth, width, nx * ny
        )
        tile = field.reshape(nsrc, two, depth, nx, ny)
        solutions.append(tile)
        trace = tile[:, :, depth - 1]
        if tick + 1 < ticks:
            incoming = flat_extended(halo_pieces(trace, width, ("slab",), (-1,)), nx, width, padded)
    return (jnp.stack(solutions, axis=0), trace[:, :, None])


def solution(mesh):
    in_specs = (
        P(None, None, None, "slab", "tx", "ty"),
        P("slab", "tx", "ty"),
        P("slab", None, None, None, None),
        P("slab", "tx", "ty"),
        P(None, "slab", None),
        P(None, None, "slab", "tx", "ty"),
    )
    out_specs = (P(None, None, None, "slab", "tx", "ty"), P(None, None, "slab", "tx", "ty"))
    return jax.shard_map(
        per_device, mesh=mesh, in_specs=in_specs, out_specs=out_specs, check_vma=False
    )
```

```python
import functools

import jax
import jax.numpy as jnp
from jax import lax
from jax.experimental import pallas as pl
from jax.experimental.pallas import tpu as pltpu
from jax.sharding import PartitionSpec as P

CORR = 3
TICKS = 2


DAMPING = 0.25
PRECISE = lax.Precision.HIGHEST
SPLIT = 65537.0


def fetch(block, axes, offsets):
    sizes = [lax.axis_size(a) for a in axes]
    pairs = []
    total = 1
    for s in sizes:
        total *= s
    for linear in range(total):
        coords = []
        rest = linear
        for s in reversed(sizes):
            coords.append(rest % s)
            rest //= s
        coords = coords[::-1]
        source = [c + d for c, d in zip(coords, offsets)]
        if all(0 <= c < s for c, s in zip(source, sizes)):
            src_linear = 0
            for c, s in zip(source, sizes):
                src_linear = src_linear * s + c
            pairs.append((src_linear, linear))
    if len(axes) == 1:
        return lax.ppermute(block, axes[0], pairs)
    return lax.ppermute(block, tuple(axes), pairs)


def halo_pieces(block, width, lead_axes=(), lead_offsets=()):
    nx, ny = block.shape[-2], block.shape[-1]
    rows = {-1: slice(nx - width, nx), 0: slice(0, nx), 1: slice(0, width)}
    cols = {-1: slice(ny - width, ny), 0: slice(0, ny), 1: slice(0, width)}
    pieces = {}
    for dx in (-1, 0, 1):
        for dy in (-1, 0, 1):
            piece = block[..., rows[dx], cols[dy]]
            if dx == 0 and dy == 0 and not lead_axes:
                pieces[dx, dy] = piece
            else:
                pieces[dx, dy] = fetch(
                    piece, tuple(lead_axes) + ("tx", "ty"), tuple(lead_offsets) + (dx, dy)
                )
    return pieces


def flat_extended(pieces, nx, width, padded):
    segments = []
    for ix in range(nx + 2 * width):
        dx = -1 if ix < width else (0 if ix < width + nx else 1)
        r = ix - (0 if dx == -1 else (width if dx == 0 else width + nx))
        for dy in (-1, 0, 1):
            segments.append(pieces[dx, dy][..., r, :])
    used = sum(s.shape[-1] for s in segments)
    lead = segments[0].shape[:-1]
    segments.append(jnp.zeros(lead + (padded - used,), segments[0].dtype))
    return jnp.concatenate(segments, axis=-1)


def tick_kernel(order_ref, frc_ref, pk_ref, inc_ref, ins_ref, bhi_ref, blo_ref, out_ref, *, row, depth, width):
    nsrc, rows, owned = out_ref.shape
    cols = pk_ref.shape[1]
    classes = bhi_ref.shape[1] // rows
    lanes = 128
    wave0 = pk_ref.shape[0] - depth - 2 * nsrc - 1
    zrow = lax.broadcasted_iota(jnp.int32, (rows, cols), 0) % depth
    top = zrow == 0
    bottom = zrow == depth - 1

    def precond(x):
        scaled = x * SPLIT
        high = scaled - (scaled - x)
        low = x - high
        label = pk_ref[pl.ds(wave0 + depth + 2 * nsrc, 1), :]
        hots = [(label == float(k)).astype(jnp.float32) for k in range(classes)]
        high = jnp.concatenate([high * h for h in hots], axis=0).astype(jnp.bfloat16)
        low = jnp.concatenate([low * h for h in hots], axis=0).astype(jnp.bfloat16)
        bhi = bhi_ref[...]
        blo = blo_ref[...]
        out = jnp.dot(bhi, low, preferred_element_type=jnp.float32)
        out = out + jnp.dot(blo, high, preferred_element_type=jnp.float32)
        return out + jnp.dot(bhi, high, preferred_element_type=jnp.float32)

    def apply_a(u):
        wave = pk_ref[pl.ds(wave0, depth), :]
        dr = 6.0 - wave
        di = -DAMPING * wave
        real = u[:depth]
        imaginary = u[depth:]
        diagonal = jnp.concatenate(
            [dr * real - di * imaginary, dr * imaginary + di * real], axis=0
        )
        down = jnp.where(top, 0.0, pltpu.roll(u, 1, 0))
        up = jnp.where(bottom, 0.0, pltpu.roll(u, rows - 1, 0))
        beside = up + down
        beside = beside + pltpu.roll(u, cols - row, 1) + pltpu.roll(u, row, 1)
        beside = beside + pltpu.roll(u, cols - 1, 1) + pltpu.roll(u, 1, 1)
        return diagonal - beside

    def one_source(s, carry):
        first = pl.multiple_of(order_ref[s] * rows, rows)
        forcing = frc_ref[pl.ds(first, rows), :]
        incoming = inc_ref[s]
        layer = jnp.concatenate(
            [
                jnp.broadcast_to(incoming[0:1], (depth, cols)),
                jnp.broadcast_to(incoming[1:2], (depth, cols)),
            ],
            axis=0,
        )
        rhs = jnp.where(top, forcing + layer, forcing)

        def correct(i, u):
            return u + precond(ins_ref[...] * (rhs - apply_a(u)))

        u = lax.fori_loop(0, CORR, correct, precond(rhs))
        for x in range(owned // lanes):
            begin = (x + width) * row + width
            out_ref[s, :, x * lanes : (x + 1) * lanes] = pltpu.roll(u, cols - begin, 1)[:, :lanes]
        return carry

    lax.fori_loop(0, nsrc, one_source, 0)


def run_tick(order, forcing, packed, incoming, ins, bhi, blo, row, depth, width, owned):
    nsrc = incoming.shape[0]
    rows, stacked = bhi.shape
    cols = packed.shape[1]
    flops = nsrc * (CORR + 1) * 3 * 2 * rows * stacked * cols
    vmem = pl.BlockSpec(memory_space=pltpu.VMEM)
    return pl.pallas_call(
        functools.partial(tick_kernel, row=row, depth=depth, width=width),
        out_shape=jax.ShapeDtypeStruct((nsrc, rows, owned), jnp.float32),
        in_specs=[pl.BlockSpec(memory_space=pltpu.SMEM)] + [vmem] * 6,
        out_specs=vmem,
        cost_estimate=pl.CostEstimate(
            flops=flops,
            transcendentals=0,
            bytes_accessed=4 * (forcing.size + packed.size // 4 + nsrc * rows * owned),
        ),
    )(order, forcing, packed, incoming, ins, bhi, blo)


def block_matrix(inverse):
    real = inverse[:, 0]
    imaginary = inverse[:, 1]
    upper = jnp.concatenate([real, -imaginary], axis=2)
    lower = jnp.concatenate([imaginary, real], axis=2)
    return jnp.concatenate([upper, lower], axis=1)


def per_device(forcing, wavenumber_sq, line_inverse, column_class, batch_order, pending_trace):
    width = CORR
    ticks, nsrc, two, depth, nx, ny = forcing.shape
    classes = line_inverse.shape[1]
    ntx = lax.axis_size("tx")
    nty = lax.axis_size("ty")
    ex, ey = nx + 2 * width, ny + 2 * width
    cols = ex * ey
    padded = -(-cols // 128) * 128
    assert width <= nx and width <= ny

    per_tick = forcing.reshape(ticks, -1, nx, ny)
    packed = jnp.concatenate(
        [
            per_tick[0],
            wavenumber_sq,
            pending_trace.reshape(-1, nx, ny),
            column_class[0][None].astype(jnp.float32),
        ],
        axis=0,
    )
    packed = flat_extended(halo_pieces(packed, width), nx, width, padded)
    later = [halo_pieces(per_tick[t], width) for t in range(1, ticks)]
    first_pending = nsrc * two * depth + depth

    gx = lax.axis_index("tx") * nx - width + jnp.arange(ex)
    gy = lax.axis_index("ty") * ny - width + jnp.arange(ey)
    inside = ((gx >= 0) & (gx < nx * ntx))[:, None] & ((gy >= 0) & (gy < ny * nty))[None, :]
    inside = jnp.pad(inside.reshape(1, cols).astype(jnp.float32), ((0, 0), (0, padded - cols)))

    blocks = block_matrix(line_inverse[0])
    side_by_side = jnp.concatenate([blocks[k] for k in range(classes)], axis=1)
    rounded = lax.reduce_precision(side_by_side, exponent_bits=8, mantissa_bits=7)
    bhi = rounded.astype(jnp.bfloat16)
    blo = (side_by_side - rounded).astype(jnp.bfloat16)
    orders = batch_order[:, 0]

    incoming = packed[first_pending : first_pending + nsrc * two].reshape(nsrc, two, padded)
    solutions = []
    trace = None
    forcing_f = packed
    for tick in range(ticks):
        field = run_tick(
            orders[tick], forcing_f, packed, incoming, inside, bhi, blo, ey, depth, width, nx * ny
        )
        if tick + 1 < ticks:
            field, pieces = lax.optimization_barrier((field, later[tick]))
            forcing_f = flat_extended(pieces, nx, width, padded)
        tile = field.reshape(nsrc, two, depth, nx, ny)
        solutions.append(tile)
        trace = tile[:, :, depth - 1]
        if tick + 1 < ticks:
            incoming = flat_extended(halo_pieces(trace, width, ("slab",), (-1,)), nx, width, padded)
    return (jnp.stack(solutions, axis=0), trace[:, :, None])


def solution(mesh):
    in_specs = (
        P(None, None, None, "slab", "tx", "ty"),
        P("slab", "tx", "ty"),
        P("slab", None, None, None, None),
        P("slab", "tx", "ty"),
        P(None, "slab", None),
        P(None, None, "slab", "tx", "ty"),
    )
    out_specs = (P(None, None, None, "slab", "tx", "ty"), P(None, None, "slab", "tx", "ty"))
    return jax.shard_map(
        per_device, mesh=mesh, in_specs=in_specs, out_specs=out_specs, check_vma=False
    )
```

```python
import functools

import jax
import jax.numpy as jnp
from jax import lax
from jax.experimental import pallas as pl
from jax.experimental.pallas import tpu as pltpu
from jax.sharding import PartitionSpec as P

CORR = 3
TICKS = 2


DAMPING = 0.25
PRECISE = lax.Precision.HIGHEST
SPLIT = 65537.0


def fetch(block, axes, offsets):
    sizes = [lax.axis_size(a) for a in axes]
    pairs = []
    total = 1
    for s in sizes:
        total *= s
    for linear in range(total):
        coords = []
        rest = linear
        for s in reversed(sizes):
            coords.append(rest % s)
            rest //= s
        coords = coords[::-1]
        source = [c + d for c, d in zip(coords, offsets)]
        if all(0 <= c < s for c, s in zip(source, sizes)):
            src_linear = 0
            for c, s in zip(source, sizes):
                src_linear = src_linear * s + c
            pairs.append((src_linear, linear))
    if len(axes) == 1:
        return lax.ppermute(block, axes[0], pairs)
    return lax.ppermute(block, tuple(axes), pairs)


def extend_y(block, width):
    ny = block.shape[-1]
    low = fetch(block[..., ny - width :], ("ty",), (-1,))
    high = fetch(block[..., :width], ("ty",), (1,))
    return jnp.concatenate([low, block, high], axis=-1)


def flat_extended(block, width, padded, lead_axes=(), lead_offsets=()):
    nx = block.shape[-2]
    pieces = {
        -1: fetch(block[..., nx - width :, :], tuple(lead_axes) + ("tx",), tuple(lead_offsets) + (-1,)),
        1: fetch(block[..., :width, :], tuple(lead_axes) + ("tx",), tuple(lead_offsets) + (1,)),
    }
    if lead_axes:
        pieces[0] = fetch(block, tuple(lead_axes) + ("tx",), tuple(lead_offsets) + (0,))
    else:
        pieces[0] = block
    segments = []
    for ix in range(nx + 2 * width):
        dx = -1 if ix < width else (0 if ix < width + nx else 1)
        r = ix - (0 if dx == -1 else (width if dx == 0 else width + nx))
        segments.append(pieces[dx][..., r, :])
    used = sum(s.shape[-1] for s in segments)
    lead = segments[0].shape[:-1]
    segments.append(jnp.zeros(lead + (padded - used,), segments[0].dtype))
    return jnp.concatenate(segments, axis=-1)


def tick_kernel(order_ref, pk_ref, inc_ref, ins_ref, bhi_ref, blo_ref, out_ref, *, tick, row, depth, width):
    nsrc, rows, owned = out_ref.shape
    cols = pk_ref.shape[1]
    classes = bhi_ref.shape[1] // rows
    lanes = 128
    waves = tick * nsrc * rows
    wave0 = pk_ref.shape[0] - depth - 2 * nsrc - 1
    zrow = lax.broadcasted_iota(jnp.int32, (rows, cols), 0) % depth
    top = zrow == 0
    bottom = zrow == depth - 1

    def precond(x):
        scaled = x * SPLIT
        high = scaled - (scaled - x)
        low = x - high
        label = pk_ref[pl.ds(wave0 + depth + 2 * nsrc, 1), :]
        hots = [(label == float(k)).astype(jnp.float32) for k in range(classes)]
        high = jnp.concatenate([high * h for h in hots], axis=0).astype(jnp.bfloat16)
        low = jnp.concatenate([low * h for h in hots], axis=0).astype(jnp.bfloat16)
        bhi = bhi_ref[...]
        blo = blo_ref[...]
        out = jnp.dot(bhi, low, preferred_element_type=jnp.float32)
        out = out + jnp.dot(blo, high, preferred_element_type=jnp.float32)
        return out + jnp.dot(bhi, high, preferred_element_type=jnp.float32)

    def apply_a(u):
        wave = pk_ref[pl.ds(wave0, depth), :]
        dr = 6.0 - wave
        di = -DAMPING * wave
        real = u[:depth]
        imaginary = u[depth:]
        diagonal = jnp.concatenate(
            [dr * real - di * imaginary, dr * imaginary + di * real], axis=0
        )
        down = jnp.where(top, 0.0, pltpu.roll(u, 1, 0))
        up = jnp.where(bottom, 0.0, pltpu.roll(u, rows - 1, 0))
        beside = up + down
        beside = beside + pltpu.roll(u, cols - row, 1) + pltpu.roll(u, row, 1)
        beside = beside + pltpu.roll(u, cols - 1, 1) + pltpu.roll(u, 1, 1)
        return diagonal - beside

    def one_source(s, carry):
        first = pl.multiple_of(waves + order_ref[s] * rows, rows)
        forcing = pk_ref[pl.ds(first, rows), :]
        incoming = inc_ref[s]
        layer = jnp.concatenate(
            [
                jnp.broadcast_to(incoming[0:1], (depth, cols)),
                jnp.broadcast_to(incoming[1:2], (depth, cols)),
            ],
            axis=0,
        )
        rhs = jnp.where(top, forcing + layer, forcing)

        def correct(i, u):
            return u + precond(ins_ref[...] * (rhs - apply_a(u)))

        u = lax.fori_loop(0, CORR, correct, precond(rhs))
        for x in range(owned // lanes):
            begin = (x + width) * row + width
            out_ref[s, :, x * lanes : (x + 1) * lanes] = pltpu.roll(u, cols - begin, 1)[:, :lanes]
        return carry

    lax.fori_loop(0, nsrc, one_source, 0)


def run_tick(order, packed, incoming, ins, bhi, blo, tick, row, depth, width, owned):
    nsrc = incoming.shape[0]
    rows, stacked = bhi.shape
    cols = packed.shape[1]
    flops = nsrc * (CORR + 1) * 3 * 2 * rows * stacked * cols
    vmem = pl.BlockSpec(memory_space=pltpu.VMEM)
    return pl.pallas_call(
        functools.partial(tick_kernel, tick=tick, row=row, depth=depth, width=width),
        out_shape=jax.ShapeDtypeStruct((nsrc, rows, owned), jnp.float32),
        in_specs=[pl.BlockSpec(memory_space=pltpu.SMEM)] + [vmem] * 5,
        out_specs=vmem,
        cost_estimate=pl.CostEstimate(
            flops=flops, transcendentals=0, bytes_accessed=4 * (packed.size // 2 + nsrc * rows * owned)
        ),
    )(order, packed, incoming, ins, bhi, blo)


def block_matrix(inverse):
    real = inverse[:, 0]
    imaginary = inverse[:, 1]
    upper = jnp.concatenate([real, -imaginary], axis=2)
    lower = jnp.concatenate([imaginary, real], axis=2)
    return jnp.concatenate([upper, lower], axis=1)


def per_device(forcing, wavenumber_sq, line_inverse, column_class, batch_order, pending_trace):
    width = CORR
    ticks, nsrc, two, depth, nx, ny = forcing.shape
    classes = line_inverse.shape[1]
    ntx = lax.axis_size("tx")
    nty = lax.axis_size("ty")
    ex, ey = nx + 2 * width, ny + 2 * width
    cols = ex * ey
    padded = -(-cols // 128) * 128
    assert width <= nx and width <= ny

    packed = jnp.concatenate(
        [
            forcing.reshape(-1, nx, ny),
            wavenumber_sq,
            pending_trace.reshape(-1, nx, ny),
            column_class[0][None].astype(jnp.float32),
        ],
        axis=0,
    )
    packed = flat_extended(extend_y(packed, width), width, padded)
    first_pending = ticks * nsrc * two * depth + depth

    gx = lax.axis_index("tx") * nx - width + jnp.arange(ex)
    gy = lax.axis_index("ty") * ny - width + jnp.arange(ey)
    inside = ((gx >= 0) & (gx < nx * ntx))[:, None] & ((gy >= 0) & (gy < ny * nty))[None, :]
    inside = jnp.pad(inside.reshape(1, cols).astype(jnp.float32), ((0, 0), (0, padded - cols)))

    blocks = block_matrix(line_inverse[0])
    side_by_side = jnp.concatenate([blocks[k] for k in range(classes)], axis=1)
    rounded = lax.reduce_precision(side_by_side, exponent_bits=8, mantissa_bits=7)
    bhi = rounded.astype(jnp.bfloat16)
    blo = (side_by_side - rounded).astype(jnp.bfloat16)
    orders = batch_order[:, 0]

    incoming = packed[first_pending : first_pending + nsrc * two].reshape(nsrc, two, padded)
    solutions = []
    trace = None
    for tick in range(ticks):
        field = run_tick(
            orders[tick], packed, incoming, inside, bhi, blo, tick, ey, depth, width, nx * ny
        )
        tile = field.reshape(nsrc, two, depth, nx, ny)
        solutions.append(tile)
        trace = tile[:, :, depth - 1]
        if tick + 1 < ticks:
            incoming = flat_extended(extend_y(trace, width), width, padded, ("slab",), (-1,))
    return (jnp.stack(solutions, axis=0), trace[:, :, None])


def solution(mesh):
    in_specs = (
        P(None, None, None, "slab", "tx", "ty"),
        P("slab", "tx", "ty"),
        P("slab", None, None, None, None),
        P("slab", "tx", "ty"),
        P(None, "slab", None),
        P(None, None, "slab", "tx", "ty"),
    )
    out_specs = (P(None, None, None, "slab", "tx", "ty"), P(None, None, "slab", "tx", "ty"))
    return jax.shard_map(
        per_device, mesh=mesh, in_specs=in_specs, out_specs=out_specs, check_vma=False
    )
```

```python
import functools

import jax
import jax.numpy as jnp
from jax import lax
from jax.experimental import pallas as pl
from jax.experimental.pallas import tpu as pltpu
from jax.sharding import PartitionSpec as P

CORR = 3
TICKS = 2


DAMPING = 0.25
PRECISE = lax.Precision.HIGHEST
SPLIT = 65537.0


def fetch(block, axes, offsets):
    sizes = [lax.axis_size(a) for a in axes]
    pairs = []
    total = 1
    for s in sizes:
        total *= s
    for linear in range(total):
        coords = []
        rest = linear
        for s in reversed(sizes):
            coords.append(rest % s)
            rest //= s
        coords = coords[::-1]
        source = [c + d for c, d in zip(coords, offsets)]
        if all(0 <= c < s for c, s in zip(source, sizes)):
            src_linear = 0
            for c, s in zip(source, sizes):
                src_linear = src_linear * s + c
            pairs.append((src_linear, linear))
    if len(axes) == 1:
        return lax.ppermute(block, axes[0], pairs)
    return lax.ppermute(block, tuple(axes), pairs)


def extend_x(block, width, lead_axes=(), lead_offsets=()):
    nx = block.shape[-2]
    axes = tuple(lead_axes) + ("tx",)
    low = fetch(block[..., nx - width :, :], axes, tuple(lead_offsets) + (-1,))
    high = fetch(block[..., :width, :], axes, tuple(lead_offsets) + (1,))
    middle = fetch(block, axes, tuple(lead_offsets) + (0,)) if lead_axes else block
    return jnp.concatenate([low, middle, high], axis=-2)


def flat_extended(block, width, padded):
    ny = block.shape[-1]
    low = fetch(block[..., ny - width :], ("ty",), (-1,))
    high = fetch(block[..., :width], ("ty",), (1,))
    segments = []
    for ix in range(block.shape[-2]):
        segments += [low[..., ix, :], block[..., ix, :], high[..., ix, :]]
    used = sum(s.shape[-1] for s in segments)
    lead = segments[0].shape[:-1]
    segments.append(jnp.zeros(lead + (padded - used,), segments[0].dtype))
    return jnp.concatenate(segments, axis=-1)


def tick_kernel(order_ref, pk_ref, inc_ref, ins_ref, bhi_ref, blo_ref, out_ref, *, tick, row, depth, width):
    nsrc, rows, owned = out_ref.shape
    cols = pk_ref.shape[1]
    classes = bhi_ref.shape[1] // rows
    lanes = 128
    waves = tick * nsrc * rows
    wave0 = pk_ref.shape[0] - depth - 2 * nsrc - 1
    zrow = lax.broadcasted_iota(jnp.int32, (rows, cols), 0) % depth
    top = zrow == 0
    bottom = zrow == depth - 1

    def precond(x):
        scaled = x * SPLIT
        high = scaled - (scaled - x)
        low = x - high
        label = pk_ref[pl.ds(wave0 + depth + 2 * nsrc, 1), :]
        hots = [(label == float(k)).astype(jnp.float32) for k in range(classes)]
        high = jnp.concatenate([high * h for h in hots], axis=0).astype(jnp.bfloat16)
        low = jnp.concatenate([low * h for h in hots], axis=0).astype(jnp.bfloat16)
        bhi = bhi_ref[...]
        blo = blo_ref[...]
        out = jnp.dot(bhi, low, preferred_element_type=jnp.float32)
        out = out + jnp.dot(blo, high, preferred_element_type=jnp.float32)
        return out + jnp.dot(bhi, high, preferred_element_type=jnp.float32)

    def apply_a(u):
        wave = pk_ref[pl.ds(wave0, depth), :]
        dr = 6.0 - wave
        di = -DAMPING * wave
        real = u[:depth]
        imaginary = u[depth:]
        diagonal = jnp.concatenate(
            [dr * real - di * imaginary, dr * imaginary + di * real], axis=0
        )
        down = jnp.where(top, 0.0, pltpu.roll(u, 1, 0))
        up = jnp.where(bottom, 0.0, pltpu.roll(u, rows - 1, 0))
        beside = up + down
        beside = beside + pltpu.roll(u, cols - row, 1) + pltpu.roll(u, row, 1)
        beside = beside + pltpu.roll(u, cols - 1, 1) + pltpu.roll(u, 1, 1)
        return diagonal - beside

    def one_source(s, carry):
        first = pl.multiple_of(waves + order_ref[s] * rows, rows)
        forcing = pk_ref[pl.ds(first, rows), :]
        incoming = inc_ref[s]
        layer = jnp.concatenate(
            [
                jnp.broadcast_to(incoming[0:1], (depth, cols)),
                jnp.broadcast_to(incoming[1:2], (depth, cols)),
            ],
            axis=0,
        )
        rhs = jnp.where(top, forcing + layer, forcing)

        def correct(i, u):
            return u + precond(ins_ref[...] * (rhs - apply_a(u)))

        u = lax.fori_loop(0, CORR, correct, precond(rhs))
        for x in range(owned // lanes):
            begin = (x + width) * row + width
            out_ref[s, :, x * lanes : (x + 1) * lanes] = pltpu.roll(u, cols - begin, 1)[:, :lanes]
        return carry

    lax.fori_loop(0, nsrc, one_source, 0)


def run_tick(order, packed, incoming, ins, bhi, blo, tick, row, depth, width, owned):
    nsrc = incoming.shape[0]
    rows, stacked = bhi.shape
    cols = packed.shape[1]
    flops = nsrc * (CORR + 1) * 3 * 2 * rows * stacked * cols
    vmem = pl.BlockSpec(memory_space=pltpu.VMEM)
    return pl.pallas_call(
        functools.partial(tick_kernel, tick=tick, row=row, depth=depth, width=width),
        out_shape=jax.ShapeDtypeStruct((nsrc, rows, owned), jnp.float32),
        in_specs=[pl.BlockSpec(memory_space=pltpu.SMEM)] + [vmem] * 5,
        out_specs=vmem,
        cost_estimate=pl.CostEstimate(
            flops=flops, transcendentals=0, bytes_accessed=4 * (packed.size // 2 + nsrc * rows * owned)
        ),
    )(order, packed, incoming, ins, bhi, blo)


def block_matrix(inverse):
    real = inverse[:, 0]
    imaginary = inverse[:, 1]
    upper = jnp.concatenate([real, -imaginary], axis=2)
    lower = jnp.concatenate([imaginary, real], axis=2)
    return jnp.concatenate([upper, lower], axis=1)


def per_device(forcing, wavenumber_sq, line_inverse, column_class, batch_order, pending_trace):
    width = CORR
    ticks, nsrc, two, depth, nx, ny = forcing.shape
    classes = line_inverse.shape[1]
    ntx = lax.axis_size("tx")
    nty = lax.axis_size("ty")
    ex, ey = nx + 2 * width, ny + 2 * width
    cols = ex * ey
    padded = -(-cols // 128) * 128
    assert width <= nx and width <= ny

    packed = jnp.concatenate(
        [
            forcing.reshape(-1, nx, ny),
            wavenumber_sq,
            pending_trace.reshape(-1, nx, ny),
            column_class[0][None].astype(jnp.float32),
        ],
        axis=0,
    )
    packed = flat_extended(extend_x(packed, width), width, padded)
    first_pending = ticks * nsrc * two * depth + depth

    gx = lax.axis_index("tx") * nx - width + jnp.arange(ex)
    gy = lax.axis_index("ty") * ny - width + jnp.arange(ey)
    inside = ((gx >= 0) & (gx < nx * ntx))[:, None] & ((gy >= 0) & (gy < ny * nty))[None, :]
    inside = jnp.pad(inside.reshape(1, cols).astype(jnp.float32), ((0, 0), (0, padded - cols)))

    blocks = block_matrix(line_inverse[0])
    side_by_side = jnp.concatenate([blocks[k] for k in range(classes)], axis=1)
    rounded = lax.reduce_precision(side_by_side, exponent_bits=8, mantissa_bits=7)
    bhi = rounded.astype(jnp.bfloat16)
    blo = (side_by_side - rounded).astype(jnp.bfloat16)
    orders = batch_order[:, 0]

    incoming = packed[first_pending : first_pending + nsrc * two].reshape(nsrc, two, padded)
    solutions = []
    trace = None
    for tick in range(ticks):
        field = run_tick(
            orders[tick], packed, incoming, inside, bhi, blo, tick, ey, depth, width, nx * ny
        )
        tile = field.reshape(nsrc, two, depth, nx, ny)
        solutions.append(tile)
        trace = tile[:, :, depth - 1]
        if tick + 1 < ticks:
            incoming = flat_extended(extend_x(trace, width, ("slab",), (-1,)), width, padded)
    return (jnp.stack(solutions, axis=0), trace[:, :, None])


def solution(mesh):
    in_specs = (
        P(None, None, None, "slab", "tx", "ty"),
        P("slab", "tx", "ty"),
        P("slab", None, None, None, None),
        P("slab", "tx", "ty"),
        P(None, "slab", None),
        P(None, None, "slab", "tx", "ty"),
    )
    out_specs = (P(None, None, None, "slab", "tx", "ty"), P(None, None, "slab", "tx", "ty"))
    return jax.shard_map(
        per_device, mesh=mesh, in_specs=in_specs, out_specs=out_specs, check_vma=False
    )
```

```python
import functools

import jax
import jax.numpy as jnp
from jax import lax
from jax.experimental import pallas as pl
from jax.experimental.pallas import tpu as pltpu
from jax.sharding import PartitionSpec as P

CORR = 3
TICKS = 2


DAMPING = 0.25
PRECISE = lax.Precision.HIGHEST
SPLIT = 65537.0


def fetch(block, axes, offsets):
    sizes = [lax.axis_size(a) for a in axes]
    pairs = []
    total = 1
    for s in sizes:
        total *= s
    for linear in range(total):
        coords = []
        rest = linear
        for s in reversed(sizes):
            coords.append(rest % s)
            rest //= s
        coords = coords[::-1]
        source = [c + d for c, d in zip(coords, offsets)]
        if all(0 <= c < s for c, s in zip(source, sizes)):
            src_linear = 0
            for c, s in zip(source, sizes):
                src_linear = src_linear * s + c
            pairs.append((src_linear, linear))
    if len(axes) == 1:
        return lax.ppermute(block, axes[0], pairs)
    return lax.ppermute(block, tuple(axes), pairs)


def extend_y(block, width):
    ny = block.shape[-1]
    low = fetch(block[..., ny - width :], ("ty",), (-1,))
    high = fetch(block[..., :width], ("ty",), (1,))
    return jnp.concatenate([low, block, high], axis=-1)


def flat_extended(block, width, padded, lead_axes=(), lead_offsets=()):
    nx = block.shape[-2]
    pieces = {
        -1: fetch(block[..., nx - width :, :], tuple(lead_axes) + ("tx",), tuple(lead_offsets) + (-1,)),
        1: fetch(block[..., :width, :], tuple(lead_axes) + ("tx",), tuple(lead_offsets) + (1,)),
    }
    if lead_axes:
        pieces[0] = fetch(block, tuple(lead_axes) + ("tx",), tuple(lead_offsets) + (0,))
    else:
        pieces[0] = block
    segments = []
    for ix in range(nx + 2 * width):
        dx = -1 if ix < width else (0 if ix < width + nx else 1)
        r = ix - (0 if dx == -1 else (width if dx == 0 else width + nx))
        segments.append(pieces[dx][..., r, :])
    used = sum(s.shape[-1] for s in segments)
    lead = segments[0].shape[:-1]
    segments.append(jnp.zeros(lead + (padded - used,), segments[0].dtype))
    return jnp.concatenate(segments, axis=-1)


def tick_kernel(order_ref, frc_ref, pk_ref, inc_ref, ins_ref, bhi_ref, blo_ref, out_ref, *, row, depth, width):
    nsrc, rows, owned = out_ref.shape
    cols = pk_ref.shape[1]
    classes = bhi_ref.shape[1] // rows
    lanes = 128
    wave0 = pk_ref.shape[0] - depth - 2 * nsrc - 1
    zrow = lax.broadcasted_iota(jnp.int32, (rows, cols), 0) % depth
    top = zrow == 0
    bottom = zrow == depth - 1

    def precond(x):
        scaled = x * SPLIT
        high = scaled - (scaled - x)
        low = x - high
        label = pk_ref[pl.ds(wave0 + depth + 2 * nsrc, 1), :]
        hots = [(label == float(k)).astype(jnp.float32) for k in range(classes)]
        high = jnp.concatenate([high * h for h in hots], axis=0).astype(jnp.bfloat16)
        low = jnp.concatenate([low * h for h in hots], axis=0).astype(jnp.bfloat16)
        bhi = bhi_ref[...]
        blo = blo_ref[...]
        out = jnp.dot(bhi, low, preferred_element_type=jnp.float32)
        out = out + jnp.dot(blo, high, preferred_element_type=jnp.float32)
        return out + jnp.dot(bhi, high, preferred_element_type=jnp.float32)

    def apply_a(u):
        wave = pk_ref[pl.ds(wave0, depth), :]
        dr = 6.0 - wave
        di = -DAMPING * wave
        real = u[:depth]
        imaginary = u[depth:]
        diagonal = jnp.concatenate(
            [dr * real - di * imaginary, dr * imaginary + di * real], axis=0
        )
        down = jnp.where(top, 0.0, pltpu.roll(u, 1, 0))
        up = jnp.where(bottom, 0.0, pltpu.roll(u, rows - 1, 0))
        beside = up + down
        beside = beside + pltpu.roll(u, cols - row, 1) + pltpu.roll(u, row, 1)
        beside = beside + pltpu.roll(u, cols - 1, 1) + pltpu.roll(u, 1, 1)
        return diagonal - beside

    def one_source(s, carry):
        first = pl.multiple_of(order_ref[s] * rows, rows)
        forcing = frc_ref[pl.ds(first, rows), :]
        incoming = inc_ref[s]
        layer = jnp.concatenate(
            [
                jnp.broadcast_to(incoming[0:1], (depth, cols)),
                jnp.broadcast_to(incoming[1:2], (depth, cols)),
            ],
            axis=0,
        )
        rhs = jnp.where(top, forcing + layer, forcing)

        def correct(i, u):
            return u + precond(ins_ref[...] * (rhs - apply_a(u)))

        u = lax.fori_loop(0, CORR, correct, precond(rhs))
        for x in range(owned // lanes):
            begin = (x + width) * row + width
            out_ref[s, :, x * lanes : (x + 1) * lanes] = pltpu.roll(u, cols - begin, 1)[:, :lanes]
        return carry

    lax.fori_loop(0, nsrc, one_source, 0)


def run_tick(order, forcing, packed, incoming, ins, bhi, blo, row, depth, width, owned):
    nsrc = incoming.shape[0]
    rows, stacked = bhi.shape
    cols = packed.shape[1]
    flops = nsrc * (CORR + 1) * 3 * 2 * rows * stacked * cols
    vmem = pl.BlockSpec(memory_space=pltpu.VMEM)
    return pl.pallas_call(
        functools.partial(tick_kernel, row=row, depth=depth, width=width),
        out_shape=jax.ShapeDtypeStruct((nsrc, rows, owned), jnp.float32),
        in_specs=[pl.BlockSpec(memory_space=pltpu.SMEM)] + [vmem] * 6,
        out_specs=vmem,
        cost_estimate=pl.CostEstimate(
            flops=flops,
            transcendentals=0,
            bytes_accessed=4 * (forcing.size + packed.size // 4 + nsrc * rows * owned),
        ),
    )(order, forcing, packed, incoming, ins, bhi, blo)


def block_matrix(inverse):
    real = inverse[:, 0]
    imaginary = inverse[:, 1]
    upper = jnp.concatenate([real, -imaginary], axis=2)
    lower = jnp.concatenate([imaginary, real], axis=2)
    return jnp.concatenate([upper, lower], axis=1)


def per_device(forcing, wavenumber_sq, line_inverse, column_class, batch_order, pending_trace):
    width = CORR
    ticks, nsrc, two, depth, nx, ny = forcing.shape
    classes = line_inverse.shape[1]
    ntx = lax.axis_size("tx")
    nty = lax.axis_size("ty")
    ex, ey = nx + 2 * width, ny + 2 * width
    cols = ex * ey
    padded = -(-cols // 128) * 128
    assert width <= nx and width <= ny

    per_tick = forcing.reshape(ticks, -1, nx, ny)
    packed = jnp.concatenate(
        [
            per_tick[0],
            wavenumber_sq,
            pending_trace.reshape(-1, nx, ny),
            column_class[0][None].astype(jnp.float32),
        ]
        + [per_tick[t] for t in range(1, ticks)],
        axis=0,
    )
    packed = extend_y(packed, width)
    rows_now = per_tick.shape[1] + depth + nsrc * two + 1
    later = [
        packed[rows_now + (t - 1) * per_tick.shape[1] : rows_now + t * per_tick.shape[1]]
        for t in range(1, ticks)
    ]
    packed = flat_extended(packed[:rows_now], width, padded)
    first_pending = nsrc * two * depth + depth

    gx = lax.axis_index("tx") * nx - width + jnp.arange(ex)
    gy = lax.axis_index("ty") * ny - width + jnp.arange(ey)
    inside = ((gx >= 0) & (gx < nx * ntx))[:, None] & ((gy >= 0) & (gy < ny * nty))[None, :]
    inside = jnp.pad(inside.reshape(1, cols).astype(jnp.float32), ((0, 0), (0, padded - cols)))

    blocks = block_matrix(line_inverse[0])
    side_by_side = jnp.concatenate([blocks[k] for k in range(classes)], axis=1)
    rounded = lax.reduce_precision(side_by_side, exponent_bits=8, mantissa_bits=7)
    bhi = rounded.astype(jnp.bfloat16)
    blo = (side_by_side - rounded).astype(jnp.bfloat16)
    orders = batch_order[:, 0]

    incoming = packed[first_pending : first_pending + nsrc * two].reshape(nsrc, two, padded)
    solutions = []
    trace = None
    forcing_f = packed
    for tick in range(ticks):
        field = run_tick(
            orders[tick], forcing_f, packed, incoming, inside, bhi, blo, ey, depth, width, nx * ny
        )
        if tick + 1 < ticks:
            field, rows = lax.optimization_barrier((field, later[tick]))
            forcing_f = flat_extended(rows, width, padded)
        tile = field.reshape(nsrc, two, depth, nx, ny)
        solutions.append(tile)
        trace = tile[:, :, depth - 1]
        if tick + 1 < ticks:
            incoming = flat_extended(extend_y(trace, width), width, padded, ("slab",), (-1,))
    return (jnp.stack(solutions, axis=0), trace[:, :, None])


def solution(mesh):
    in_specs = (
        P(None, None, None, "slab", "tx", "ty"),
        P("slab", "tx", "ty"),
        P("slab", None, None, None, None),
        P("slab", "tx", "ty"),
        P(None, "slab", None),
        P(None, None, "slab", "tx", "ty"),
    )
    out_specs = (P(None, None, None, "slab", "tx", "ty"), P(None, None, "slab", "tx", "ty"))
    return jax.shard_map(
        per_device, mesh=mesh, in_specs=in_specs, out_specs=out_specs, check_vma=False
    )
```

```python
import functools

import jax
import jax.numpy as jnp
from jax import lax
from jax.experimental import pallas as pl
from jax.experimental.pallas import tpu as pltpu
from jax.sharding import PartitionSpec as P

CORR = 3
TICKS = 2


DAMPING = 0.25
PRECISE = lax.Precision.HIGHEST
SPLIT = 65537.0


def fetch(block, axes, offsets):
    sizes = [lax.axis_size(a) for a in axes]
    pairs = []
    total = 1
    for s in sizes:
        total *= s
    for linear in range(total):
        coords = []
        rest = linear
        for s in reversed(sizes):
            coords.append(rest % s)
            rest //= s
        coords = coords[::-1]
        source = [c + d for c, d in zip(coords, offsets)]
        if all(0 <= c < s for c, s in zip(source, sizes)):
            src_linear = 0
            for c, s in zip(source, sizes):
                src_linear = src_linear * s + c
            pairs.append((src_linear, linear))
    if len(axes) == 1:
        return lax.ppermute(block, axes[0], pairs)
    return lax.ppermute(block, tuple(axes), pairs)


def extend_y(block, width):
    ny = block.shape[-1]
    low = fetch(block[..., ny - width :], ("ty",), (-1,))
    high = fetch(block[..., :width], ("ty",), (1,))
    return jnp.concatenate([low, block, high], axis=-1)


def flat_extended(block, width, padded, lead_axes=(), lead_offsets=()):
    nx = block.shape[-2]
    pieces = {
        -1: fetch(block[..., nx - width :, :], tuple(lead_axes) + ("tx",), tuple(lead_offsets) + (-1,)),
        1: fetch(block[..., :width, :], tuple(lead_axes) + ("tx",), tuple(lead_offsets) + (1,)),
    }
    if lead_axes:
        pieces[0] = fetch(block, tuple(lead_axes) + ("tx",), tuple(lead_offsets) + (0,))
    else:
        pieces[0] = block
    segments = []
    for ix in range(nx + 2 * width):
        dx = -1 if ix < width else (0 if ix < width + nx else 1)
        r = ix - (0 if dx == -1 else (width if dx == 0 else width + nx))
        segments.append(pieces[dx][..., r, :])
    used = sum(s.shape[-1] for s in segments)
    lead = segments[0].shape[:-1]
    segments.append(jnp.zeros(lead + (padded - used,), segments[0].dtype))
    return jnp.concatenate(segments, axis=-1)


def tick_kernel(
    order_ref, frc_ref, pk_ref, inc_ref, ins_ref, bhi_ref, blo_ref, out_ref, field_ref, *, row, depth, width
):
    nsrc, rows, owned = out_ref.shape
    cols = pk_ref.shape[1]
    classes = bhi_ref.shape[1] // rows
    lanes = 128
    wave0 = pk_ref.shape[0] - depth - 2 * nsrc - 1
    label_row = wave0 + depth + 2 * nsrc
    extent = owned // lanes + 2 * width

    def edges(lo, hi):
        zrow = lax.broadcasted_iota(jnp.int32, (rows, hi - lo), 0) % depth
        return zrow == 0, zrow == depth - 1

    def precond(x, lo, hi):
        scaled = x * SPLIT
        high = scaled - (scaled - x)
        low = x - high
        label = pk_ref[pl.ds(label_row, 1), lo:hi]
        hots = [(label == float(k)).astype(jnp.float32) for k in range(classes)]
        high = jnp.concatenate([high * h for h in hots], axis=0).astype(jnp.bfloat16)
        low = jnp.concatenate([low * h for h in hots], axis=0).astype(jnp.bfloat16)
        bhi = bhi_ref[...]
        blo = blo_ref[...]
        out = jnp.dot(bhi, low, preferred_element_type=jnp.float32)
        out = out + jnp.dot(blo, high, preferred_element_type=jnp.float32)
        return out + jnp.dot(bhi, high, preferred_element_type=jnp.float32)

    def apply_a(u, lo, hi):
        span = hi - lo
        top, bottom = edges(lo, hi)
        wave = pk_ref[pl.ds(wave0, depth), lo:hi]
        dr = 6.0 - wave
        di = -DAMPING * wave
        real = u[:depth]
        imaginary = u[depth:]
        diagonal = jnp.concatenate(
            [dr * real - di * imaginary, dr * imaginary + di * real], axis=0
        )
        down = jnp.where(top, 0.0, pltpu.roll(u, 1, 0))
        up = jnp.where(bottom, 0.0, pltpu.roll(u, rows - 1, 0))
        beside = up + down
        beside = beside + pltpu.roll(u, span - row, 1) + pltpu.roll(u, row, 1)
        beside = beside + pltpu.roll(u, span - 1, 1) + pltpu.roll(u, 1, 1)
        return diagonal - beside

    def one_source(s, carry):
        first = pl.multiple_of(order_ref[s] * rows, rows)
        forcing = frc_ref[pl.ds(first, rows), :]
        incoming = inc_ref[s]
        layer = jnp.concatenate(
            [
                jnp.broadcast_to(incoming[0:1], (depth, cols)),
                jnp.broadcast_to(incoming[1:2], (depth, cols)),
            ],
            axis=0,
        )
        top, _ = edges(0, cols)
        rhs = jnp.where(top, forcing + layer, forcing)
        field_ref[...] = precond(rhs, 0, cols)
        for step in range(1, CORR + 1):
            a = (step * row) // lanes * lanes
            b = min(-(-((extent - step) * row) // lanes) * lanes, cols)
            lo = max(a - 2 * lanes, 0)
            hi = min(b + 2 * lanes, cols)
            stencil = apply_a(field_ref[:, lo:hi], lo, hi)[:, a - lo : b - lo]
            residual = ins_ref[:, a:b] * (rhs[:, a:b] - stencil)
            field_ref[:, a:b] = field_ref[:, a:b] + precond(residual, a, b)
        u = field_ref[...]
        for x in range(owned // lanes):
            begin = (x + width) * row + width
            out_ref[s, :, x * lanes : (x + 1) * lanes] = pltpu.roll(u, cols - begin, 1)[:, :lanes]
        return carry

    lax.fori_loop(0, nsrc, one_source, 0)


def run_tick(order, forcing, packed, incoming, ins, bhi, blo, row, depth, width, owned):
    nsrc = incoming.shape[0]
    rows, stacked = bhi.shape
    cols = packed.shape[1]
    flops = nsrc * (CORR + 1) * 3 * 2 * rows * stacked * cols
    vmem = pl.BlockSpec(memory_space=pltpu.VMEM)
    return pl.pallas_call(
        functools.partial(tick_kernel, row=row, depth=depth, width=width),
        out_shape=jax.ShapeDtypeStruct((nsrc, rows, owned), jnp.float32),
        in_specs=[pl.BlockSpec(memory_space=pltpu.SMEM)] + [vmem] * 6,
        out_specs=vmem,
        scratch_shapes=[pltpu.VMEM((rows, cols), jnp.float32)],
        cost_estimate=pl.CostEstimate(
            flops=flops,
            transcendentals=0,
            bytes_accessed=4 * (forcing.size + packed.size // 4 + nsrc * rows * owned),
        ),
    )(order, forcing, packed, incoming, ins, bhi, blo)


def block_matrix(inverse):
    real = inverse[:, 0]
    imaginary = inverse[:, 1]
    upper = jnp.concatenate([real, -imaginary], axis=2)
    lower = jnp.concatenate([imaginary, real], axis=2)
    return jnp.concatenate([upper, lower], axis=1)


def per_device(forcing, wavenumber_sq, line_inverse, column_class, batch_order, pending_trace):
    width = CORR
    ticks, nsrc, two, depth, nx, ny = forcing.shape
    classes = line_inverse.shape[1]
    ntx = lax.axis_size("tx")
    nty = lax.axis_size("ty")
    ex, ey = nx + 2 * width, ny + 2 * width
    cols = ex * ey
    padded = -(-cols // 128) * 128
    assert width <= nx and width <= ny

    per_tick = forcing.reshape(ticks, -1, nx, ny)
    packed = jnp.concatenate(
        [
            per_tick[0],
            wavenumber_sq,
            pending_trace.reshape(-1, nx, ny),
            column_class[0][None].astype(jnp.float32),
        ]
        + [per_tick[t] for t in range(1, ticks)],
        axis=0,
    )
    packed = extend_y(packed, width)
    rows_now = per_tick.shape[1] + depth + nsrc * two + 1
    later = [
        packed[rows_now + (t - 1) * per_tick.shape[1] : rows_now + t * per_tick.shape[1]]
        for t in range(1, ticks)
    ]
    packed = flat_extended(packed[:rows_now], width, padded)
    first_pending = nsrc * two * depth + depth

    gx = lax.axis_index("tx") * nx - width + jnp.arange(ex)
    gy = lax.axis_index("ty") * ny - width + jnp.arange(ey)
    inside = ((gx >= 0) & (gx < nx * ntx))[:, None] & ((gy >= 0) & (gy < ny * nty))[None, :]
    inside = jnp.pad(inside.reshape(1, cols).astype(jnp.float32), ((0, 0), (0, padded - cols)))

    blocks = block_matrix(line_inverse[0])
    side_by_side = jnp.concatenate([blocks[k] for k in range(classes)], axis=1)
    rounded = lax.reduce_precision(side_by_side, exponent_bits=8, mantissa_bits=7)
    bhi = rounded.astype(jnp.bfloat16)
    blo = (side_by_side - rounded).astype(jnp.bfloat16)
    orders = batch_order[:, 0]

    incoming = packed[first_pending : first_pending + nsrc * two].reshape(nsrc, two, padded)
    solutions = []
    trace = None
    forcing_f = packed
    for tick in range(ticks):
        field = run_tick(
            orders[tick], forcing_f, packed, incoming, inside, bhi, blo, ey, depth, width, nx * ny
        )
        if tick + 1 < ticks:
            field, rows = lax.optimization_barrier((field, later[tick]))
            forcing_f = flat_extended(rows, width, padded)
        tile = field.reshape(nsrc, two, depth, nx, ny)
        solutions.append(tile)
        trace = tile[:, :, depth - 1]
        if tick + 1 < ticks:
            incoming = flat_extended(extend_y(trace, width), width, padded, ("slab",), (-1,))
    return (jnp.stack(solutions, axis=0), trace[:, :, None])


def solution(mesh):
    in_specs = (
        P(None, None, None, "slab", "tx", "ty"),
        P("slab", "tx", "ty"),
        P("slab", None, None, None, None),
        P("slab", "tx", "ty"),
        P(None, "slab", None),
        P(None, None, "slab", "tx", "ty"),
    )
    out_specs = (P(None, None, None, "slab", "tx", "ty"), P(None, None, "slab", "tx", "ty"))
    return jax.shard_map(
        per_device, mesh=mesh, in_specs=in_specs, out_specs=out_specs, check_vma=False
    )
```

```python
import functools

import jax
import jax.numpy as jnp
from jax import lax
from jax.experimental import pallas as pl
from jax.experimental.pallas import tpu as pltpu
from jax.sharding import PartitionSpec as P

CORR = 3
TICKS = 2


DAMPING = 0.25
PRECISE = lax.Precision.HIGHEST
SPLIT = 65537.0


def fetch(block, axes, offsets):
    sizes = [lax.axis_size(a) for a in axes]
    pairs = []
    total = 1
    for s in sizes:
        total *= s
    for linear in range(total):
        coords = []
        rest = linear
        for s in reversed(sizes):
            coords.append(rest % s)
            rest //= s
        coords = coords[::-1]
        source = [c + d for c, d in zip(coords, offsets)]
        if all(0 <= c < s for c, s in zip(source, sizes)):
            src_linear = 0
            for c, s in zip(source, sizes):
                src_linear = src_linear * s + c
            pairs.append((src_linear, linear))
    if len(axes) == 1:
        return lax.ppermute(block, axes[0], pairs)
    return lax.ppermute(block, tuple(axes), pairs)


def extend_y(block, width):
    ny = block.shape[-1]
    low = fetch(block[..., ny - width :], ("ty",), (-1,))
    high = fetch(block[..., :width], ("ty",), (1,))
    return jnp.concatenate([low, block, high], axis=-1)


def flat_extended(block, width, padded, lead_axes=(), lead_offsets=()):
    nx = block.shape[-2]
    pieces = {
        -1: fetch(block[..., nx - width :, :], tuple(lead_axes) + ("tx",), tuple(lead_offsets) + (-1,)),
        1: fetch(block[..., :width, :], tuple(lead_axes) + ("tx",), tuple(lead_offsets) + (1,)),
    }
    if lead_axes:
        pieces[0] = fetch(block, tuple(lead_axes) + ("tx",), tuple(lead_offsets) + (0,))
    else:
        pieces[0] = block
    segments = []
    for ix in range(nx + 2 * width):
        dx = -1 if ix < width else (0 if ix < width + nx else 1)
        r = ix - (0 if dx == -1 else (width if dx == 0 else width + nx))
        segments.append(pieces[dx][..., r, :])
    used = sum(s.shape[-1] for s in segments)
    lead = segments[0].shape[:-1]
    segments.append(jnp.zeros(lead + (padded - used,), segments[0].dtype))
    return jnp.concatenate(segments, axis=-1)


def tick_kernel(
    order_ref, frc_ref, pk_ref, inc_ref, ins_ref, bhi_ref, blo_ref, out_ref, field_ref, *, row, depth, width
):
    nsrc, rows, owned = out_ref.shape
    cols = pk_ref.shape[1]
    classes = bhi_ref.shape[1] // rows
    lanes = 128
    wave0 = pk_ref.shape[0] - depth - 2 * nsrc - 1
    label_row = wave0 + depth + 2 * nsrc
    extent = owned // lanes + 2 * width

    def edges(lo, hi):
        zrow = lax.broadcasted_iota(jnp.int32, (rows, hi - lo), 0) % depth
        return zrow == 0, zrow == depth - 1

    def precond(x, lo, hi):
        scaled = x * SPLIT
        high = scaled - (scaled - x)
        low = x - high
        label = pk_ref[pl.ds(label_row, 1), lo:hi]
        hots = [(label == float(k)).astype(jnp.float32) for k in range(classes)]
        high = jnp.concatenate([high * h for h in hots], axis=0).astype(jnp.bfloat16)
        low = jnp.concatenate([low * h for h in hots], axis=0).astype(jnp.bfloat16)
        bhi = bhi_ref[...]
        blo = blo_ref[...]
        out = jnp.dot(bhi, low, preferred_element_type=jnp.float32)
        out = out + jnp.dot(blo, high, preferred_element_type=jnp.float32)
        return out + jnp.dot(bhi, high, preferred_element_type=jnp.float32)

    def apply_a(u, lo, hi):
        span = hi - lo
        top, bottom = edges(lo, hi)
        wave = pk_ref[pl.ds(wave0, depth), lo:hi]
        dr = 6.0 - wave
        di = -DAMPING * wave
        real = u[:depth]
        imaginary = u[depth:]
        diagonal = jnp.concatenate(
            [dr * real - di * imaginary, dr * imaginary + di * real], axis=0
        )
        down = jnp.where(top, 0.0, pltpu.roll(u, 1, 0))
        up = jnp.where(bottom, 0.0, pltpu.roll(u, rows - 1, 0))
        beside = up + down
        beside = beside + pltpu.roll(u, span - row, 1) + pltpu.roll(u, row, 1)
        beside = beside + pltpu.roll(u, span - 1, 1) + pltpu.roll(u, 1, 1)
        return diagonal - beside

    def one_source(s, carry):
        first = pl.multiple_of(order_ref[s] * rows, rows)
        forcing = frc_ref[pl.ds(first, rows), :]
        incoming = inc_ref[s]
        layer = jnp.concatenate(
            [
                jnp.broadcast_to(incoming[0:1], (depth, cols)),
                jnp.broadcast_to(incoming[1:2], (depth, cols)),
            ],
            axis=0,
        )
        top, _ = edges(0, cols)
        rhs = jnp.where(top, forcing + layer, forcing)
        field_ref[...] = precond(rhs, 0, cols)
        for step in range(1, CORR + 1):
            a = (step * row) // lanes * lanes
            b = min(-(-((extent - step) * row) // lanes) * lanes, cols)
            lo = max(a - 2 * lanes, 0)
            hi = min(b + 2 * lanes, cols)
            stencil = apply_a(field_ref[:, lo:hi], lo, hi)[:, a - lo : b - lo]
            residual = ins_ref[:, a:b] * (rhs[:, a:b] - stencil)
            field_ref[:, a:b] = field_ref[:, a:b] + precond(residual, a, b)
        u = field_ref[...]
        for x in range(owned // lanes):
            begin = (x + width) * row + width
            out_ref[s, :, x * lanes : (x + 1) * lanes] = pltpu.roll(u, cols - begin, 1)[:, :lanes]
        return carry

    lax.fori_loop(0, nsrc, one_source, 0)


def run_tick(order, forcing, packed, incoming, ins, bhi, blo, row, depth, width, owned):
    nsrc = incoming.shape[0]
    rows, stacked = bhi.shape
    cols = packed.shape[1]
    flops = nsrc * (CORR + 1) * 3 * 2 * rows * stacked * cols
    vmem = pl.BlockSpec(memory_space=pltpu.VMEM)
    return pl.pallas_call(
        functools.partial(tick_kernel, row=row, depth=depth, width=width),
        out_shape=jax.ShapeDtypeStruct((nsrc, rows, owned), jnp.float32),
        in_specs=[pl.BlockSpec(memory_space=pltpu.SMEM)] + [vmem] * 6,
        out_specs=vmem,
        scratch_shapes=[pltpu.VMEM((rows, cols), jnp.float32)],
        cost_estimate=pl.CostEstimate(
            flops=flops,
            transcendentals=0,
            bytes_accessed=4 * (forcing.size + packed.size // 4 + nsrc * rows * owned),
        ),
    )(order, forcing, packed, incoming, ins, bhi, blo)


def block_matrix(inverse):
    real = inverse[:, 0]
    imaginary = inverse[:, 1]
    upper = jnp.concatenate([real, -imaginary], axis=2)
    lower = jnp.concatenate([imaginary, real], axis=2)
    return jnp.concatenate([upper, lower], axis=1)


def per_device(forcing, wavenumber_sq, line_inverse, column_class, batch_order, pending_trace):
    width = CORR
    ticks, nsrc, two, depth, nx, ny = forcing.shape
    classes = line_inverse.shape[1]
    ntx = lax.axis_size("tx")
    nty = lax.axis_size("ty")
    ex, ey = nx + 2 * width, ny + 2 * width
    cols = ex * ey
    padded = -(-cols // 128) * 128
    assert width <= nx and width <= ny

    per_tick = forcing.reshape(ticks, -1, nx, ny)
    packed = jnp.concatenate(
        [
            per_tick[0],
            wavenumber_sq,
            pending_trace.reshape(-1, nx, ny),
            column_class[0][None].astype(jnp.float32),
        ]
        + [per_tick[t] for t in range(1, ticks)],
        axis=0,
    )
    rows_now = per_tick.shape[1] + depth + nsrc * two + 1
    now = packed[:rows_now]
    low_x = fetch(now[:, nx - width :, :], ("tx",), (-1,))
    high_x = fetch(now[:, :width, :], ("tx",), (1,))
    widened = extend_y(packed, width)
    later = [
        widened[rows_now + (t - 1) * per_tick.shape[1] : rows_now + t * per_tick.shape[1]]
        for t in range(1, ticks)
    ]
    low_y = widened[:rows_now, :, :width]
    high_y = widened[:rows_now, :, width + ny :]
    rims = jnp.concatenate([low_x, high_x], axis=1)
    corner_low = fetch(rims[..., ny - width :], ("ty",), (-1,))
    corner_high = fetch(rims[..., :width], ("ty",), (1,))
    segments = []
    for ix in range(ex):
        if ix < width:
            segments += [corner_low[:, ix], low_x[:, ix], corner_high[:, ix]]
        elif ix < width + nx:
            r = ix - width
            segments += [low_y[:, r], now[:, r], high_y[:, r]]
        else:
            r = ix - width - nx
            segments += [corner_low[:, width + r], high_x[:, r], corner_high[:, width + r]]
    segments.append(jnp.zeros((rows_now, padded - cols), jnp.float32))
    packed = jnp.concatenate(segments, axis=-1)
    first_pending = nsrc * two * depth + depth

    gx = lax.axis_index("tx") * nx - width + jnp.arange(ex)
    gy = lax.axis_index("ty") * ny - width + jnp.arange(ey)
    inside = ((gx >= 0) & (gx < nx * ntx))[:, None] & ((gy >= 0) & (gy < ny * nty))[None, :]
    inside = jnp.pad(inside.reshape(1, cols).astype(jnp.float32), ((0, 0), (0, padded - cols)))

    blocks = block_matrix(line_inverse[0])
    side_by_side = jnp.concatenate([blocks[k] for k in range(classes)], axis=1)
    rounded = lax.reduce_precision(side_by_side, exponent_bits=8, mantissa_bits=7)
    bhi = rounded.astype(jnp.bfloat16)
    blo = (side_by_side - rounded).astype(jnp.bfloat16)
    orders = batch_order[:, 0]

    incoming = packed[first_pending : first_pending + nsrc * two].reshape(nsrc, two, padded)
    solutions = []
    trace = None
    forcing_f = packed
    for tick in range(ticks):
        field = run_tick(
            orders[tick], forcing_f, packed, incoming, inside, bhi, blo, ey, depth, width, nx * ny
        )
        if tick + 1 < ticks:
            field, rows = lax.optimization_barrier((field, later[tick]))
            forcing_f = flat_extended(rows, width, padded)
        tile = field.reshape(nsrc, two, depth, nx, ny)
        solutions.append(tile)
        trace = tile[:, :, depth - 1]
        if tick + 1 < ticks:
            incoming = flat_extended(extend_y(trace, width), width, padded, ("slab",), (-1,))
    return (jnp.stack(solutions, axis=0), trace[:, :, None])


def solution(mesh):
    in_specs = (
        P(None, None, None, "slab", "tx", "ty"),
        P("slab", "tx", "ty"),
        P("slab", None, None, None, None),
        P("slab", "tx", "ty"),
        P(None, "slab", None),
        P(None, None, "slab", "tx", "ty"),
    )
    out_specs = (P(None, None, None, "slab", "tx", "ty"), P(None, None, "slab", "tx", "ty"))
    return jax.shard_map(
        per_device, mesh=mesh, in_specs=in_specs, out_specs=out_specs, check_vma=False
    )
```

```python
import functools

import jax
import jax.numpy as jnp
from jax import lax
from jax.experimental import pallas as pl
from jax.experimental.pallas import tpu as pltpu
from jax.sharding import PartitionSpec as P

CORR = 3
TICKS = 2


DAMPING = 0.25
PRECISE = lax.Precision.HIGHEST
SPLIT = 65537.0


def fetch(block, axes, offsets):
    sizes = [lax.axis_size(a) for a in axes]
    pairs = []
    total = 1
    for s in sizes:
        total *= s
    for linear in range(total):
        coords = []
        rest = linear
        for s in reversed(sizes):
            coords.append(rest % s)
            rest //= s
        coords = coords[::-1]
        source = [c + d for c, d in zip(coords, offsets)]
        if all(0 <= c < s for c, s in zip(source, sizes)):
            src_linear = 0
            for c, s in zip(source, sizes):
                src_linear = src_linear * s + c
            pairs.append((src_linear, linear))
    if len(axes) == 1:
        return lax.ppermute(block, axes[0], pairs)
    return lax.ppermute(block, tuple(axes), pairs)


def extend_y(block, width):
    ny = block.shape[-1]
    low = fetch(block[..., ny - width :], ("ty",), (-1,))
    high = fetch(block[..., :width], ("ty",), (1,))
    return jnp.concatenate([low, block, high], axis=-1)


def flat_extended(block, width, padded, lead_axes=(), lead_offsets=()):
    nx = block.shape[-2]
    pieces = {
        -1: fetch(block[..., nx - width :, :], tuple(lead_axes) + ("tx",), tuple(lead_offsets) + (-1,)),
        1: fetch(block[..., :width, :], tuple(lead_axes) + ("tx",), tuple(lead_offsets) + (1,)),
    }
    if lead_axes:
        pieces[0] = fetch(block, tuple(lead_axes) + ("tx",), tuple(lead_offsets) + (0,))
    else:
        pieces[0] = block
    segments = []
    for ix in range(nx + 2 * width):
        dx = -1 if ix < width else (0 if ix < width + nx else 1)
        r = ix - (0 if dx == -1 else (width if dx == 0 else width + nx))
        segments.append(pieces[dx][..., r, :])
    used = sum(s.shape[-1] for s in segments)
    lead = segments[0].shape[:-1]
    segments.append(jnp.zeros(lead + (padded - used,), segments[0].dtype))
    return jnp.concatenate(segments, axis=-1)


def tick_kernel(
    order_ref, frc_ref, pk_ref, inc_ref, ins_ref, bhi_ref, blo_ref, out_ref, field_ref, *, row, depth, width
):
    nsrc, rows, owned = out_ref.shape
    cols = pk_ref.shape[1]
    classes = bhi_ref.shape[1] // rows
    lanes = 128
    wave0 = pk_ref.shape[0] - depth - 2 * nsrc - 1
    label_row = wave0 + depth + 2 * nsrc
    extent = owned // lanes + 2 * width

    def edges(lo, hi):
        zrow = lax.broadcasted_iota(jnp.int32, (rows, hi - lo), 0) % depth
        return zrow == 0, zrow == depth - 1

    def precond(x, lo, hi):
        scaled = x * SPLIT
        high = scaled - (scaled - x)
        low = x - high
        label = pk_ref[pl.ds(label_row, 1), lo:hi]
        hots = [(label == float(k)).astype(jnp.float32) for k in range(classes)]
        high = jnp.concatenate([high * h for h in hots], axis=0).astype(jnp.bfloat16)
        low = jnp.concatenate([low * h for h in hots], axis=0).astype(jnp.bfloat16)
        bhi = bhi_ref[...]
        blo = blo_ref[...]
        out = jnp.dot(bhi, low, preferred_element_type=jnp.float32)
        out = out + jnp.dot(blo, high, preferred_element_type=jnp.float32)
        return out + jnp.dot(bhi, high, preferred_element_type=jnp.float32)

    def apply_a(u, lo, hi):
        span = hi - lo
        top, bottom = edges(lo, hi)
        wave = pk_ref[pl.ds(wave0, depth), lo:hi]
        dr = 6.0 - wave
        di = -DAMPING * wave
        real = u[:depth]
        imaginary = u[depth:]
        diagonal = jnp.concatenate(
            [dr * real - di * imaginary, dr * imaginary + di * real], axis=0
        )
        down = jnp.where(top, 0.0, pltpu.roll(u, 1, 0))
        up = jnp.where(bottom, 0.0, pltpu.roll(u, rows - 1, 0))
        beside = up + down
        beside = beside + pltpu.roll(u, span - row, 1) + pltpu.roll(u, row, 1)
        beside = beside + pltpu.roll(u, span - 1, 1) + pltpu.roll(u, 1, 1)
        return diagonal - beside

    def one_source(s, carry):
        first = pl.multiple_of(order_ref[s] * rows, rows)
        forcing = frc_ref[pl.ds(first, rows), :]
        incoming = inc_ref[s]
        layer = jnp.concatenate(
            [
                jnp.broadcast_to(incoming[0:1], (depth, cols)),
                jnp.broadcast_to(incoming[1:2], (depth, cols)),
            ],
            axis=0,
        )
        top, _ = edges(0, cols)
        rhs = jnp.where(top, forcing + layer, forcing)
        field_ref[...] = precond(rhs, 0, cols)
        for step in range(1, CORR + 1):
            a = (step * row) // lanes * lanes
            b = min(-(-((extent - step) * row) // lanes) * lanes, cols)
            lo = max(a - 2 * lanes, 0)
            hi = min(b + 2 * lanes, cols)
            stencil = apply_a(field_ref[:, lo:hi], lo, hi)[:, a - lo : b - lo]
            residual = ins_ref[:, a:b] * (rhs[:, a:b] - stencil)
            field_ref[:, a:b] = field_ref[:, a:b] + precond(residual, a, b)
        u = field_ref[...]
        for x in range(owned // lanes):
            begin = (x + width) * row + width
            out_ref[s, :, x * lanes : (x + 1) * lanes] = pltpu.roll(u, cols - begin, 1)[:, :lanes]
        return carry

    lax.fori_loop(0, nsrc, one_source, 0)


def run_tick(order, forcing, packed, incoming, ins, bhi, blo, row, depth, width, owned):
    nsrc = incoming.shape[0]
    rows, stacked = bhi.shape
    cols = packed.shape[1]
    flops = nsrc * (CORR + 1) * 3 * 2 * rows * stacked * cols
    vmem = pl.BlockSpec(memory_space=pltpu.VMEM)
    return pl.pallas_call(
        functools.partial(tick_kernel, row=row, depth=depth, width=width),
        out_shape=jax.ShapeDtypeStruct((nsrc, rows, owned), jnp.float32),
        in_specs=[pl.BlockSpec(memory_space=pltpu.SMEM)] + [vmem] * 6,
        out_specs=vmem,
        scratch_shapes=[pltpu.VMEM((rows, cols), jnp.float32)],
        cost_estimate=pl.CostEstimate(
            flops=flops,
            transcendentals=0,
            bytes_accessed=4 * (forcing.size + packed.size // 4 + nsrc * rows * owned),
        ),
    )(order, forcing, packed, incoming, ins, bhi, blo)


def block_matrix(inverse):
    real = inverse[:, 0]
    imaginary = inverse[:, 1]
    upper = jnp.concatenate([real, -imaginary], axis=2)
    lower = jnp.concatenate([imaginary, real], axis=2)
    return jnp.concatenate([upper, lower], axis=1)


def per_device(forcing, wavenumber_sq, line_inverse, column_class, batch_order, pending_trace):
    width = CORR
    ticks, nsrc, two, depth, nx, ny = forcing.shape
    classes = line_inverse.shape[1]
    ntx = lax.axis_size("tx")
    nty = lax.axis_size("ty")
    ex, ey = nx + 2 * width, ny + 2 * width
    cols = ex * ey
    padded = -(-cols // 128) * 128
    assert width <= nx and width <= ny

    per_tick = forcing.reshape(ticks, -1, nx, ny)
    packed = jnp.concatenate(
        [
            per_tick[0],
            wavenumber_sq,
            pending_trace.reshape(-1, nx, ny),
            column_class[0][None].astype(jnp.float32),
        ]
        + [per_tick[t] for t in range(1, ticks)],
        axis=0,
    )
    rows_now = per_tick.shape[1] + depth + nsrc * two + 1
    now = packed[:rows_now]
    low_x = fetch(now[:, nx - width :, :], ("tx",), (-1,))
    high_x = fetch(now[:, :width, :], ("tx",), (1,))
    widened = extend_y(packed, width)
    later = [
        widened[rows_now + (t - 1) * per_tick.shape[1] : rows_now + t * per_tick.shape[1]]
        for t in range(1, ticks)
    ]
    rims = jnp.concatenate([low_x, high_x], axis=1)
    corner_low = fetch(rims[..., ny - width :], ("ty",), (-1,))
    corner_high = fetch(rims[..., :width], ("ty",), (1,))
    rims = jnp.concatenate([corner_low, rims, corner_high], axis=-1)
    segments = []
    for ix in range(ex):
        if ix < width:
            segments.append(rims[:, ix])
        elif ix < width + nx:
            segments.append(widened[:rows_now, ix - width])
        else:
            segments.append(rims[:, ix - nx])
    segments.append(jnp.zeros((rows_now, padded - cols), jnp.float32))
    packed = jnp.concatenate(segments, axis=-1)
    first_pending = nsrc * two * depth + depth

    gx = lax.axis_index("tx") * nx - width + jnp.arange(ex)
    gy = lax.axis_index("ty") * ny - width + jnp.arange(ey)
    inside = ((gx >= 0) & (gx < nx * ntx))[:, None] & ((gy >= 0) & (gy < ny * nty))[None, :]
    inside = jnp.pad(inside.reshape(1, cols).astype(jnp.float32), ((0, 0), (0, padded - cols)))

    blocks = block_matrix(line_inverse[0])
    side_by_side = jnp.concatenate([blocks[k] for k in range(classes)], axis=1)
    rounded = lax.reduce_precision(side_by_side, exponent_bits=8, mantissa_bits=7)
    bhi = rounded.astype(jnp.bfloat16)
    blo = (side_by_side - rounded).astype(jnp.bfloat16)
    orders = batch_order[:, 0]

    incoming = packed[first_pending : first_pending + nsrc * two].reshape(nsrc, two, padded)
    solutions = []
    trace = None
    forcing_f = packed
    for tick in range(ticks):
        field = run_tick(
            orders[tick], forcing_f, packed, incoming, inside, bhi, blo, ey, depth, width, nx * ny
        )
        if tick + 1 < ticks:
            field, rows = lax.optimization_barrier((field, later[tick]))
            forcing_f = flat_extended(rows, width, padded)
        tile = field.reshape(nsrc, two, depth, nx, ny)
        solutions.append(tile)
        trace = tile[:, :, depth - 1]
        if tick + 1 < ticks:
            incoming = flat_extended(extend_y(trace, width), width, padded, ("slab",), (-1,))
    return (jnp.stack(solutions, axis=0), trace[:, :, None])


def solution(mesh):
    in_specs = (
        P(None, None, None, "slab", "tx", "ty"),
        P("slab", "tx", "ty"),
        P("slab", None, None, None, None),
        P("slab", "tx", "ty"),
        P(None, "slab", None),
        P(None, None, "slab", "tx", "ty"),
    )
    out_specs = (P(None, None, None, "slab", "tx", "ty"), P(None, None, "slab", "tx", "ty"))
    return jax.shard_map(
        per_device, mesh=mesh, in_specs=in_specs, out_specs=out_specs, check_vma=False
    )
```

```python
import functools

import jax
import jax.numpy as jnp
from jax import lax
from jax.experimental import pallas as pl
from jax.experimental.pallas import tpu as pltpu
from jax.sharding import PartitionSpec as P

CORR = 3
TICKS = 2


DAMPING = 0.25
PRECISE = lax.Precision.HIGHEST
SPLIT = 65537.0


def fetch(block, axes, offsets):
    sizes = [lax.axis_size(a) for a in axes]
    pairs = []
    total = 1
    for s in sizes:
        total *= s
    for linear in range(total):
        coords = []
        rest = linear
        for s in reversed(sizes):
            coords.append(rest % s)
            rest //= s
        coords = coords[::-1]
        source = [c + d for c, d in zip(coords, offsets)]
        if all(0 <= c < s for c, s in zip(source, sizes)):
            src_linear = 0
            for c, s in zip(source, sizes):
                src_linear = src_linear * s + c
            pairs.append((src_linear, linear))
    if len(axes) == 1:
        return lax.ppermute(block, axes[0], pairs)
    return lax.ppermute(block, tuple(axes), pairs)


def extend_y(block, width):
    ny = block.shape[-1]
    low = fetch(block[..., ny - width :], ("ty",), (-1,))
    high = fetch(block[..., :width], ("ty",), (1,))
    return jnp.concatenate([low, block, high], axis=-1)


def flat_extended(block, width, padded, lead_axes=(), lead_offsets=()):
    nx = block.shape[-2]
    pieces = {
        -1: fetch(block[..., nx - width :, :], tuple(lead_axes) + ("tx",), tuple(lead_offsets) + (-1,)),
        1: fetch(block[..., :width, :], tuple(lead_axes) + ("tx",), tuple(lead_offsets) + (1,)),
    }
    if lead_axes:
        pieces[0] = fetch(block, tuple(lead_axes) + ("tx",), tuple(lead_offsets) + (0,))
    else:
        pieces[0] = block
    segments = []
    for ix in range(nx + 2 * width):
        dx = -1 if ix < width else (0 if ix < width + nx else 1)
        r = ix - (0 if dx == -1 else (width if dx == 0 else width + nx))
        segments.append(pieces[dx][..., r, :])
    used = sum(s.shape[-1] for s in segments)
    lead = segments[0].shape[:-1]
    segments.append(jnp.zeros(lead + (padded - used,), segments[0].dtype))
    return jnp.concatenate(segments, axis=-1)


def tick_kernel(
    order_ref, frc_ref, pk_ref, inc_ref, ins_ref, bhi_ref, blo_ref, out_ref, field_ref, *, row, depth, width
):
    nsrc, rows, owned = out_ref.shape
    cols = pk_ref.shape[1]
    classes = bhi_ref.shape[1] // rows
    lanes = 128
    wave0 = pk_ref.shape[0] - depth - 2 * nsrc - 1
    label_row = wave0 + depth + 2 * nsrc
    extent = owned // lanes + 2 * width

    def edges(lo, hi):
        zrow = lax.broadcasted_iota(jnp.int32, (rows, hi - lo), 0) % depth
        return zrow == 0, zrow == depth - 1

    def precond(x, lo, hi):
        scaled = x * SPLIT
        high = scaled - (scaled - x)
        low = x - high
        label = pk_ref[pl.ds(label_row, 1), lo:hi]
        hots = [(label == float(k)).astype(jnp.float32) for k in range(classes)]
        high = jnp.concatenate([high * h for h in hots], axis=0).astype(jnp.bfloat16)
        low = jnp.concatenate([low * h for h in hots], axis=0).astype(jnp.bfloat16)
        bhi = bhi_ref[...]
        blo = blo_ref[...]
        out = jnp.dot(bhi, low, preferred_element_type=jnp.float32)
        out = out + jnp.dot(blo, high, preferred_element_type=jnp.float32)
        return out + jnp.dot(bhi, high, preferred_element_type=jnp.float32)

    def apply_a(u, lo, hi):
        span = hi - lo
        top, bottom = edges(lo, hi)
        wave = pk_ref[pl.ds(wave0, depth), lo:hi]
        dr = 6.0 - wave
        di = -DAMPING * wave
        real = u[:depth]
        imaginary = u[depth:]
        diagonal = jnp.concatenate(
            [dr * real - di * imaginary, dr * imaginary + di * real], axis=0
        )
        down = jnp.where(top, 0.0, pltpu.roll(u, 1, 0))
        up = jnp.where(bottom, 0.0, pltpu.roll(u, rows - 1, 0))
        beside = up + down
        beside = beside + pltpu.roll(u, span - row, 1) + pltpu.roll(u, row, 1)
        beside = beside + pltpu.roll(u, span - 1, 1) + pltpu.roll(u, 1, 1)
        return diagonal - beside

    def one_source(s, carry):
        first = pl.multiple_of(order_ref[s] * rows, rows)
        forcing = frc_ref[pl.ds(first, rows), :]
        incoming = inc_ref[s]
        layer = jnp.concatenate(
            [
                jnp.broadcast_to(incoming[0:1], (depth, cols)),
                jnp.broadcast_to(incoming[1:2], (depth, cols)),
            ],
            axis=0,
        )
        top, _ = edges(0, cols)
        rhs = jnp.where(top, forcing + layer, forcing)
        field_ref[...] = precond(rhs, 0, cols)
        for step in range(1, CORR + 1):
            a = (step * row) // lanes * lanes
            b = min(-(-((extent - step) * row) // lanes) * lanes, cols)
            lo = max(a - 2 * lanes, 0)
            hi = min(b + 2 * lanes, cols)
            stencil = apply_a(field_ref[:, lo:hi], lo, hi)[:, a - lo : b - lo]
            residual = ins_ref[:, a:b] * (rhs[:, a:b] - stencil)
            field_ref[:, a:b] = field_ref[:, a:b] + precond(residual, a, b)
        u = field_ref[...]
        for x in range(owned // lanes):
            begin = (x + width) * row + width
            out_ref[s, :, x * lanes : (x + 1) * lanes] = pltpu.roll(u, cols - begin, 1)[:, :lanes]
        return carry

    lax.fori_loop(0, nsrc, one_source, 0)


def run_tick(order, forcing, packed, incoming, ins, bhi, blo, row, depth, width, owned):
    nsrc = incoming.shape[0]
    rows, stacked = bhi.shape
    cols = packed.shape[1]
    flops = nsrc * (CORR + 1) * 3 * 2 * rows * stacked * cols
    vmem = pl.BlockSpec(memory_space=pltpu.VMEM)
    return pl.pallas_call(
        functools.partial(tick_kernel, row=row, depth=depth, width=width),
        out_shape=jax.ShapeDtypeStruct((nsrc, rows, owned), jnp.float32),
        in_specs=[pl.BlockSpec(memory_space=pltpu.SMEM)] + [vmem] * 6,
        out_specs=vmem,
        scratch_shapes=[pltpu.VMEM((rows, cols), jnp.float32)],
        cost_estimate=pl.CostEstimate(
            flops=flops,
            transcendentals=0,
            bytes_accessed=4 * (forcing.size + packed.size // 4 + nsrc * rows * owned),
        ),
    )(order, forcing, packed, incoming, ins, bhi, blo)


def block_matrix(inverse):
    real = inverse[:, 0]
    imaginary = inverse[:, 1]
    upper = jnp.concatenate([real, -imaginary], axis=2)
    lower = jnp.concatenate([imaginary, real], axis=2)
    return jnp.concatenate([upper, lower], axis=1)


def per_device(forcing, wavenumber_sq, line_inverse, column_class, batch_order, pending_trace):
    width = CORR
    ticks, nsrc, two, depth, nx, ny = forcing.shape
    classes = line_inverse.shape[1]
    ntx = lax.axis_size("tx")
    nty = lax.axis_size("ty")
    ex, ey = nx + 2 * width, ny + 2 * width
    cols = ex * ey
    padded = -(-cols // 128) * 128
    assert width <= nx and width <= ny

    per_tick = forcing.reshape(ticks, -1, nx, ny)
    packed = jnp.concatenate(
        [
            per_tick[0],
            wavenumber_sq,
            pending_trace.reshape(-1, nx, ny),
            column_class[0][None].astype(jnp.float32),
        ]
        + [per_tick[t] for t in range(1, ticks)],
        axis=0,
    )
    rows_now = per_tick.shape[1] + depth + nsrc * two + 1
    now = packed[:rows_now]
    low_x = fetch(now[:, nx - width :, :], ("tx",), (-1,))
    high_x = fetch(now[:, :width, :], ("tx",), (1,))
    widened = extend_y(packed, width)
    later = [
        widened[rows_now + (t - 1) * per_tick.shape[1] : rows_now + t * per_tick.shape[1]]
        for t in range(1, ticks)
    ]
    corner = {}
    for dx, rows in ((-1, slice(nx - width, nx)), (1, slice(0, width))):
        for dy, lanes in ((-1, slice(ny - width, ny)), (1, slice(0, width))):
            corner[dx, dy] = fetch(now[:, rows, lanes], ("tx", "ty"), (dx, dy))
    rims_low = jnp.concatenate([corner[-1, -1], low_x, corner[-1, 1]], axis=-1)
    rims_high = jnp.concatenate([corner[1, -1], high_x, corner[1, 1]], axis=-1)
    segments = []
    for ix in range(ex):
        if ix < width:
            segments.append(rims_low[:, ix])
        elif ix < width + nx:
            segments.append(widened[:rows_now, ix - width])
        else:
            segments.append(rims_high[:, ix - width - nx])
    segments.append(jnp.zeros((rows_now, padded - cols), jnp.float32))
    packed = jnp.concatenate(segments, axis=-1)
    first_pending = nsrc * two * depth + depth

    gx = lax.axis_index("tx") * nx - width + jnp.arange(ex)
    gy = lax.axis_index("ty") * ny - width + jnp.arange(ey)
    inside = ((gx >= 0) & (gx < nx * ntx))[:, None] & ((gy >= 0) & (gy < ny * nty))[None, :]
    inside = jnp.pad(inside.reshape(1, cols).astype(jnp.float32), ((0, 0), (0, padded - cols)))

    blocks = block_matrix(line_inverse[0])
    side_by_side = jnp.concatenate([blocks[k] for k in range(classes)], axis=1)
    rounded = lax.reduce_precision(side_by_side, exponent_bits=8, mantissa_bits=7)
    bhi = rounded.astype(jnp.bfloat16)
    blo = (side_by_side - rounded).astype(jnp.bfloat16)
    orders = batch_order[:, 0]

    incoming = packed[first_pending : first_pending + nsrc * two].reshape(nsrc, two, padded)
    solutions = []
    trace = None
    forcing_f = packed
    for tick in range(ticks):
        field = run_tick(
            orders[tick], forcing_f, packed, incoming, inside, bhi, blo, ey, depth, width, nx * ny
        )
        if tick + 1 < ticks:
            field, rows = lax.optimization_barrier((field, later[tick]))
            forcing_f = flat_extended(rows, width, padded)
        tile = field.reshape(nsrc, two, depth, nx, ny)
        solutions.append(tile)
        trace = tile[:, :, depth - 1]
        if tick + 1 < ticks:
            incoming = flat_extended(extend_y(trace, width), width, padded, ("slab",), (-1,))
    return (jnp.stack(solutions, axis=0), trace[:, :, None])


def solution(mesh):
    in_specs = (
        P(None, None, None, "slab", "tx", "ty"),
        P("slab", "tx", "ty"),
        P("slab", None, None, None, None),
        P("slab", "tx", "ty"),
        P(None, "slab", None),
        P(None, None, "slab", "tx", "ty"),
    )
    out_specs = (P(None, None, None, "slab", "tx", "ty"), P(None, None, "slab", "tx", "ty"))
    return jax.shard_map(
        per_device, mesh=mesh, in_specs=in_specs, out_specs=out_specs, check_vma=False
    )
```

```python
import functools

import jax
import jax.numpy as jnp
from jax import lax
from jax.experimental import pallas as pl
from jax.experimental.pallas import tpu as pltpu
from jax.sharding import PartitionSpec as P

CORR = 3
TICKS = 2


DAMPING = 0.25
PRECISE = lax.Precision.HIGHEST
SPLIT = 65537.0


def fetch(block, axes, offsets):
    sizes = [lax.axis_size(a) for a in axes]
    pairs = []
    total = 1
    for s in sizes:
        total *= s
    for linear in range(total):
        coords = []
        rest = linear
        for s in reversed(sizes):
            coords.append(rest % s)
            rest //= s
        coords = coords[::-1]
        source = [c + d for c, d in zip(coords, offsets)]
        if all(0 <= c < s for c, s in zip(source, sizes)):
            src_linear = 0
            for c, s in zip(source, sizes):
                src_linear = src_linear * s + c
            pairs.append((src_linear, linear))
    if len(axes) == 1:
        return lax.ppermute(block, axes[0], pairs)
    return lax.ppermute(block, tuple(axes), pairs)


def extend_y(block, width):
    ny = block.shape[-1]
    low = fetch(block[..., ny - width :], ("ty",), (-1,))
    high = fetch(block[..., :width], ("ty",), (1,))
    return jnp.concatenate([low, block, high], axis=-1)


def flat_extended(block, width, padded, lead_axes=(), lead_offsets=()):
    nx = block.shape[-2]
    pieces = {
        -1: fetch(block[..., nx - width :, :], tuple(lead_axes) + ("tx",), tuple(lead_offsets) + (-1,)),
        1: fetch(block[..., :width, :], tuple(lead_axes) + ("tx",), tuple(lead_offsets) + (1,)),
    }
    if lead_axes:
        pieces[0] = fetch(block, tuple(lead_axes) + ("tx",), tuple(lead_offsets) + (0,))
    else:
        pieces[0] = block
    segments = []
    for ix in range(nx + 2 * width):
        dx = -1 if ix < width else (0 if ix < width + nx else 1)
        r = ix - (0 if dx == -1 else (width if dx == 0 else width + nx))
        segments.append(pieces[dx][..., r, :])
    used = sum(s.shape[-1] for s in segments)
    lead = segments[0].shape[:-1]
    segments.append(jnp.zeros(lead + (padded - used,), segments[0].dtype))
    return jnp.concatenate(segments, axis=-1)


def tick_kernel(
    order_ref, frc_ref, pk_ref, inc_ref, ins_ref, bhi_ref, blo_ref, out_ref, field_ref, *, row, depth, width
):
    nsrc, rows, owned = out_ref.shape
    cols = pk_ref.shape[1]
    classes = bhi_ref.shape[1] // rows
    lanes = 128
    wave0 = pk_ref.shape[0] - depth - 2 * nsrc - 1
    label_row = wave0 + depth + 2 * nsrc
    extent = owned // lanes + 2 * width

    def edges(lo, hi):
        zrow = lax.broadcasted_iota(jnp.int32, (rows, hi - lo), 0) % depth
        return zrow == 0, zrow == depth - 1

    def precond(x, lo, hi):
        scaled = x * SPLIT
        high = scaled - (scaled - x)
        low = x - high
        label = pk_ref[pl.ds(label_row, 1), lo:hi]
        hots = [(label == float(k)).astype(jnp.bfloat16) for k in range(classes)]
        high = high.astype(jnp.bfloat16)
        low = low.astype(jnp.bfloat16)
        high = jnp.concatenate([high * h for h in hots], axis=0)
        low = jnp.concatenate([low * h for h in hots], axis=0)
        bhi = bhi_ref[...]
        blo = blo_ref[...]
        out = jnp.dot(bhi, low, preferred_element_type=jnp.float32)
        out = out + jnp.dot(blo, high, preferred_element_type=jnp.float32)
        return out + jnp.dot(bhi, high, preferred_element_type=jnp.float32)

    def apply_a(u, lo, hi):
        span = hi - lo
        top, bottom = edges(lo, hi)
        wave = pk_ref[pl.ds(wave0, depth), lo:hi]
        dr = 6.0 - wave
        di = -DAMPING * wave
        real = u[:depth]
        imaginary = u[depth:]
        diagonal = jnp.concatenate(
            [dr * real - di * imaginary, dr * imaginary + di * real], axis=0
        )
        down = jnp.where(top, 0.0, pltpu.roll(u, 1, 0))
        up = jnp.where(bottom, 0.0, pltpu.roll(u, rows - 1, 0))
        beside = up + down
        beside = beside + pltpu.roll(u, span - row, 1) + pltpu.roll(u, row, 1)
        beside = beside + pltpu.roll(u, span - 1, 1) + pltpu.roll(u, 1, 1)
        return diagonal - beside

    def one_source(s, carry):
        first = pl.multiple_of(order_ref[s] * rows, rows)
        forcing = frc_ref[pl.ds(first, rows), :]
        incoming = inc_ref[s]
        layer = jnp.concatenate(
            [
                jnp.broadcast_to(incoming[0:1], (depth, cols)),
                jnp.broadcast_to(incoming[1:2], (depth, cols)),
            ],
            axis=0,
        )
        top, _ = edges(0, cols)
        rhs = jnp.where(top, forcing + layer, forcing)
        field_ref[...] = precond(rhs, 0, cols)
        for step in range(1, CORR + 1):
            a = (step * row) // lanes * lanes
            b = min(-(-((extent - step) * row) // lanes) * lanes, cols)
            lo = max(a - 2 * lanes, 0)
            hi = min(b + 2 * lanes, cols)
            stencil = apply_a(field_ref[:, lo:hi], lo, hi)[:, a - lo : b - lo]
            residual = ins_ref[:, a:b] * (rhs[:, a:b] - stencil)
            field_ref[:, a:b] = field_ref[:, a:b] + precond(residual, a, b)
        u = field_ref[...]
        for x in range(owned // lanes):
            begin = (x + width) * row + width
            out_ref[s, :, x * lanes : (x + 1) * lanes] = pltpu.roll(u, cols - begin, 1)[:, :lanes]
        return carry

    lax.fori_loop(0, nsrc, one_source, 0)


def run_tick(order, forcing, packed, incoming, ins, bhi, blo, row, depth, width, owned):
    nsrc = incoming.shape[0]
    rows, stacked = bhi.shape
    cols = packed.shape[1]
    flops = nsrc * (CORR + 1) * 3 * 2 * rows * stacked * cols
    vmem = pl.BlockSpec(memory_space=pltpu.VMEM)
    return pl.pallas_call(
        functools.partial(tick_kernel, row=row, depth=depth, width=width),
        out_shape=jax.ShapeDtypeStruct((nsrc, rows, owned), jnp.float32),
        in_specs=[pl.BlockSpec(memory_space=pltpu.SMEM)] + [vmem] * 6,
        out_specs=vmem,
        scratch_shapes=[pltpu.VMEM((rows, cols), jnp.float32)],
        cost_estimate=pl.CostEstimate(
            flops=flops,
            transcendentals=0,
            bytes_accessed=4 * (forcing.size + packed.size // 4 + nsrc * rows * owned),
        ),
    )(order, forcing, packed, incoming, ins, bhi, blo)


def block_matrix(inverse):
    real = inverse[:, 0]
    imaginary = inverse[:, 1]
    upper = jnp.concatenate([real, -imaginary], axis=2)
    lower = jnp.concatenate([imaginary, real], axis=2)
    return jnp.concatenate([upper, lower], axis=1)


def per_device(forcing, wavenumber_sq, line_inverse, column_class, batch_order, pending_trace):
    width = CORR
    ticks, nsrc, two, depth, nx, ny = forcing.shape
    classes = line_inverse.shape[1]
    ntx = lax.axis_size("tx")
    nty = lax.axis_size("ty")
    ex, ey = nx + 2 * width, ny + 2 * width
    cols = ex * ey
    padded = -(-cols // 128) * 128
    assert width <= nx and width <= ny

    per_tick = forcing.reshape(ticks, -1, nx, ny)
    packed = jnp.concatenate(
        [
            per_tick[0],
            wavenumber_sq,
            pending_trace.reshape(-1, nx, ny),
            column_class[0][None].astype(jnp.float32),
        ]
        + [per_tick[t] for t in range(1, ticks)],
        axis=0,
    )
    rows_now = per_tick.shape[1] + depth + nsrc * two + 1
    now = packed[:rows_now]
    low_x = fetch(now[:, nx - width :, :], ("tx",), (-1,))
    high_x = fetch(now[:, :width, :], ("tx",), (1,))
    widened = extend_y(packed, width)
    later = [
        widened[rows_now + (t - 1) * per_tick.shape[1] : rows_now + t * per_tick.shape[1]]
        for t in range(1, ticks)
    ]
    rims = jnp.concatenate([low_x, high_x], axis=1)
    corner_low = fetch(rims[..., ny - width :], ("ty",), (-1,))
    corner_high = fetch(rims[..., :width], ("ty",), (1,))
    rims = jnp.concatenate([corner_low, rims, corner_high], axis=-1)
    segments = []
    for ix in range(ex):
        if ix < width:
            segments.append(rims[:, ix])
        elif ix < width + nx:
            segments.append(widened[:rows_now, ix - width])
        else:
            segments.append(rims[:, ix - nx])
    segments.append(jnp.zeros((rows_now, padded - cols), jnp.float32))
    packed = jnp.concatenate(segments, axis=-1)
    first_pending = nsrc * two * depth + depth

    gx = lax.axis_index("tx") * nx - width + jnp.arange(ex)
    gy = lax.axis_index("ty") * ny - width + jnp.arange(ey)
    inside = ((gx >= 0) & (gx < nx * ntx))[:, None] & ((gy >= 0) & (gy < ny * nty))[None, :]
    inside = jnp.pad(inside.reshape(1, cols).astype(jnp.float32), ((0, 0), (0, padded - cols)))

    blocks = block_matrix(line_inverse[0])
    side_by_side = jnp.concatenate([blocks[k] for k in range(classes)], axis=1)
    rounded = lax.reduce_precision(side_by_side, exponent_bits=8, mantissa_bits=7)
    bhi = rounded.astype(jnp.bfloat16)
    blo = (side_by_side - rounded).astype(jnp.bfloat16)
    orders = batch_order[:, 0]

    incoming = packed[first_pending : first_pending + nsrc * two].reshape(nsrc, two, padded)
    solutions = []
    trace = None
    forcing_f = packed
    for tick in range(ticks):
        field = run_tick(
            orders[tick], forcing_f, packed, incoming, inside, bhi, blo, ey, depth, width, nx * ny
        )
        if tick + 1 < ticks:
            field, rows = lax.optimization_barrier((field, later[tick]))
            forcing_f = flat_extended(rows, width, padded)
        tile = field.reshape(nsrc, two, depth, nx, ny)
        solutions.append(tile)
        trace = tile[:, :, depth - 1]
        if tick + 1 < ticks:
            incoming = flat_extended(extend_y(trace, width), width, padded, ("slab",), (-1,))
    return (jnp.stack(solutions, axis=0), trace[:, :, None])


def solution(mesh):
    in_specs = (
        P(None, None, None, "slab", "tx", "ty"),
        P("slab", "tx", "ty"),
        P("slab", None, None, None, None),
        P("slab", "tx", "ty"),
        P(None, "slab", None),
        P(None, None, "slab", "tx", "ty"),
    )
    out_specs = (P(None, None, None, "slab", "tx", "ty"), P(None, None, "slab", "tx", "ty"))
    return jax.shard_map(
        per_device, mesh=mesh, in_specs=in_specs, out_specs=out_specs, check_vma=False
    )
```

```python
import functools

import jax
import jax.numpy as jnp
from jax import lax
from jax.experimental import pallas as pl
from jax.experimental.pallas import tpu as pltpu
from jax.sharding import PartitionSpec as P

CORR = 3
TICKS = 2


DAMPING = 0.25
PRECISE = lax.Precision.HIGHEST
SPLIT = 65537.0


def fetch(block, axes, offsets):
    sizes = [lax.axis_size(a) for a in axes]
    pairs = []
    total = 1
    for s in sizes:
        total *= s
    for linear in range(total):
        coords = []
        rest = linear
        for s in reversed(sizes):
            coords.append(rest % s)
            rest //= s
        coords = coords[::-1]
        source = [c + d for c, d in zip(coords, offsets)]
        if all(0 <= c < s for c, s in zip(source, sizes)):
            src_linear = 0
            for c, s in zip(source, sizes):
                src_linear = src_linear * s + c
            pairs.append((src_linear, linear))
    if len(axes) == 1:
        return lax.ppermute(block, axes[0], pairs)
    return lax.ppermute(block, tuple(axes), pairs)


def extend_y(block, width):
    ny = block.shape[-1]
    low = fetch(block[..., ny - width :], ("ty",), (-1,))
    high = fetch(block[..., :width], ("ty",), (1,))
    return jnp.concatenate([low, block, high], axis=-1)


def flat_extended(block, width, padded, lead_axes=(), lead_offsets=()):
    nx = block.shape[-2]
    pieces = {
        -1: fetch(block[..., nx - width :, :], tuple(lead_axes) + ("tx",), tuple(lead_offsets) + (-1,)),
        1: fetch(block[..., :width, :], tuple(lead_axes) + ("tx",), tuple(lead_offsets) + (1,)),
    }
    if lead_axes:
        pieces[0] = fetch(block, tuple(lead_axes) + ("tx",), tuple(lead_offsets) + (0,))
    else:
        pieces[0] = block
    segments = []
    for ix in range(nx + 2 * width):
        dx = -1 if ix < width else (0 if ix < width + nx else 1)
        r = ix - (0 if dx == -1 else (width if dx == 0 else width + nx))
        segments.append(pieces[dx][..., r, :])
    used = sum(s.shape[-1] for s in segments)
    lead = segments[0].shape[:-1]
    segments.append(jnp.zeros(lead + (padded - used,), segments[0].dtype))
    return jnp.concatenate(segments, axis=-1)


def tick_kernel(
    order_ref, frc_ref, pk_ref, inc_ref, ins_ref, bhi_ref, blo_ref, out_ref, field_ref, *, row, depth, width
):
    nsrc, rows, owned = out_ref.shape
    cols = pk_ref.shape[1]
    classes = bhi_ref.shape[1] // rows
    lanes = 128
    wave0 = pk_ref.shape[0] - depth - 2 * nsrc - 1
    label_row = wave0 + depth + 2 * nsrc
    extent = owned // lanes + 2 * width

    def edges(lo, hi):
        zrow = lax.broadcasted_iota(jnp.int32, (rows, hi - lo), 0) % depth
        return zrow == 0, zrow == depth - 1

    def precond(x, lo, hi):
        scaled = x * SPLIT
        high = scaled - (scaled - x)
        low = x - high
        label = pk_ref[pl.ds(label_row, 1), lo:hi]
        hots = [(label == float(k)).astype(jnp.bfloat16) for k in range(classes)]
        high = high.astype(jnp.bfloat16)
        low = low.astype(jnp.bfloat16)
        high = jnp.concatenate([high * h for h in hots], axis=0)
        low = jnp.concatenate([low * h for h in hots], axis=0)
        bhi = bhi_ref[...]
        blo = blo_ref[...]
        out = jnp.dot(bhi, low, preferred_element_type=jnp.float32)
        out = out + jnp.dot(blo, high, preferred_element_type=jnp.float32)
        return out + jnp.dot(bhi, high, preferred_element_type=jnp.float32)

    def apply_a(u, lo, hi):
        span = hi - lo
        top, bottom = edges(lo, hi)
        wave = pk_ref[pl.ds(wave0, depth), lo:hi]
        dr = 6.0 - wave
        di = -DAMPING * wave
        real = u[:depth]
        imaginary = u[depth:]
        diagonal = jnp.concatenate(
            [dr * real - di * imaginary, dr * imaginary + di * real], axis=0
        )
        down = jnp.where(top, 0.0, pltpu.roll(u, 1, 0))
        up = jnp.where(bottom, 0.0, pltpu.roll(u, rows - 1, 0))
        beside = up + down
        beside = beside + pltpu.roll(u, span - row, 1) + pltpu.roll(u, row, 1)
        beside = beside + pltpu.roll(u, span - 1, 1) + pltpu.roll(u, 1, 1)
        return diagonal - beside

    def one_source(s, carry):
        first = pl.multiple_of(order_ref[s] * rows, rows)
        forcing = frc_ref[pl.ds(first, rows), :]
        incoming = inc_ref[s]
        layer = jnp.concatenate(
            [
                jnp.broadcast_to(incoming[0:1], (depth, cols)),
                jnp.broadcast_to(incoming[1:2], (depth, cols)),
            ],
            axis=0,
        )
        top, _ = edges(0, cols)
        rhs = jnp.where(top, forcing + layer, forcing)
        field_ref[...] = precond(rhs, 0, cols)
        for step in range(1, CORR + 1):
            a = (step * row) // lanes * lanes
            b = min(-(-((extent - step) * row) // lanes) * lanes, cols)
            lo = max(a - 2 * lanes, 0)
            hi = min(b + 2 * lanes, cols)
            stencil = apply_a(field_ref[:, lo:hi], lo, hi)[:, a - lo : b - lo]
            residual = ins_ref[:, a:b] * (rhs[:, a:b] - stencil)
            field_ref[:, a:b] = field_ref[:, a:b] + precond(residual, a, b)
        u = field_ref[...]
        for x in range(owned // lanes):
            begin = (x + width) * row + width
            out_ref[s, :, x * lanes : (x + 1) * lanes] = pltpu.roll(u, cols - begin, 1)[:, :lanes]
        return carry

    lax.fori_loop(0, nsrc, one_source, 0)


def run_tick(order, forcing, packed, incoming, ins, bhi, blo, row, depth, width, owned):
    nsrc = incoming.shape[0]
    rows, stacked = bhi.shape
    cols = packed.shape[1]
    flops = nsrc * (CORR + 1) * 3 * 2 * rows * stacked * cols
    vmem = pl.BlockSpec(memory_space=pltpu.VMEM)
    return pl.pallas_call(
        functools.partial(tick_kernel, row=row, depth=depth, width=width),
        out_shape=jax.ShapeDtypeStruct((nsrc, rows, owned), jnp.float32),
        in_specs=[pl.BlockSpec(memory_space=pltpu.SMEM)] + [vmem] * 6,
        out_specs=vmem,
        scratch_shapes=[pltpu.VMEM((rows, cols), jnp.float32)],
        cost_estimate=pl.CostEstimate(
            flops=flops,
            transcendentals=0,
            bytes_accessed=4 * (forcing.size + packed.size // 4 + nsrc * rows * owned),
        ),
    )(order, forcing, packed, incoming, ins, bhi, blo)


def block_matrix(inverse):
    real = inverse[:, 0]
    imaginary = inverse[:, 1]
    upper = jnp.concatenate([real, -imaginary], axis=2)
    lower = jnp.concatenate([imaginary, real], axis=2)
    return jnp.concatenate([upper, lower], axis=1)


def per_device(forcing, wavenumber_sq, line_inverse, column_class, batch_order, pending_trace):
    width = CORR
    ticks, nsrc, two, depth, nx, ny = forcing.shape
    classes = line_inverse.shape[1]
    ntx = lax.axis_size("tx")
    nty = lax.axis_size("ty")
    ex, ey = nx + 2 * width, ny + 2 * width
    cols = ex * ey
    padded = -(-cols // 128) * 128
    assert width <= nx and width <= ny

    per_tick = forcing.reshape(ticks, -1, nx, ny)
    packed = jnp.concatenate(
        [
            per_tick[0],
            wavenumber_sq,
            pending_trace.reshape(-1, nx, ny),
            column_class[0][None].astype(jnp.float32),
        ]
        + [per_tick[t] for t in range(1, ticks)],
        axis=0,
    )
    rows_now = per_tick.shape[1] + depth + nsrc * two + 1
    now = packed[:rows_now]
    low_x = fetch(now[:, nx - width :, :], ("tx",), (-1,))
    high_x = fetch(now[:, :width, :], ("tx",), (1,))
    widened = extend_y(packed, width)
    later = [
        widened[rows_now + (t - 1) * per_tick.shape[1] : rows_now + t * per_tick.shape[1]]
        for t in range(1, ticks)
    ]
    rims = jnp.concatenate([low_x, high_x], axis=1)
    corner_low = fetch(rims[..., ny - width :], ("ty",), (-1,))
    corner_high = fetch(rims[..., :width], ("ty",), (1,))
    rims = jnp.concatenate([corner_low, rims, corner_high], axis=-1)
    segments = []
    for ix in range(ex):
        if ix < width:
            segments.append(rims[:, ix])
        elif ix < width + nx:
            segments.append(widened[:rows_now, ix - width])
        else:
            segments.append(rims[:, ix - nx])
    segments.append(jnp.zeros((rows_now, padded - cols), jnp.float32))
    packed = jnp.concatenate(segments, axis=-1)
    first_pending = nsrc * two * depth + depth

    gx = lax.axis_index("tx") * nx - width + jnp.arange(ex)
    gy = lax.axis_index("ty") * ny - width + jnp.arange(ey)
    inside = ((gx >= 0) & (gx < nx * ntx))[:, None] & ((gy >= 0) & (gy < ny * nty))[None, :]
    inside = jnp.pad(inside.reshape(1, cols).astype(jnp.float32), ((0, 0), (0, padded - cols)))

    blocks = block_matrix(line_inverse[0])
    side_by_side = jnp.concatenate([blocks[k] for k in range(classes)], axis=1)
    rounded = lax.reduce_precision(side_by_side, exponent_bits=8, mantissa_bits=7)
    bhi = rounded.astype(jnp.bfloat16)
    blo = (side_by_side - rounded).astype(jnp.bfloat16)
    orders = batch_order[:, 0]

    incoming = packed[first_pending : first_pending + nsrc * two].reshape(nsrc, two, padded)
    low_later = [fetch(r[:, nx - width :, :], ("tx",), (-1,)) for r in later]
    high_later = [fetch(r[:, :width, :], ("tx",), (1,)) for r in later]
    solutions = []
    trace = None
    forcing_f = packed
    for tick in range(ticks):
        field = run_tick(
            orders[tick], forcing_f, packed, incoming, inside, bhi, blo, ey, depth, width, nx * ny
        )
        if tick + 1 < ticks:
            rows = later[tick]
            field, low, high = lax.optimization_barrier((field, low_later[tick], high_later[tick]))
            segments = [low[:, ix] for ix in range(width)]
            segments += [rows[:, r] for r in range(nx)]
            segments += [high[:, r] for r in range(width)]
            segments.append(jnp.zeros((rows.shape[0], padded - cols), jnp.float32))
            forcing_f = jnp.concatenate(segments, axis=-1)
        tile = field.reshape(nsrc, two, depth, nx, ny)
        solutions.append(tile)
        trace = tile[:, :, depth - 1]
        if tick + 1 < ticks:
            incoming = flat_extended(extend_y(trace, width), width, padded, ("slab",), (-1,))
    return (jnp.stack(solutions, axis=0), trace[:, :, None])


def solution(mesh):
    in_specs = (
        P(None, None, None, "slab", "tx", "ty"),
        P("slab", "tx", "ty"),
        P("slab", None, None, None, None),
        P("slab", "tx", "ty"),
        P(None, "slab", None),
        P(None, None, "slab", "tx", "ty"),
    )
    out_specs = (P(None, None, None, "slab", "tx", "ty"), P(None, None, "slab", "tx", "ty"))
    return jax.shard_map(
        per_device, mesh=mesh, in_specs=in_specs, out_specs=out_specs, check_vma=False
    )
```

```python
import functools

import jax
import jax.numpy as jnp
from jax import lax
from jax.experimental import pallas as pl
from jax.experimental.pallas import tpu as pltpu
from jax.sharding import PartitionSpec as P

CORR = 3
TICKS = 2


DAMPING = 0.25
PRECISE = lax.Precision.HIGHEST
SPLIT = 65537.0


def fetch(block, axes, offsets):
    sizes = [lax.axis_size(a) for a in axes]
    pairs = []
    total = 1
    for s in sizes:
        total *= s
    for linear in range(total):
        coords = []
        rest = linear
        for s in reversed(sizes):
            coords.append(rest % s)
            rest //= s
        coords = coords[::-1]
        source = [c + d for c, d in zip(coords, offsets)]
        if all(0 <= c < s for c, s in zip(source, sizes)):
            src_linear = 0
            for c, s in zip(source, sizes):
                src_linear = src_linear * s + c
            pairs.append((src_linear, linear))
    if len(axes) == 1:
        return lax.ppermute(block, axes[0], pairs)
    return lax.ppermute(block, tuple(axes), pairs)


def extend_y(block, width):
    ny = block.shape[-1]
    low = fetch(block[..., ny - width :], ("ty",), (-1,))
    high = fetch(block[..., :width], ("ty",), (1,))
    return jnp.concatenate([low, block, high], axis=-1)


def flat_extended(block, width, padded, lead_axes=(), lead_offsets=()):
    nx = block.shape[-2]
    pieces = {
        -1: fetch(block[..., nx - width :, :], tuple(lead_axes) + ("tx",), tuple(lead_offsets) + (-1,)),
        1: fetch(block[..., :width, :], tuple(lead_axes) + ("tx",), tuple(lead_offsets) + (1,)),
    }
    if lead_axes:
        pieces[0] = fetch(block, tuple(lead_axes) + ("tx",), tuple(lead_offsets) + (0,))
    else:
        pieces[0] = block
    segments = []
    for ix in range(nx + 2 * width):
        dx = -1 if ix < width else (0 if ix < width + nx else 1)
        r = ix - (0 if dx == -1 else (width if dx == 0 else width + nx))
        segments.append(pieces[dx][..., r, :])
    used = sum(s.shape[-1] for s in segments)
    lead = segments[0].shape[:-1]
    segments.append(jnp.zeros(lead + (padded - used,), segments[0].dtype))
    return jnp.concatenate(segments, axis=-1)


def tick_kernel(
    order_ref, frc_ref, pk_ref, inc_ref, ins_ref, bhi_ref, blo_ref, out_ref, trace_ref, field_ref, *, row, depth,
    width,
):
    nsrc, rows, owned = out_ref.shape
    cols = pk_ref.shape[1]
    classes = bhi_ref.shape[1] // rows
    lanes = 128
    wave0 = pk_ref.shape[0] - depth - 2 * nsrc - 1
    label_row = wave0 + depth + 2 * nsrc
    extent = owned // lanes + 2 * width

    def edges(lo, hi):
        zrow = lax.broadcasted_iota(jnp.int32, (rows, hi - lo), 0) % depth
        return zrow == 0, zrow == depth - 1

    def precond(x, lo, hi):
        scaled = x * SPLIT
        high = scaled - (scaled - x)
        low = x - high
        label = pk_ref[pl.ds(label_row, 1), lo:hi]
        hots = [(label == float(k)).astype(jnp.bfloat16) for k in range(classes)]
        high = high.astype(jnp.bfloat16)
        low = low.astype(jnp.bfloat16)
        high = jnp.concatenate([high * h for h in hots], axis=0)
        low = jnp.concatenate([low * h for h in hots], axis=0)
        bhi = bhi_ref[...]
        blo = blo_ref[...]
        out = jnp.dot(bhi, low, preferred_element_type=jnp.float32)
        out = out + jnp.dot(blo, high, preferred_element_type=jnp.float32)
        return out + jnp.dot(bhi, high, preferred_element_type=jnp.float32)

    def apply_a(u, lo, hi):
        span = hi - lo
        top, bottom = edges(lo, hi)
        wave = pk_ref[pl.ds(wave0, depth), lo:hi]
        dr = 6.0 - wave
        di = -DAMPING * wave
        real = u[:depth]
        imaginary = u[depth:]
        diagonal = jnp.concatenate(
            [dr * real - di * imaginary, dr * imaginary + di * real], axis=0
        )
        down = jnp.where(top, 0.0, pltpu.roll(u, 1, 0))
        up = jnp.where(bottom, 0.0, pltpu.roll(u, rows - 1, 0))
        beside = up + down
        beside = beside + pltpu.roll(u, span - row, 1) + pltpu.roll(u, row, 1)
        beside = beside + pltpu.roll(u, span - 1, 1) + pltpu.roll(u, 1, 1)
        return diagonal - beside

    def one_source(s, carry):
        first = pl.multiple_of(order_ref[s] * rows, rows)
        forcing = frc_ref[pl.ds(first, rows), :]
        incoming = inc_ref[s]
        layer = jnp.concatenate(
            [
                jnp.broadcast_to(incoming[0:1], (depth, cols)),
                jnp.broadcast_to(incoming[1:2], (depth, cols)),
            ],
            axis=0,
        )
        top, _ = edges(0, cols)
        rhs = jnp.where(top, forcing + layer, forcing)
        field_ref[...] = precond(rhs, 0, cols)
        for step in range(1, CORR + 1):
            a = (step * row) // lanes * lanes
            b = min(-(-((extent - step) * row) // lanes) * lanes, cols)
            lo = max(a - 2 * lanes, 0)
            hi = min(b + 2 * lanes, cols)
            stencil = apply_a(field_ref[:, lo:hi], lo, hi)[:, a - lo : b - lo]
            residual = ins_ref[:, a:b] * (rhs[:, a:b] - stencil)
            field_ref[:, a:b] = field_ref[:, a:b] + precond(residual, a, b)
        u = field_ref[...]
        for x in range(owned // lanes):
            begin = (x + width) * row + width
            chunk = pltpu.roll(u, cols - begin, 1)[:, :lanes]
            out_ref[s, :, x * lanes : (x + 1) * lanes] = chunk
            for part in range(rows // depth):
                bottom = (part + 1) * depth - 1
                trace_ref[s, part, pl.ds(x, 1), :] = chunk[bottom : bottom + 1, :]
        return carry

    lax.fori_loop(0, nsrc, one_source, 0)


def run_tick(order, forcing, packed, incoming, ins, bhi, blo, row, depth, width, owned):
    nsrc = incoming.shape[0]
    rows, stacked = bhi.shape
    cols = packed.shape[1]
    flops = nsrc * (CORR + 1) * 3 * 2 * rows * stacked * cols
    vmem = pl.BlockSpec(memory_space=pltpu.VMEM)
    return pl.pallas_call(
        functools.partial(tick_kernel, row=row, depth=depth, width=width),
        out_shape=(
            jax.ShapeDtypeStruct((nsrc, rows, owned), jnp.float32),
            jax.ShapeDtypeStruct((nsrc, rows // depth, owned // 128, 128), jnp.float32),
        ),
        in_specs=[pl.BlockSpec(memory_space=pltpu.SMEM)] + [vmem] * 6,
        out_specs=(vmem, vmem),
        scratch_shapes=[pltpu.VMEM((rows, cols), jnp.float32)],
        cost_estimate=pl.CostEstimate(
            flops=flops,
            transcendentals=0,
            bytes_accessed=4 * (forcing.size + packed.size // 4 + nsrc * rows * owned),
        ),
    )(order, forcing, packed, incoming, ins, bhi, blo)


def block_matrix(inverse):
    real = inverse[:, 0]
    imaginary = inverse[:, 1]
    upper = jnp.concatenate([real, -imaginary], axis=2)
    lower = jnp.concatenate([imaginary, real], axis=2)
    return jnp.concatenate([upper, lower], axis=1)


def per_device(forcing, wavenumber_sq, line_inverse, column_class, batch_order, pending_trace):
    width = CORR
    ticks, nsrc, two, depth, nx, ny = forcing.shape
    classes = line_inverse.shape[1]
    ntx = lax.axis_size("tx")
    nty = lax.axis_size("ty")
    ex, ey = nx + 2 * width, ny + 2 * width
    cols = ex * ey
    padded = -(-cols // 128) * 128
    assert width <= nx and width <= ny

    per_tick = forcing.reshape(ticks, -1, nx, ny)
    packed = jnp.concatenate(
        [
            per_tick[0],
            wavenumber_sq,
            pending_trace.reshape(-1, nx, ny),
            column_class[0][None].astype(jnp.float32),
        ]
        + [per_tick[t] for t in range(1, ticks)],
        axis=0,
    )
    rows_now = per_tick.shape[1] + depth + nsrc * two + 1
    now = packed[:rows_now]
    low_x = fetch(now[:, nx - width :, :], ("tx",), (-1,))
    high_x = fetch(now[:, :width, :], ("tx",), (1,))
    widened = extend_y(packed, width)
    later = [
        widened[rows_now + (t - 1) * per_tick.shape[1] : rows_now + t * per_tick.shape[1]]
        for t in range(1, ticks)
    ]
    rims = jnp.concatenate([low_x, high_x], axis=1)
    corner_low = fetch(rims[..., ny - width :], ("ty",), (-1,))
    corner_high = fetch(rims[..., :width], ("ty",), (1,))
    rims = jnp.concatenate([corner_low, rims, corner_high], axis=-1)
    segments = []
    for ix in range(ex):
        if ix < width:
            segments.append(rims[:, ix])
        elif ix < width + nx:
            segments.append(widened[:rows_now, ix - width])
        else:
            segments.append(rims[:, ix - nx])
    segments.append(jnp.zeros((rows_now, padded - cols), jnp.float32))
    packed = jnp.concatenate(segments, axis=-1)
    first_pending = nsrc * two * depth + depth

    gx = lax.axis_index("tx") * nx - width + jnp.arange(ex)
    gy = lax.axis_index("ty") * ny - width + jnp.arange(ey)
    inside = ((gx >= 0) & (gx < nx * ntx))[:, None] & ((gy >= 0) & (gy < ny * nty))[None, :]
    inside = jnp.pad(inside.reshape(1, cols).astype(jnp.float32), ((0, 0), (0, padded - cols)))

    blocks = block_matrix(line_inverse[0])
    side_by_side = jnp.concatenate([blocks[k] for k in range(classes)], axis=1)
    rounded = lax.reduce_precision(side_by_side, exponent_bits=8, mantissa_bits=7)
    bhi = rounded.astype(jnp.bfloat16)
    blo = (side_by_side - rounded).astype(jnp.bfloat16)
    orders = batch_order[:, 0]

    incoming = packed[first_pending : first_pending + nsrc * two].reshape(nsrc, two, padded)
    low_later = [fetch(r[:, nx - width :, :], ("tx",), (-1,)) for r in later]
    high_later = [fetch(r[:, :width, :], ("tx",), (1,)) for r in later]
    solutions = []
    trace = None
    forcing_f = packed
    for tick in range(ticks):
        field, trace = run_tick(
            orders[tick], forcing_f, packed, incoming, inside, bhi, blo, ey, depth, width, nx * ny
        )
        if tick + 1 < ticks:
            rows = later[tick]
            field, low, high = lax.optimization_barrier((field, low_later[tick], high_later[tick]))
            segments = [low[:, ix] for ix in range(width)]
            segments += [rows[:, r] for r in range(nx)]
            segments += [high[:, r] for r in range(width)]
            segments.append(jnp.zeros((rows.shape[0], padded - cols), jnp.float32))
            forcing_f = jnp.concatenate(segments, axis=-1)
        tile = field.reshape(nsrc, two, depth, nx, ny)
        solutions.append(tile)
        if tick + 1 < ticks:
            incoming = flat_extended(extend_y(trace, width), width, padded, ("slab",), (-1,))
    return (jnp.stack(solutions, axis=0), trace[:, :, None])


def solution(mesh):
    in_specs = (
        P(None, None, None, "slab", "tx", "ty"),
        P("slab", "tx", "ty"),
        P("slab", None, None, None, None),
        P("slab", "tx", "ty"),
        P(None, "slab", None),
        P(None, None, "slab", "tx", "ty"),
    )
    out_specs = (P(None, None, None, "slab", "tx", "ty"), P(None, None, "slab", "tx", "ty"))
    return jax.shard_map(
        per_device, mesh=mesh, in_specs=in_specs, out_specs=out_specs, check_vma=False
    )
```

```python
import functools

import jax
import jax.numpy as jnp
from jax import lax
from jax.experimental import pallas as pl
from jax.experimental.pallas import tpu as pltpu
from jax.sharding import PartitionSpec as P

CORR = 3
TICKS = 2


DAMPING = 0.25
PRECISE = lax.Precision.HIGHEST
SPLIT = 65537.0


def fetch(block, axes, offsets):
    sizes = [lax.axis_size(a) for a in axes]
    pairs = []
    total = 1
    for s in sizes:
        total *= s
    for linear in range(total):
        coords = []
        rest = linear
        for s in reversed(sizes):
            coords.append(rest % s)
            rest //= s
        coords = coords[::-1]
        source = [c + d for c, d in zip(coords, offsets)]
        if all(0 <= c < s for c, s in zip(source, sizes)):
            src_linear = 0
            for c, s in zip(source, sizes):
                src_linear = src_linear * s + c
            pairs.append((src_linear, linear))
    if len(axes) == 1:
        return lax.ppermute(block, axes[0], pairs)
    return lax.ppermute(block, tuple(axes), pairs)


def extend_y(block, width):
    ny = block.shape[-1]
    low = fetch(block[..., ny - width :], ("ty",), (-1,))
    high = fetch(block[..., :width], ("ty",), (1,))
    return jnp.concatenate([low, block, high], axis=-1)


def flat_extended(block, width, padded, lead_axes=(), lead_offsets=()):
    nx = block.shape[-2]
    pieces = {
        -1: fetch(block[..., nx - width :, :], tuple(lead_axes) + ("tx",), tuple(lead_offsets) + (-1,)),
        1: fetch(block[..., :width, :], tuple(lead_axes) + ("tx",), tuple(lead_offsets) + (1,)),
    }
    if lead_axes:
        pieces[0] = fetch(block, tuple(lead_axes) + ("tx",), tuple(lead_offsets) + (0,))
    else:
        pieces[0] = block
    segments = []
    for ix in range(nx + 2 * width):
        dx = -1 if ix < width else (0 if ix < width + nx else 1)
        r = ix - (0 if dx == -1 else (width if dx == 0 else width + nx))
        segments.append(pieces[dx][..., r, :])
    used = sum(s.shape[-1] for s in segments)
    lead = segments[0].shape[:-1]
    segments.append(jnp.zeros(lead + (padded - used,), segments[0].dtype))
    return jnp.concatenate(segments, axis=-1)


def tick_kernel(
    order_ref, frc_ref, pk_ref, inc_ref, ins_ref, bhi_ref, blo_ref, out_ref, trace_ref, field_ref, *, row, depth,
    width,
):
    nsrc, rows, owned = trace_ref.shape[0], bhi_ref.shape[0], trace_ref.shape[2] * 128
    cols = pk_ref.shape[1]
    classes = bhi_ref.shape[1] // rows
    lanes = 128
    wave0 = pk_ref.shape[0] - depth - 2 * nsrc - 1
    label_row = wave0 + depth + 2 * nsrc
    extent = owned // lanes + 2 * width

    def edges(lo, hi):
        zrow = lax.broadcasted_iota(jnp.int32, (rows, hi - lo), 0) % depth
        return zrow == 0, zrow == depth - 1

    def precond(x, lo, hi):
        scaled = x * SPLIT
        high = scaled - (scaled - x)
        low = x - high
        label = pk_ref[pl.ds(label_row, 1), lo:hi]
        hots = [(label == float(k)).astype(jnp.bfloat16) for k in range(classes)]
        high = high.astype(jnp.bfloat16)
        low = low.astype(jnp.bfloat16)
        high = jnp.concatenate([high * h for h in hots], axis=0)
        low = jnp.concatenate([low * h for h in hots], axis=0)
        bhi = bhi_ref[...]
        blo = blo_ref[...]
        out = jnp.dot(bhi, low, preferred_element_type=jnp.float32)
        out = out + jnp.dot(blo, high, preferred_element_type=jnp.float32)
        return out + jnp.dot(bhi, high, preferred_element_type=jnp.float32)

    def apply_a(u, lo, hi):
        span = hi - lo
        top, bottom = edges(lo, hi)
        wave = pk_ref[pl.ds(wave0, depth), lo:hi]
        dr = 6.0 - wave
        di = -DAMPING * wave
        real = u[:depth]
        imaginary = u[depth:]
        diagonal = jnp.concatenate(
            [dr * real - di * imaginary, dr * imaginary + di * real], axis=0
        )
        down = jnp.where(top, 0.0, pltpu.roll(u, 1, 0))
        up = jnp.where(bottom, 0.0, pltpu.roll(u, rows - 1, 0))
        beside = up + down
        beside = beside + pltpu.roll(u, span - row, 1) + pltpu.roll(u, row, 1)
        beside = beside + pltpu.roll(u, span - 1, 1) + pltpu.roll(u, 1, 1)
        return diagonal - beside

    def one_source(s, carry):
        first = pl.multiple_of(order_ref[s] * rows, rows)
        forcing = frc_ref[pl.ds(first, rows), :]
        incoming = inc_ref[s]
        layer = jnp.concatenate(
            [
                jnp.broadcast_to(incoming[0:1], (depth, cols)),
                jnp.broadcast_to(incoming[1:2], (depth, cols)),
            ],
            axis=0,
        )
        top, _ = edges(0, cols)
        rhs = jnp.where(top, forcing + layer, forcing)
        field_ref[...] = precond(rhs, 0, cols)
        for step in range(1, CORR + 1):
            a = (step * row) // lanes * lanes
            b = min(-(-((extent - step) * row) // lanes) * lanes, cols)
            lo = max(a - 2 * lanes, 0)
            hi = min(b + 2 * lanes, cols)
            stencil = apply_a(field_ref[:, lo:hi], lo, hi)[:, a - lo : b - lo]
            residual = ins_ref[:, a:b] * (rhs[:, a:b] - stencil)
            field_ref[:, a:b] = field_ref[:, a:b] + precond(residual, a, b)
        u = field_ref[...]
        for x in range(owned // lanes):
            begin = (x + width) * row + width
            chunk = pltpu.roll(u, cols - begin, 1)[:, :lanes]
            for part in range(rows // depth):
                out_ref[s, part, :, x, :] = chunk[part * depth : (part + 1) * depth, :]
            for part in range(rows // depth):
                bottom = (part + 1) * depth - 1
                trace_ref[s, part, pl.ds(x, 1), :] = chunk[bottom : bottom + 1, :]
        return carry

    lax.fori_loop(0, nsrc, one_source, 0)


def run_tick(order, forcing, packed, incoming, ins, bhi, blo, row, depth, width, owned):
    nsrc = incoming.shape[0]
    rows, stacked = bhi.shape
    cols = packed.shape[1]
    flops = nsrc * (CORR + 1) * 3 * 2 * rows * stacked * cols
    vmem = pl.BlockSpec(memory_space=pltpu.VMEM)
    return pl.pallas_call(
        functools.partial(tick_kernel, row=row, depth=depth, width=width),
        out_shape=(
            jax.ShapeDtypeStruct((nsrc, rows // depth, depth, owned // 128, 128), jnp.float32),
            jax.ShapeDtypeStruct((nsrc, rows // depth, owned // 128, 128), jnp.float32),
        ),
        in_specs=[pl.BlockSpec(memory_space=pltpu.SMEM)] + [vmem] * 6,
        out_specs=(vmem, vmem),
        scratch_shapes=[pltpu.VMEM((rows, cols), jnp.float32)],
        cost_estimate=pl.CostEstimate(
            flops=flops,
            transcendentals=0,
            bytes_accessed=4 * (forcing.size + packed.size // 4 + nsrc * rows * owned),
        ),
    )(order, forcing, packed, incoming, ins, bhi, blo)


def block_matrix(inverse):
    real = inverse[:, 0]
    imaginary = inverse[:, 1]
    upper = jnp.concatenate([real, -imaginary], axis=2)
    lower = jnp.concatenate([imaginary, real], axis=2)
    return jnp.concatenate([upper, lower], axis=1)


def per_device(forcing, wavenumber_sq, line_inverse, column_class, batch_order, pending_trace):
    width = CORR
    ticks, nsrc, two, depth, nx, ny = forcing.shape
    classes = line_inverse.shape[1]
    ntx = lax.axis_size("tx")
    nty = lax.axis_size("ty")
    ex, ey = nx + 2 * width, ny + 2 * width
    cols = ex * ey
    padded = -(-cols // 128) * 128
    assert width <= nx and width <= ny

    per_tick = forcing.reshape(ticks, -1, nx, ny)
    packed = jnp.concatenate(
        [
            per_tick[0],
            wavenumber_sq,
            pending_trace.reshape(-1, nx, ny),
            column_class[0][None].astype(jnp.float32),
        ]
        + [per_tick[t] for t in range(1, ticks)],
        axis=0,
    )
    rows_now = per_tick.shape[1] + depth + nsrc * two + 1
    now = packed[:rows_now]
    low_x = fetch(now[:, nx - width :, :], ("tx",), (-1,))
    high_x = fetch(now[:, :width, :], ("tx",), (1,))
    widened = extend_y(packed, width)
    later = [
        widened[rows_now + (t - 1) * per_tick.shape[1] : rows_now + t * per_tick.shape[1]]
        for t in range(1, ticks)
    ]
    rims = jnp.concatenate([low_x, high_x], axis=1)
    corner_low = fetch(rims[..., ny - width :], ("ty",), (-1,))
    corner_high = fetch(rims[..., :width], ("ty",), (1,))
    rims = jnp.concatenate([corner_low, rims, corner_high], axis=-1)
    segments = []
    for ix in range(ex):
        if ix < width:
            segments.append(rims[:, ix])
        elif ix < width + nx:
            segments.append(widened[:rows_now, ix - width])
        else:
            segments.append(rims[:, ix - nx])
    segments.append(jnp.zeros((rows_now, padded - cols), jnp.float32))
    packed = jnp.concatenate(segments, axis=-1)
    first_pending = nsrc * two * depth + depth

    gx = lax.axis_index("tx") * nx - width + jnp.arange(ex)
    gy = lax.axis_index("ty") * ny - width + jnp.arange(ey)
    inside = ((gx >= 0) & (gx < nx * ntx))[:, None] & ((gy >= 0) & (gy < ny * nty))[None, :]
    inside = jnp.pad(inside.reshape(1, cols).astype(jnp.float32), ((0, 0), (0, padded - cols)))

    blocks = block_matrix(line_inverse[0])
    side_by_side = jnp.concatenate([blocks[k] for k in range(classes)], axis=1)
    rounded = lax.reduce_precision(side_by_side, exponent_bits=8, mantissa_bits=7)
    bhi = rounded.astype(jnp.bfloat16)
    blo = (side_by_side - rounded).astype(jnp.bfloat16)
    orders = batch_order[:, 0]

    incoming = packed[first_pending : first_pending + nsrc * two].reshape(nsrc, two, padded)
    low_later = [fetch(r[:, nx - width :, :], ("tx",), (-1,)) for r in later]
    high_later = [fetch(r[:, :width, :], ("tx",), (1,)) for r in later]
    solutions = []
    trace = None
    forcing_f = packed
    for tick in range(ticks):
        field, trace = run_tick(
            orders[tick], forcing_f, packed, incoming, inside, bhi, blo, ey, depth, width, nx * ny
        )
        if tick + 1 < ticks:
            rows = later[tick]
            field, low, high = lax.optimization_barrier((field, low_later[tick], high_later[tick]))
            segments = [low[:, ix] for ix in range(width)]
            segments += [rows[:, r] for r in range(nx)]
            segments += [high[:, r] for r in range(width)]
            segments.append(jnp.zeros((rows.shape[0], padded - cols), jnp.float32))
            forcing_f = jnp.concatenate(segments, axis=-1)
        tile = field
        solutions.append(tile)
        if tick + 1 < ticks:
            incoming = flat_extended(extend_y(trace, width), width, padded, ("slab",), (-1,))
    return (jnp.stack(solutions, axis=0), trace[:, :, None])


def solution(mesh):
    in_specs = (
        P(None, None, None, "slab", "tx", "ty"),
        P("slab", "tx", "ty"),
        P("slab", None, None, None, None),
        P("slab", "tx", "ty"),
        P(None, "slab", None),
        P(None, None, "slab", "tx", "ty"),
    )
    out_specs = (P(None, None, None, "slab", "tx", "ty"), P(None, None, "slab", "tx", "ty"))
    return jax.shard_map(
        per_device, mesh=mesh, in_specs=in_specs, out_specs=out_specs, check_vma=False
    )
```

```python
import functools

import jax
import jax.numpy as jnp
from jax import lax
from jax.experimental import pallas as pl
from jax.experimental.pallas import tpu as pltpu
from jax.sharding import PartitionSpec as P

CORR = 3
TICKS = 2


DAMPING = 0.25
PRECISE = lax.Precision.HIGHEST
SPLIT = 65537.0


def fetch(block, axes, offsets):
    sizes = [lax.axis_size(a) for a in axes]
    pairs = []
    total = 1
    for s in sizes:
        total *= s
    for linear in range(total):
        coords = []
        rest = linear
        for s in reversed(sizes):
            coords.append(rest % s)
            rest //= s
        coords = coords[::-1]
        source = [c + d for c, d in zip(coords, offsets)]
        if all(0 <= c < s for c, s in zip(source, sizes)):
            src_linear = 0
            for c, s in zip(source, sizes):
                src_linear = src_linear * s + c
            pairs.append((src_linear, linear))
    if len(axes) == 1:
        return lax.ppermute(block, axes[0], pairs)
    return lax.ppermute(block, tuple(axes), pairs)


def extend_y(block, width):
    ny = block.shape[-1]
    low = fetch(block[..., ny - width :], ("ty",), (-1,))
    high = fetch(block[..., :width], ("ty",), (1,))
    return jnp.concatenate([low, block, high], axis=-1)


def flat_extended(block, width, padded, lead_axes=(), lead_offsets=()):
    nx = block.shape[-2]
    pieces = {
        -1: fetch(block[..., nx - width :, :], tuple(lead_axes) + ("tx",), tuple(lead_offsets) + (-1,)),
        1: fetch(block[..., :width, :], tuple(lead_axes) + ("tx",), tuple(lead_offsets) + (1,)),
    }
    if lead_axes:
        pieces[0] = fetch(block, tuple(lead_axes) + ("tx",), tuple(lead_offsets) + (0,))
    else:
        pieces[0] = block
    segments = []
    for ix in range(nx + 2 * width):
        dx = -1 if ix < width else (0 if ix < width + nx else 1)
        r = ix - (0 if dx == -1 else (width if dx == 0 else width + nx))
        segments.append(pieces[dx][..., r, :])
    used = sum(s.shape[-1] for s in segments)
    lead = segments[0].shape[:-1]
    segments.append(jnp.zeros(lead + (padded - used,), segments[0].dtype))
    return jnp.concatenate(segments, axis=-1)


def tick_kernel(
    order_ref, frc_ref, pk_ref, inc_ref, ins_ref, bhi_ref, blo_ref, *rest, row, depth, width, tick
):
    out_ref, trace_ref, field_ref = rest[-3:]
    if tick:
        out_ref[:tick] = rest[0][...]
    nsrc, rows, owned = trace_ref.shape[0], bhi_ref.shape[0], trace_ref.shape[2] * 128
    cols = pk_ref.shape[1]
    classes = bhi_ref.shape[1] // rows
    lanes = 128
    wave0 = pk_ref.shape[0] - depth - 2 * nsrc - 1
    label_row = wave0 + depth + 2 * nsrc
    extent = owned // lanes + 2 * width

    def edges(lo, hi):
        zrow = lax.broadcasted_iota(jnp.int32, (rows, hi - lo), 0) % depth
        return zrow == 0, zrow == depth - 1

    def precond(x, lo, hi):
        scaled = x * SPLIT
        high = scaled - (scaled - x)
        low = x - high
        label = pk_ref[pl.ds(label_row, 1), lo:hi]
        hots = [(label == float(k)).astype(jnp.bfloat16) for k in range(classes)]
        high = high.astype(jnp.bfloat16)
        low = low.astype(jnp.bfloat16)
        high = jnp.concatenate([high * h for h in hots], axis=0)
        low = jnp.concatenate([low * h for h in hots], axis=0)
        bhi = bhi_ref[...]
        blo = blo_ref[...]
        out = jnp.dot(bhi, low, preferred_element_type=jnp.float32)
        out = out + jnp.dot(blo, high, preferred_element_type=jnp.float32)
        return out + jnp.dot(bhi, high, preferred_element_type=jnp.float32)

    def apply_a(u, lo, hi):
        span = hi - lo
        top, bottom = edges(lo, hi)
        wave = pk_ref[pl.ds(wave0, depth), lo:hi]
        dr = 6.0 - wave
        di = -DAMPING * wave
        real = u[:depth]
        imaginary = u[depth:]
        diagonal = jnp.concatenate(
            [dr * real - di * imaginary, dr * imaginary + di * real], axis=0
        )
        down = jnp.where(top, 0.0, pltpu.roll(u, 1, 0))
        up = jnp.where(bottom, 0.0, pltpu.roll(u, rows - 1, 0))
        beside = up + down
        beside = beside + pltpu.roll(u, span - row, 1) + pltpu.roll(u, row, 1)
        beside = beside + pltpu.roll(u, span - 1, 1) + pltpu.roll(u, 1, 1)
        return diagonal - beside

    def one_source(s, carry):
        first = pl.multiple_of(order_ref[s] * rows, rows)
        forcing = frc_ref[pl.ds(first, rows), :]
        incoming = inc_ref[s]
        layer = jnp.concatenate(
            [
                jnp.broadcast_to(incoming[0:1], (depth, cols)),
                jnp.broadcast_to(incoming[1:2], (depth, cols)),
            ],
            axis=0,
        )
        top, _ = edges(0, cols)
        rhs = jnp.where(top, forcing + layer, forcing)
        field_ref[...] = precond(rhs, 0, cols)
        for step in range(1, CORR + 1):
            a = (step * row) // lanes * lanes
            b = min(-(-((extent - step) * row) // lanes) * lanes, cols)
            lo = max(a - 2 * lanes, 0)
            hi = min(b + 2 * lanes, cols)
            stencil = apply_a(field_ref[:, lo:hi], lo, hi)[:, a - lo : b - lo]
            residual = ins_ref[:, a:b] * (rhs[:, a:b] - stencil)
            field_ref[:, a:b] = field_ref[:, a:b] + precond(residual, a, b)
        u = field_ref[...]
        for x in range(owned // lanes):
            begin = (x + width) * row + width
            chunk = pltpu.roll(u, cols - begin, 1)[:, :lanes]
            for part in range(rows // depth):
                out_ref[tick, s, part, :, x, :] = chunk[part * depth : (part + 1) * depth, :]
            for part in range(rows // depth):
                bottom = (part + 1) * depth - 1
                trace_ref[s, part, pl.ds(x, 1), :] = chunk[bottom : bottom + 1, :]
        return carry

    lax.fori_loop(0, nsrc, one_source, 0)


def run_tick(order, forcing, packed, incoming, ins, bhi, blo, row, depth, width, owned, tick, done):
    nsrc = incoming.shape[0]
    rows, stacked = bhi.shape
    cols = packed.shape[1]
    flops = nsrc * (CORR + 1) * 3 * 2 * rows * stacked * cols
    vmem = pl.BlockSpec(memory_space=pltpu.VMEM)
    return pl.pallas_call(
        functools.partial(tick_kernel, row=row, depth=depth, width=width, tick=tick),
        out_shape=(
            jax.ShapeDtypeStruct((tick + 1, nsrc, rows // depth, depth, owned // 128, 128), jnp.float32),
            jax.ShapeDtypeStruct((nsrc, rows // depth, owned // 128, 128), jnp.float32),
        ),
        in_specs=[pl.BlockSpec(memory_space=pltpu.SMEM)] + [vmem] * (6 + (tick > 0)),
        out_specs=(vmem, vmem),
        scratch_shapes=[pltpu.VMEM((rows, cols), jnp.float32)],
        cost_estimate=pl.CostEstimate(
            flops=flops,
            transcendentals=0,
            bytes_accessed=4 * (forcing.size + packed.size // 4 + nsrc * rows * owned),
        ),
    )(*([order, forcing, packed, incoming, ins, bhi, blo] + ([done] if tick else [])))


def block_matrix(inverse):
    real = inverse[:, 0]
    imaginary = inverse[:, 1]
    upper = jnp.concatenate([real, -imaginary], axis=2)
    lower = jnp.concatenate([imaginary, real], axis=2)
    return jnp.concatenate([upper, lower], axis=1)


def per_device(forcing, wavenumber_sq, line_inverse, column_class, batch_order, pending_trace):
    width = CORR
    ticks, nsrc, two, depth, nx, ny = forcing.shape
    classes = line_inverse.shape[1]
    ntx = lax.axis_size("tx")
    nty = lax.axis_size("ty")
    ex, ey = nx + 2 * width, ny + 2 * width
    cols = ex * ey
    padded = -(-cols // 128) * 128
    assert width <= nx and width <= ny

    per_tick = forcing.reshape(ticks, -1, nx, ny)
    packed = jnp.concatenate(
        [
            per_tick[0],
            wavenumber_sq,
            pending_trace.reshape(-1, nx, ny),
            column_class[0][None].astype(jnp.float32),
        ]
        + [per_tick[t] for t in range(1, ticks)],
        axis=0,
    )
    rows_now = per_tick.shape[1] + depth + nsrc * two + 1
    now = packed[:rows_now]
    low_x = fetch(now[:, nx - width :, :], ("tx",), (-1,))
    high_x = fetch(now[:, :width, :], ("tx",), (1,))
    widened = extend_y(packed, width)
    later = [
        widened[rows_now + (t - 1) * per_tick.shape[1] : rows_now + t * per_tick.shape[1]]
        for t in range(1, ticks)
    ]
    rims = jnp.concatenate([low_x, high_x], axis=1)
    corner_low = fetch(rims[..., ny - width :], ("ty",), (-1,))
    corner_high = fetch(rims[..., :width], ("ty",), (1,))
    rims = jnp.concatenate([corner_low, rims, corner_high], axis=-1)
    segments = []
    for ix in range(ex):
        if ix < width:
            segments.append(rims[:, ix])
        elif ix < width + nx:
            segments.append(widened[:rows_now, ix - width])
        else:
            segments.append(rims[:, ix - nx])
    segments.append(jnp.zeros((rows_now, padded - cols), jnp.float32))
    packed = jnp.concatenate(segments, axis=-1)
    first_pending = nsrc * two * depth + depth

    gx = lax.axis_index("tx") * nx - width + jnp.arange(ex)
    gy = lax.axis_index("ty") * ny - width + jnp.arange(ey)
    inside = ((gx >= 0) & (gx < nx * ntx))[:, None] & ((gy >= 0) & (gy < ny * nty))[None, :]
    inside = jnp.pad(inside.reshape(1, cols).astype(jnp.float32), ((0, 0), (0, padded - cols)))

    blocks = block_matrix(line_inverse[0])
    side_by_side = jnp.concatenate([blocks[k] for k in range(classes)], axis=1)
    rounded = lax.reduce_precision(side_by_side, exponent_bits=8, mantissa_bits=7)
    bhi = rounded.astype(jnp.bfloat16)
    blo = (side_by_side - rounded).astype(jnp.bfloat16)
    orders = batch_order[:, 0]

    incoming = packed[first_pending : first_pending + nsrc * two].reshape(nsrc, two, padded)
    low_later = [fetch(r[:, nx - width :, :], ("tx",), (-1,)) for r in later]
    high_later = [fetch(r[:, :width, :], ("tx",), (1,)) for r in later]
    trace = None
    field = None
    forcing_f = packed
    for tick in range(ticks):
        field, trace = run_tick(
            orders[tick], forcing_f, packed, incoming, inside, bhi, blo, ey, depth, width, nx * ny,
            tick, field,
        )
        if tick + 1 < ticks:
            rows = later[tick]
            field, low, high = lax.optimization_barrier((field, low_later[tick], high_later[tick]))
            segments = [low[:, ix] for ix in range(width)]
            segments += [rows[:, r] for r in range(nx)]
            segments += [high[:, r] for r in range(width)]
            segments.append(jnp.zeros((rows.shape[0], padded - cols), jnp.float32))
            forcing_f = jnp.concatenate(segments, axis=-1)
        if tick + 1 < ticks:
            incoming = flat_extended(extend_y(trace, width), width, padded, ("slab",), (-1,))
    return (field, trace[:, :, None])


def solution(mesh):
    in_specs = (
        P(None, None, None, "slab", "tx", "ty"),
        P("slab", "tx", "ty"),
        P("slab", None, None, None, None),
        P("slab", "tx", "ty"),
        P(None, "slab", None),
        P(None, None, "slab", "tx", "ty"),
    )
    out_specs = (P(None, None, None, "slab", "tx", "ty"), P(None, None, "slab", "tx", "ty"))
    return jax.shard_map(
        per_device, mesh=mesh, in_specs=in_specs, out_specs=out_specs, check_vma=False
    )
```

```python
import functools

import jax
import jax.numpy as jnp
from jax import lax
from jax.experimental import pallas as pl
from jax.experimental.pallas import tpu as pltpu
from jax.sharding import PartitionSpec as P

CORR = 3
TICKS = 2


DAMPING = 0.25
PRECISE = lax.Precision.HIGHEST
SPLIT = 65537.0


def fetch(block, axes, offsets):
    sizes = [lax.axis_size(a) for a in axes]
    pairs = []
    total = 1
    for s in sizes:
        total *= s
    for linear in range(total):
        coords = []
        rest = linear
        for s in reversed(sizes):
            coords.append(rest % s)
            rest //= s
        coords = coords[::-1]
        source = [c + d for c, d in zip(coords, offsets)]
        if all(0 <= c < s for c, s in zip(source, sizes)):
            src_linear = 0
            for c, s in zip(source, sizes):
                src_linear = src_linear * s + c
            pairs.append((src_linear, linear))
    if len(axes) == 1:
        return lax.ppermute(block, axes[0], pairs)
    return lax.ppermute(block, tuple(axes), pairs)


def extend_y(block, width):
    ny = block.shape[-1]
    low = fetch(block[..., ny - width :], ("ty",), (-1,))
    high = fetch(block[..., :width], ("ty",), (1,))
    return jnp.concatenate([low, block, high], axis=-1)


def flat_extended(block, width, padded, lead_axes=(), lead_offsets=()):
    nx = block.shape[-2]
    pieces = {
        -1: fetch(block[..., nx - width :, :], tuple(lead_axes) + ("tx",), tuple(lead_offsets) + (-1,)),
        1: fetch(block[..., :width, :], tuple(lead_axes) + ("tx",), tuple(lead_offsets) + (1,)),
    }
    if lead_axes:
        pieces[0] = fetch(block, tuple(lead_axes) + ("tx",), tuple(lead_offsets) + (0,))
    else:
        pieces[0] = block
    segments = []
    for ix in range(nx + 2 * width):
        dx = -1 if ix < width else (0 if ix < width + nx else 1)
        r = ix - (0 if dx == -1 else (width if dx == 0 else width + nx))
        segments.append(pieces[dx][..., r, :])
    used = sum(s.shape[-1] for s in segments)
    lead = segments[0].shape[:-1]
    segments.append(jnp.zeros(lead + (padded - used,), segments[0].dtype))
    return jnp.concatenate(segments, axis=-1)


def tick_kernel(
    order_ref, frc_ref, pk_ref, inc_ref, ins_ref, bhi_ref, blo_ref, *rest, row, depth, width, tick
):
    out_ref, trace_ref, field_ref = rest[-3:]
    if tick:
        out_ref[:tick] = rest[0][...]
    nsrc, rows, owned = trace_ref.shape[0], bhi_ref.shape[0], trace_ref.shape[2] * 128
    cols = pk_ref.shape[1]
    classes = bhi_ref.shape[1] // rows
    lanes = 128
    wave0 = pk_ref.shape[0] - depth - 2 * nsrc - 1
    label_row = wave0 + depth + 2 * nsrc
    extent = owned // lanes + 2 * width

    def edges(lo, hi):
        zrow = lax.broadcasted_iota(jnp.int32, (rows, hi - lo), 0) % depth
        return zrow == 0, zrow == depth - 1

    def precond(x, lo, hi):
        scaled = x * SPLIT
        high = scaled - (scaled - x)
        low = x - high
        label = pk_ref[pl.ds(label_row, 1), lo:hi]
        hots = [(label == float(k)).astype(jnp.bfloat16) for k in range(classes)]
        high = high.astype(jnp.bfloat16)
        low = low.astype(jnp.bfloat16)
        high = jnp.concatenate([high * h for h in hots], axis=0)
        low = jnp.concatenate([low * h for h in hots], axis=0)
        bhi = bhi_ref[...]
        blo = blo_ref[...]
        out = jnp.dot(bhi, low, preferred_element_type=jnp.float32)
        out = out + jnp.dot(blo, high, preferred_element_type=jnp.float32)
        return out + jnp.dot(bhi, high, preferred_element_type=jnp.float32)

    def apply_a(u, lo, hi):
        span = hi - lo
        top, bottom = edges(lo, hi)
        wave = pk_ref[pl.ds(wave0, depth), lo:hi]
        dr = 6.0 - wave
        di = -DAMPING * wave
        real = u[:depth]
        imaginary = u[depth:]
        diagonal = jnp.concatenate(
            [dr * real - di * imaginary, dr * imaginary + di * real], axis=0
        )
        down = jnp.where(top, 0.0, pltpu.roll(u, 1, 0))
        up = jnp.where(bottom, 0.0, pltpu.roll(u, rows - 1, 0))
        beside = up + down
        beside = beside + pltpu.roll(u, span - row, 1) + pltpu.roll(u, row, 1)
        beside = beside + pltpu.roll(u, span - 1, 1) + pltpu.roll(u, 1, 1)
        return diagonal - beside

    def one_source(s, carry):
        first = pl.multiple_of(order_ref[s] * rows, rows)
        forcing = frc_ref[pl.ds(first, rows), :]
        incoming = inc_ref[s]
        layer = jnp.concatenate(
            [
                jnp.broadcast_to(incoming[0:1], (depth, cols)),
                jnp.broadcast_to(incoming[1:2], (depth, cols)),
            ],
            axis=0,
        )
        top, _ = edges(0, cols)
        rhs = jnp.where(top, forcing + layer, forcing)
        field_ref[...] = precond(rhs, 0, cols)
        for step in range(1, CORR + 1):
            a = (step * row) // lanes * lanes
            b = min(-(-((extent - step) * row) // lanes) * lanes, cols)
            lo = max(a - 2 * lanes, 0)
            hi = min(b + 2 * lanes, cols)
            stencil = apply_a(field_ref[:, lo:hi], lo, hi)[:, a - lo : b - lo]
            residual = ins_ref[:, a:b] * (rhs[:, a:b] - stencil)
            field_ref[:, a:b] = field_ref[:, a:b] + precond(residual, a, b)
        u = field_ref[...]
        for x in range(owned // lanes):
            begin = (x + width) * row + width
            chunk = pltpu.roll(u, cols - begin, 1)[:, :lanes]
            for part in range(rows // depth):
                out_ref[tick, s, part, :, x, :] = chunk[part * depth : (part + 1) * depth, :]
            for part in range(rows // depth):
                bottom = (part + 1) * depth - 1
                trace_ref[s, part, pl.ds(x, 1), :] = chunk[bottom : bottom + 1, :]
        return carry

    lax.fori_loop(0, nsrc, one_source, 0)


def run_tick(order, forcing, packed, incoming, ins, bhi, blo, row, depth, width, owned, tick, done):
    nsrc = incoming.shape[0]
    rows, stacked = bhi.shape
    cols = packed.shape[1]
    flops = nsrc * (CORR + 1) * 3 * 2 * rows * stacked * cols
    vmem = pl.BlockSpec(memory_space=pltpu.VMEM)
    return pl.pallas_call(
        functools.partial(tick_kernel, row=row, depth=depth, width=width, tick=tick),
        out_shape=(
            jax.ShapeDtypeStruct((tick + 1, nsrc, rows // depth, depth, owned // 128, 128), jnp.float32),
            jax.ShapeDtypeStruct((nsrc, rows // depth, owned // 128, 128), jnp.float32),
        ),
        in_specs=[pl.BlockSpec(memory_space=pltpu.SMEM)] + [vmem] * (6 + (tick > 0)),
        out_specs=(vmem, vmem),
        scratch_shapes=[pltpu.VMEM((rows, cols), jnp.float32)],
        cost_estimate=pl.CostEstimate(
            flops=flops,
            transcendentals=0,
            bytes_accessed=4 * (forcing.size + packed.size // 4 + nsrc * rows * owned),
        ),
    )(*([order, forcing, packed, incoming, ins, bhi, blo] + ([done] if tick else [])))


def block_matrix(inverse):
    real = inverse[:, 0]
    imaginary = inverse[:, 1]
    upper = jnp.concatenate([real, -imaginary], axis=2)
    lower = jnp.concatenate([imaginary, real], axis=2)
    return jnp.concatenate([upper, lower], axis=1)


def per_device(forcing, wavenumber_sq, line_inverse, column_class, batch_order, pending_trace):
    width = CORR
    ticks, nsrc, two, depth, nx, ny = forcing.shape
    classes = line_inverse.shape[1]
    ntx = lax.axis_size("tx")
    nty = lax.axis_size("ty")
    ex, ey = nx + 2 * width, ny + 2 * width
    cols = ex * ey
    padded = -(-cols // 128) * 128
    assert width <= nx and width <= ny

    per_tick = forcing.reshape(ticks, -1, nx, ny)
    packed = jnp.concatenate(
        [
            per_tick[0],
            wavenumber_sq,
            pending_trace.reshape(-1, nx, ny),
            column_class[0][None].astype(jnp.float32),
        ]
        + [per_tick[t] for t in range(1, ticks)],
        axis=0,
    )
    rows_now = per_tick.shape[1] + depth + nsrc * two + 1
    now = packed[:rows_now]
    sources = [
        per_tick[0],
        wavenumber_sq,
        pending_trace.reshape(-1, nx, ny),
        column_class[0][None].astype(jnp.float32),
    ]
    low_x = fetch(jnp.concatenate([p[:, nx - width :, :] for p in sources], axis=0), ("tx",), (-1,))
    high_x = fetch(jnp.concatenate([p[:, :width, :] for p in sources], axis=0), ("tx",), (1,))
    widened = extend_y(packed, width)
    later = [
        widened[rows_now + (t - 1) * per_tick.shape[1] : rows_now + t * per_tick.shape[1]]
        for t in range(1, ticks)
    ]
    rims = jnp.concatenate([low_x, high_x], axis=1)
    corner_low = fetch(rims[..., ny - width :], ("ty",), (-1,))
    corner_high = fetch(rims[..., :width], ("ty",), (1,))
    rims = jnp.concatenate([corner_low, rims, corner_high], axis=-1)
    segments = []
    for ix in range(ex):
        if ix < width:
            segments.append(rims[:, ix])
        elif ix < width + nx:
            segments.append(widened[:rows_now, ix - width])
        else:
            segments.append(rims[:, ix - nx])
    segments.append(jnp.zeros((rows_now, padded - cols), jnp.float32))
    packed = jnp.concatenate(segments, axis=-1)
    first_pending = nsrc * two * depth + depth

    gx = lax.axis_index("tx") * nx - width + jnp.arange(ex)
    gy = lax.axis_index("ty") * ny - width + jnp.arange(ey)
    inside = ((gx >= 0) & (gx < nx * ntx))[:, None] & ((gy >= 0) & (gy < ny * nty))[None, :]
    inside = jnp.pad(inside.reshape(1, cols).astype(jnp.float32), ((0, 0), (0, padded - cols)))

    blocks = block_matrix(line_inverse[0])
    side_by_side = jnp.concatenate([blocks[k] for k in range(classes)], axis=1)
    rounded = lax.reduce_precision(side_by_side, exponent_bits=8, mantissa_bits=7)
    bhi = rounded.astype(jnp.bfloat16)
    blo = (side_by_side - rounded).astype(jnp.bfloat16)
    orders = batch_order[:, 0]

    incoming = packed[first_pending : first_pending + nsrc * two].reshape(nsrc, two, padded)
    low_later = [fetch(r[:, nx - width :, :], ("tx",), (-1,)) for r in later]
    high_later = [fetch(r[:, :width, :], ("tx",), (1,)) for r in later]
    trace = None
    field = None
    forcing_f = packed
    for tick in range(ticks):
        field, trace = run_tick(
            orders[tick], forcing_f, packed, incoming, inside, bhi, blo, ey, depth, width, nx * ny,
            tick, field,
        )
        if tick + 1 < ticks:
            rows = later[tick]
            field, low, high = lax.optimization_barrier((field, low_later[tick], high_later[tick]))
            segments = [low[:, ix] for ix in range(width)]
            segments += [rows[:, r] for r in range(nx)]
            segments += [high[:, r] for r in range(width)]
            segments.append(jnp.zeros((rows.shape[0], padded - cols), jnp.float32))
            forcing_f = jnp.concatenate(segments, axis=-1)
        if tick + 1 < ticks:
            incoming = flat_extended(extend_y(trace, width), width, padded, ("slab",), (-1,))
    return (field, trace[:, :, None])


def solution(mesh):
    in_specs = (
        P(None, None, None, "slab", "tx", "ty"),
        P("slab", "tx", "ty"),
        P("slab", None, None, None, None),
        P("slab", "tx", "ty"),
        P(None, "slab", None),
        P(None, None, "slab", "tx", "ty"),
    )
    out_specs = (P(None, None, None, "slab", "tx", "ty"), P(None, None, "slab", "tx", "ty"))
    return jax.shard_map(
        per_device, mesh=mesh, in_specs=in_specs, out_specs=out_specs, check_vma=False
    )
```

```python
import functools

import jax
import jax.numpy as jnp
from jax import lax
from jax.experimental import pallas as pl
from jax.experimental.pallas import tpu as pltpu
from jax.sharding import PartitionSpec as P

CORR = 3
TICKS = 2


DAMPING = 0.25
PRECISE = lax.Precision.HIGHEST
SPLIT = 65537.0


def fetch(block, axes, offsets):
    sizes = [lax.axis_size(a) for a in axes]
    pairs = []
    total = 1
    for s in sizes:
        total *= s
    for linear in range(total):
        coords = []
        rest = linear
        for s in reversed(sizes):
            coords.append(rest % s)
            rest //= s
        coords = coords[::-1]
        source = [c + d for c, d in zip(coords, offsets)]
        if all(0 <= c < s for c, s in zip(source, sizes)):
            src_linear = 0
            for c, s in zip(source, sizes):
                src_linear = src_linear * s + c
            pairs.append((src_linear, linear))
    if len(axes) == 1:
        return lax.ppermute(block, axes[0], pairs)
    return lax.ppermute(block, tuple(axes), pairs)


def extend_y(block, width):
    ny = block.shape[-1]
    low = fetch(block[..., ny - width :], ("ty",), (-1,))
    high = fetch(block[..., :width], ("ty",), (1,))
    return jnp.concatenate([low, block, high], axis=-1)


def flat_extended(block, width, padded, lead_axes=(), lead_offsets=()):
    nx = block.shape[-2]
    pieces = {
        -1: fetch(block[..., nx - width :, :], tuple(lead_axes) + ("tx",), tuple(lead_offsets) + (-1,)),
        1: fetch(block[..., :width, :], tuple(lead_axes) + ("tx",), tuple(lead_offsets) + (1,)),
    }
    if lead_axes:
        pieces[0] = fetch(block, tuple(lead_axes) + ("tx",), tuple(lead_offsets) + (0,))
    else:
        pieces[0] = block
    segments = []
    for ix in range(nx + 2 * width):
        dx = -1 if ix < width else (0 if ix < width + nx else 1)
        r = ix - (0 if dx == -1 else (width if dx == 0 else width + nx))
        segments.append(pieces[dx][..., r, :])
    used = sum(s.shape[-1] for s in segments)
    lead = segments[0].shape[:-1]
    segments.append(jnp.zeros(lead + (padded - used,), segments[0].dtype))
    return jnp.concatenate(segments, axis=-1)


def tick_kernel(
    order_ref, frc_ref, pk_ref, inc_ref, ins_ref, bhi_ref, blo_ref, *rest, row, depth, width, tick
):
    out_ref, trace_ref, field_ref = rest[-3:]
    if tick:
        out_ref[:tick] = rest[0][...]
    nsrc, rows, owned = trace_ref.shape[0], bhi_ref.shape[0], trace_ref.shape[2] * 128
    cols = pk_ref.shape[1]
    classes = bhi_ref.shape[1] // rows
    lanes = 128
    wave0 = pk_ref.shape[0] - depth - 2 * nsrc - 1
    label_row = wave0 + depth + 2 * nsrc
    extent = owned // lanes + 2 * width

    def edges(lo, hi):
        zrow = lax.broadcasted_iota(jnp.int32, (rows, hi - lo), 0) % depth
        return zrow == 0, zrow == depth - 1

    def precond(x, lo, hi):
        scaled = x * SPLIT
        high = scaled - (scaled - x)
        low = x - high
        label = pk_ref[pl.ds(label_row, 1), lo:hi]
        hots = [(label == float(k)).astype(jnp.bfloat16) for k in range(classes)]
        high = high.astype(jnp.bfloat16)
        low = low.astype(jnp.bfloat16)
        high = jnp.concatenate([high * h for h in hots], axis=0)
        low = jnp.concatenate([low * h for h in hots], axis=0)
        bhi = bhi_ref[...]
        blo = blo_ref[...]
        out = jnp.dot(bhi, low, preferred_element_type=jnp.float32)
        out = out + jnp.dot(blo, high, preferred_element_type=jnp.float32)
        return out + jnp.dot(bhi, high, preferred_element_type=jnp.float32)

    def apply_a(u, lo, hi):
        span = hi - lo
        top, bottom = edges(lo, hi)
        wave = pk_ref[pl.ds(wave0, depth), lo:hi]
        dr = 6.0 - wave
        di = -DAMPING * wave
        real = u[:depth]
        imaginary = u[depth:]
        diagonal = jnp.concatenate(
            [dr * real - di * imaginary, dr * imaginary + di * real], axis=0
        )
        down = jnp.where(top, 0.0, pltpu.roll(u, 1, 0))
        up = jnp.where(bottom, 0.0, pltpu.roll(u, rows - 1, 0))
        beside = up + down
        beside = beside + pltpu.roll(u, span - row, 1) + pltpu.roll(u, row, 1)
        beside = beside + pltpu.roll(u, span - 1, 1) + pltpu.roll(u, 1, 1)
        return diagonal - beside

    def one_source(s, carry):
        first = pl.multiple_of(order_ref[s] * rows, rows)
        forcing = frc_ref[pl.ds(first, rows), :]
        incoming = inc_ref[s]
        layer = jnp.concatenate(
            [
                jnp.broadcast_to(incoming[0:1], (depth, cols)),
                jnp.broadcast_to(incoming[1:2], (depth, cols)),
            ],
            axis=0,
        )
        top, _ = edges(0, cols)
        rhs = jnp.where(top, forcing + layer, forcing)
        field_ref[s] = precond(rhs, 0, cols)
        for step in range(1, CORR + 1):
            a = (step * row) // lanes * lanes
            b = min(-(-((extent - step) * row) // lanes) * lanes, cols)
            lo = max(a - 2 * lanes, 0)
            hi = min(b + 2 * lanes, cols)
            stencil = apply_a(field_ref[s, :, lo:hi], lo, hi)[:, a - lo : b - lo]
            residual = ins_ref[:, a:b] * (rhs[:, a:b] - stencil)
            field_ref[s, :, a:b] = field_ref[s, :, a:b] + precond(residual, a, b)
        u = field_ref[s]
        for x in range(owned // lanes):
            begin = (x + width) * row + width
            chunk = pltpu.roll(u, cols - begin, 1)[:, :lanes]
            for part in range(rows // depth):
                out_ref[tick, s, part, :, x, :] = chunk[part * depth : (part + 1) * depth, :]
            for part in range(rows // depth):
                bottom = (part + 1) * depth - 1
                trace_ref[s, part, pl.ds(x, 1), :] = chunk[bottom : bottom + 1, :]
        return carry

    for s in range(nsrc):
        one_source(s, 0)


def run_tick(order, forcing, packed, incoming, ins, bhi, blo, row, depth, width, owned, tick, done):
    nsrc = incoming.shape[0]
    rows, stacked = bhi.shape
    cols = packed.shape[1]
    flops = nsrc * (CORR + 1) * 3 * 2 * rows * stacked * cols
    vmem = pl.BlockSpec(memory_space=pltpu.VMEM)
    return pl.pallas_call(
        functools.partial(tick_kernel, row=row, depth=depth, width=width, tick=tick),
        out_shape=(
            jax.ShapeDtypeStruct((tick + 1, nsrc, rows // depth, depth, owned // 128, 128), jnp.float32),
            jax.ShapeDtypeStruct((nsrc, rows // depth, owned // 128, 128), jnp.float32),
        ),
        in_specs=[pl.BlockSpec(memory_space=pltpu.SMEM)] + [vmem] * (6 + (tick > 0)),
        out_specs=(vmem, vmem),
        scratch_shapes=[pltpu.VMEM((nsrc, rows, cols), jnp.float32)],
        cost_estimate=pl.CostEstimate(
            flops=flops,
            transcendentals=0,
            bytes_accessed=4 * (forcing.size + packed.size // 4 + nsrc * rows * owned),
        ),
    )(*([order, forcing, packed, incoming, ins, bhi, blo] + ([done] if tick else [])))


def block_matrix(inverse):
    real = inverse[:, 0]
    imaginary = inverse[:, 1]
    upper = jnp.concatenate([real, -imaginary], axis=2)
    lower = jnp.concatenate([imaginary, real], axis=2)
    return jnp.concatenate([upper, lower], axis=1)


def per_device(forcing, wavenumber_sq, line_inverse, column_class, batch_order, pending_trace):
    width = CORR
    ticks, nsrc, two, depth, nx, ny = forcing.shape
    classes = line_inverse.shape[1]
    ntx = lax.axis_size("tx")
    nty = lax.axis_size("ty")
    ex, ey = nx + 2 * width, ny + 2 * width
    cols = ex * ey
    padded = -(-cols // 128) * 128
    assert width <= nx and width <= ny

    per_tick = forcing.reshape(ticks, -1, nx, ny)
    packed = jnp.concatenate(
        [
            per_tick[0],
            wavenumber_sq,
            pending_trace.reshape(-1, nx, ny),
            column_class[0][None].astype(jnp.float32),
        ]
        + [per_tick[t] for t in range(1, ticks)],
        axis=0,
    )
    rows_now = per_tick.shape[1] + depth + nsrc * two + 1
    now = packed[:rows_now]
    low_x = fetch(now[:, nx - width :, :], ("tx",), (-1,))
    high_x = fetch(now[:, :width, :], ("tx",), (1,))
    widened = extend_y(packed, width)
    later = [
        widened[rows_now + (t - 1) * per_tick.shape[1] : rows_now + t * per_tick.shape[1]]
        for t in range(1, ticks)
    ]
    rims = jnp.concatenate([low_x, high_x], axis=1)
    corner_low = fetch(rims[..., ny - width :], ("ty",), (-1,))
    corner_high = fetch(rims[..., :width], ("ty",), (1,))
    rims = jnp.concatenate([corner_low, rims, corner_high], axis=-1)
    segments = []
    for ix in range(ex):
        if ix < width:
            segments.append(rims[:, ix])
        elif ix < width + nx:
            segments.append(widened[:rows_now, ix - width])
        else:
            segments.append(rims[:, ix - nx])
    segments.append(jnp.zeros((rows_now, padded - cols), jnp.float32))
    packed = jnp.concatenate(segments, axis=-1)
    first_pending = nsrc * two * depth + depth

    gx = lax.axis_index("tx") * nx - width + jnp.arange(ex)
    gy = lax.axis_index("ty") * ny - width + jnp.arange(ey)
    inside = ((gx >= 0) & (gx < nx * ntx))[:, None] & ((gy >= 0) & (gy < ny * nty))[None, :]
    inside = jnp.pad(inside.reshape(1, cols).astype(jnp.float32), ((0, 0), (0, padded - cols)))

    blocks = block_matrix(line_inverse[0])
    side_by_side = jnp.concatenate([blocks[k] for k in range(classes)], axis=1)
    rounded = lax.reduce_precision(side_by_side, exponent_bits=8, mantissa_bits=7)
    bhi = rounded.astype(jnp.bfloat16)
    blo = (side_by_side - rounded).astype(jnp.bfloat16)
    orders = batch_order[:, 0]

    incoming = packed[first_pending : first_pending + nsrc * two].reshape(nsrc, two, padded)
    low_later = [fetch(r[:, nx - width :, :], ("tx",), (-1,)) for r in later]
    high_later = [fetch(r[:, :width, :], ("tx",), (1,)) for r in later]
    trace = None
    field = None
    forcing_f = packed
    for tick in range(ticks):
        field, trace = run_tick(
            orders[tick], forcing_f, packed, incoming, inside, bhi, blo, ey, depth, width, nx * ny,
            tick, field,
        )
        if tick + 1 < ticks:
            rows = later[tick]
            field, low, high = lax.optimization_barrier((field, low_later[tick], high_later[tick]))
            segments = [low[:, ix] for ix in range(width)]
            segments += [rows[:, r] for r in range(nx)]
            segments += [high[:, r] for r in range(width)]
            segments.append(jnp.zeros((rows.shape[0], padded - cols), jnp.float32))
            forcing_f = jnp.concatenate(segments, axis=-1)
        if tick + 1 < ticks:
            incoming = flat_extended(extend_y(trace, width), width, padded, ("slab",), (-1,))
    return (field, trace[:, :, None])


def solution(mesh):
    in_specs = (
        P(None, None, None, "slab", "tx", "ty"),
        P("slab", "tx", "ty"),
        P("slab", None, None, None, None),
        P("slab", "tx", "ty"),
        P(None, "slab", None),
        P(None, None, "slab", "tx", "ty"),
    )
    out_specs = (P(None, None, None, "slab", "tx", "ty"), P(None, None, "slab", "tx", "ty"))
    return jax.shard_map(
        per_device, mesh=mesh, in_specs=in_specs, out_specs=out_specs, check_vma=False
    )
```
